256 devices in a mesh: req: 8 (over z), seq: 32 (over y, x, core).
Axes of the slice: x: 4, y: 4, z: 8, core: 2. Of those that a mesh axis runs over, the one named last changes fastest.
Arguments:
- hidden_in: bfloat16 [16, 1024, 2048], P('req', 'seq'), may hold values from -6 to 6
- norm_gain: float32 [2048], replicated, may hold values from 0.1 to 1.9
- w_query: bfloat16 [2048, 1024], P(('req', 'seq')), may hold values from -0.125 to 0.125
- w_key: bfloat16 [2048, 512], P(('req', 'seq')), may hold values from -0.3125 to 0.3125
- w_value: bfloat16 [2048, 512], P(('req', 'seq')), may hold values from -0.125 to 0.125
- cache_keys: bfloat16 [16, 8192, 512], P('req', 'seq'), may hold values from -525 to 525
- cache_values: bfloat16 [16, 8192, 512], P('req', 'seq'), may hold values from -6 to 6
- cache_lengths: int32 [16], P('req'), may hold values from 1 to 8192, as said below
Outputs:
- attended: bfloat16 [16, 1024, 1024], P('req', 'seq')
- new_keys: bfloat16 [16, 1024, 512], P('req', 'seq')
- new_values: bfloat16 [16, 1024, 512], P('req', 'seq')
The draws below stay inside these ranges and needn't reach their ends.
Inputs may be any that keep to these rules, and one draw needn't show every extreme that they name: `cache_lengths`: some request's cache holds exactly 8192 positions.
All inputs are finite; a program needn't handle non-finite values.
Results may differ from the reference program's by a relative error of at most 0.034.
Values may be sent and summed in bfloat16 or wider, within the bound.
No kernel may reach another device: no remote copies, remote signals or barrier semaphores. Data moves between devices by JAX's collectives and lax.ppermute only.
A program may use at most 128 MiB of HBM per device.

```python
import jax
import jax.numpy as jnp
from jax import lax

D = 2048
HEADS = 4
KV_HEADS = 2
HEAD = 256
CSLICE = 32
CACHE_DEV = 256
REQS = 16
SPAN = 1024
CTX = 8192
N_SEQ = 32


def draw_cache_lengths(key, part):
    first_key, second_key = jax.random.split(key)
    lengths = jax.random.randint(first_key, (REQS,), 1, CTX + 1)
    chosen = jax.random.randint(second_key, (), 0, REQS)
    return jnp.where(jnp.arange(REQS) == chosen, CTX, lengths).astype(jnp.int32)


def draw_cache_keys(key, part):
    split_keys = jax.random.split(key, 1)
    normal_rows = 2.5 * jax.random.normal(split_keys[0], (REQS, CTX, KV_HEADS * HEAD), jnp.float32)
    return jnp.clip(normal_rows, -15.0, 15.0).astype(jnp.bfloat16)


def shard_levels(stream_key, shape, cuts, low, top_value):
    def one(position, shards_of):
        heights = jax.random.uniform(jax.random.fold_in(jax.random.fold_in(stream_key, 6), position), (shards_of,), jnp.float32, low / len(cuts), top_value / len(cuts))
        return jnp.repeat(jnp.exp(heights), shape[position] // shards_of).reshape((-1,) + (1,) * (len(shape) - position - 1))

    factor_of = one(*cuts[0])
    for cut in cuts[1:]:
        factor_of = factor_of * one(*cut)
    return factor_of


def normal_values(stream_key, shape, scale, limit, cuts=(), kind=jnp.bfloat16):
    array = scale * jax.random.normal(stream_key, shape, jnp.float32)
    if cuts:
        array = array * shard_levels(stream_key, shape, cuts, -0.22, 0.18)
    return jnp.clip(array, -limit, limit).astype(kind)


def setup_inputs(seed: int = 0) -> dict:
    key_of = jax.random.split(jax.random.key(seed), 9)
    return {
        "hidden_in": normal_values(key_of[0], (REQS, SPAN, D), 1.0, 6.0, ((0, 8), (1, 32))),
        "norm_gain": jnp.clip(1.0 + 0.18 * jax.random.normal(key_of[1], (D,), jnp.float32), 0.1, 1.9),
        "w_query": normal_values(key_of[2], (D, HEADS * HEAD), D ** -0.5, 0.125, ((0, 256),)),
        "w_key": normal_values(key_of[3], (D, KV_HEADS * HEAD), (D // 6) ** -0.5, 0.3125, ((0, 256),)),
        "w_value": normal_values(key_of[4], (D, KV_HEADS * HEAD), D ** -0.5, 0.125, ((0, 256),)),
        "cache_keys": draw_cache_keys(jax.random.fold_in(key_of[8], 71), 0),
        "cache_values": normal_values(key_of[6], (REQS, CTX, KV_HEADS * HEAD), 1.0, 6.0, ((0, 8), (1, 32))),
        "cache_lengths": draw_cache_lengths(jax.random.fold_in(key_of[8], 71), 0),
    }


EPSILON = 1e-06
THETA = 1000042.0
MASKED = -1e+30

def tables(positions, head_size):
    half_size = head_size // 2
    frequency = THETA ** (-(jnp.arange(half_size, dtype=jnp.float32) * 2.0 / head_size))
    angles = positions.astype(jnp.float32)[..., None] * frequency
    return (jnp.cos(angles)[..., None, :], jnp.sin(angles)[..., None, :])

def rotate(values, cosine, sine_part):
    half_size = values.shape[-1] // 2
    first_half = values[..., :half_size]
    second_half = values[..., half_size:]
    return jnp.concatenate([first_half * cosine - second_half * sine_part, second_half * cosine + first_half * sine_part], axis=-1)

def reference(hidden_in, norm_gain, w_query, w_key, w_value, cache_keys, cache_values, cache_lengths):
    group_size = HEADS // KV_HEADS
    score_scale = HEAD ** (-0.5)
    inputs = hidden_in.astype(jnp.float32)
    normed = (inputs * lax.rsqrt(lax.optimization_barrier(jnp.mean(inputs * inputs, axis=-1, keepdims=True)) + EPSILON) * norm_gain).astype(jnp.bfloat16)
    flat_rows = normed.reshape(REQS * SPAN, D)
    query_raw = jnp.dot(flat_rows, w_query, preferred_element_type=jnp.float32).reshape(REQS, SPAN, HEADS, HEAD)
    key_raw = jnp.dot(flat_rows, w_key, preferred_element_type=jnp.float32).reshape(REQS, SPAN, KV_HEADS, HEAD)
    value_raw = jnp.dot(flat_rows, w_value, preferred_element_type=jnp.float32).reshape(REQS, SPAN, KV_HEADS * HEAD)
    positions = cache_lengths[:, None] + jnp.arange(SPAN, dtype=jnp.int32)[None, :]
    cosine, sine_part = tables(positions, HEAD)
    queries = rotate(query_raw, cosine, sine_part).astype(jnp.bfloat16)
    new_keys = rotate(key_raw, cosine, sine_part).reshape(REQS, SPAN, KV_HEADS * HEAD).astype(jnp.bfloat16)
    new_values = value_raw.astype(jnp.bfloat16)
    query_all = queries.astype(jnp.float32).reshape(REQS, SPAN, KV_HEADS, group_size, HEAD)
    span_index = jnp.arange(SPAN, dtype=jnp.int32)
    width_all = CACHE_DEV + CSLICE

    def block_terms(block_id):
        cache_start = block_id * CACHE_DEV
        new_start = block_id * CSLICE
        block_keys = jnp.concatenate([lax.dynamic_slice_in_dim(cache_keys, cache_start, CACHE_DEV, 1), lax.dynamic_slice_in_dim(new_keys, new_start, CSLICE, 1)], axis=1)
        block_values = jnp.concatenate([lax.dynamic_slice_in_dim(cache_values, cache_start, CACHE_DEV, 1), lax.dynamic_slice_in_dim(new_values, new_start, CSLICE, 1)], axis=1)
        key_all = block_keys.astype(jnp.float32).reshape(REQS, width_all, KV_HEADS, HEAD)
        value_all = block_values.astype(jnp.float32).reshape(REQS, width_all, KV_HEADS, HEAD)
        cache_pos = cache_start + jnp.arange(CACHE_DEV, dtype=jnp.int32)
        cache_live = cache_pos[None, None, :] < cache_lengths[:, None, None]
        new_pos = new_start + jnp.arange(CSLICE, dtype=jnp.int32)
        new_live = new_pos[None, None, :] <= span_index[None, :, None]
        live = jnp.concatenate([jnp.broadcast_to(cache_live, (REQS, SPAN, CACHE_DEV)), jnp.broadcast_to(new_live, (REQS, SPAN, CSLICE))], axis=2)[:, :, None, None, :]
        scores = jnp.einsum('rcgeh,rkgh->rcgek', query_all, key_all) * score_scale
        scores = jnp.where(live, scores, MASKED)
        block_max = lax.optimization_barrier(jnp.max(scores, axis=-1))
        weights = jnp.where(live, jnp.exp(scores - block_max[..., None]), 0.0)
        block_sum = lax.optimization_barrier(jnp.sum(weights, axis=-1))
        rounded = lax.optimization_barrier(weights.astype(jnp.bfloat16)).astype(jnp.float32)
        block_out = jnp.einsum('rcgek,rkgh->rcgeh', rounded, value_all)
        block_out = lax.optimization_barrier(block_out.astype(jnp.bfloat16)).astype(jnp.float32)
        return (block_max, block_sum, block_out)

    def advance(state_now, block_id):
        running_max, running_sum, summed = state_now
        block_max, block_sum, block_out = block_terms(block_id)
        new_max = jnp.maximum(running_max, block_max)
        old_factor = jnp.exp(running_max - new_max)
        new_factor = jnp.exp(block_max - new_max)
        return ((new_max, running_sum * old_factor + block_sum * new_factor, summed * old_factor[..., None] + block_out * new_factor[..., None]), None)
    start_state = (jnp.full((REQS, SPAN, KV_HEADS, group_size), MASKED, jnp.float32), jnp.zeros((REQS, SPAN, KV_HEADS, group_size), jnp.float32), jnp.zeros((REQS, SPAN, KV_HEADS, group_size, HEAD), jnp.float32))
    final_state, _ = lax.scan(advance, start_state, jnp.arange(N_SEQ, dtype=jnp.int32))
    running_max, running_sum, summed = final_state
    attended = (summed / running_sum[..., None]).reshape(REQS, SPAN, HEADS * HEAD).astype(jnp.bfloat16)
    return (attended, new_keys, new_values)
```

```python
import jax
import jax.numpy as jnp
from jax import lax
from jax.sharding import PartitionSpec as P

HEADS = 4
KV_HEADS = 2
HEAD = 256


EPSILON = 1e-06
THETA = 1000042.0
MASKED = -1e30


def tables(positions, head_size):
    half_size = head_size // 2
    frequency = THETA ** (-(jnp.arange(half_size, dtype=jnp.float32) * 2.0 / head_size))
    angles = positions.astype(jnp.float32)[..., None] * frequency
    return (jnp.cos(angles)[..., None, :], jnp.sin(angles)[..., None, :])


def rotate(values, cosine, sine_part):
    half_size = values.shape[-1] // 2
    first_half = values[..., :half_size]
    second_half = values[..., half_size:]
    return jnp.concatenate(
        [
            first_half * cosine - second_half * sine_part,
            second_half * cosine + first_half * sine_part,
        ],
        axis=-1,
    )


def attend(query_rows, key_rows, value_rows, live):
    span_len = query_rows.shape[0]
    group_size = HEADS // KV_HEADS
    query_view = query_rows.reshape(span_len, KV_HEADS, group_size, HEAD)
    key_view = key_rows.reshape(key_rows.shape[0], KV_HEADS, HEAD)
    value_view = value_rows.reshape(value_rows.shape[0], KV_HEADS, HEAD)
    scores = jnp.einsum(
        "cgeh,kgh->cgek", query_view, key_view, preferred_element_type=jnp.float32
    ) * HEAD ** (-0.5)
    mask_view = live[:, None, None, :]
    scores = jnp.where(mask_view, scores, MASKED)
    block_max = jnp.max(scores, axis=-1)
    weights = jnp.where(mask_view, jnp.exp(scores - block_max[..., None]), 0.0)
    block_sum = jnp.sum(weights, axis=-1)
    block_out = jnp.einsum(
        "cgek,kgh->cgeh",
        weights.astype(jnp.bfloat16),
        value_view,
        preferred_element_type=jnp.float32,
    )
    return (
        block_max.reshape(span_len, HEADS),
        block_sum.reshape(span_len, HEADS),
        block_out.reshape(span_len, HEADS * HEAD).astype(jnp.bfloat16),
    )


def attend_rows(query_rows, key_rows, value_rows, live):
    total_rows = query_rows.shape[0]
    row_block = min(512, total_rows)
    pieces = []
    for begin in range(0, total_rows, row_block):
        pieces.append(
            attend(
                query_rows[begin : begin + row_block],
                key_rows,
                value_rows,
                live[begin : begin + row_block],
            )
        )
    return tuple((jnp.concatenate([piece[slot] for piece in pieces], axis=0) for slot in range(3)))


def body(hidden_in, norm_gain, w_query, w_key, w_value, cache_keys, cache_values, cache_lengths):
    seq_count = lax.axis_size("seq")
    seq_seat = lax.axis_index("seq")
    req_local, slice_len, model_width = hidden_in.shape
    cache_len_dev = cache_keys.shape[1]
    span_len = slice_len * seq_count
    inputs = hidden_in.astype(jnp.float32)
    normed = (
        inputs * lax.rsqrt(jnp.mean(inputs * inputs, axis=-1, keepdims=True) + EPSILON) * norm_gain
    ).astype(jnp.bfloat16)
    flat_rows = normed.reshape(req_local * slice_len, model_width)
    req_count = lax.axis_size("req")
    row_local = w_query.shape[0]
    query_cols = w_query.shape[1]
    key_cols = w_key.shape[1]
    joined = jnp.concatenate([w_query, w_key, w_value], axis=1)
    joined = lax.all_gather(joined, "req", axis=0, tiled=True)
    joined = lax.all_gather(joined, "seq", axis=0, tiled=True)
    permuted_rows = (
        flat_rows.reshape(-1, req_count, seq_count, row_local)
        .transpose(0, 2, 1, 3)
        .reshape(-1, model_width)
    )
    projected = jnp.dot(permuted_rows, joined, preferred_element_type=jnp.float32)
    query_raw = projected[:, :query_cols]
    key_raw = projected[:, query_cols : query_cols + key_cols]
    value_raw = projected[:, query_cols + key_cols :]
    local_index = jnp.arange(slice_len, dtype=jnp.int32)
    positions = cache_lengths[:, None] + seq_seat * slice_len + local_index[None, :]
    cosine, sine_part = tables(positions, HEAD)
    queries = (
        rotate(query_raw.reshape(req_local, slice_len, HEADS, HEAD), cosine, sine_part)
        .reshape(req_local, slice_len, HEADS * HEAD)
        .astype(jnp.bfloat16)
    )
    new_keys = (
        rotate(key_raw.reshape(req_local, slice_len, KV_HEADS, HEAD), cosine, sine_part)
        .reshape(req_local, slice_len, KV_HEADS * HEAD)
        .astype(jnp.bfloat16)
    )
    new_values = value_raw.reshape(req_local, slice_len, KV_HEADS * HEAD).astype(jnp.bfloat16)
    all_queries = lax.all_gather(queries, "seq", axis=1, tiled=True)
    key_block = jnp.concatenate([cache_keys, new_keys], axis=1)
    value_block = jnp.concatenate([cache_values, new_values], axis=1)
    span_index = jnp.arange(span_len, dtype=jnp.int32)
    cache_pos = seq_seat * cache_len_dev + jnp.arange(cache_len_dev, dtype=jnp.int32)
    new_pos = seq_seat * slice_len + local_index
    new_live = new_pos[None, :] <= span_index[:, None]
    max_list = []
    sum_list = []
    out_list = []
    for request in range(req_local):
        cache_live = cache_pos < cache_lengths[request]
        live_full = jnp.concatenate(
            [jnp.broadcast_to(cache_live[None, :], (span_len, cache_len_dev)), new_live], axis=1
        )
        query_rows = all_queries[request]
        terms = attend_rows(query_rows, key_block[request], value_block[request], live_full)
        max_list.append(terms[0])
        sum_list.append(terms[1])
        out_list.append(terms[2])
    max_all = jnp.stack(max_list)
    sum_all = jnp.stack(sum_list)
    out_all = jnp.stack(out_list)
    got_max, got_sum = (
        lax.all_to_all(max_all, "seq", split_axis=1, concat_axis=0, tiled=True),
        lax.all_to_all(sum_all, "seq", split_axis=1, concat_axis=0, tiled=True),
    )
    got_out = lax.all_to_all(out_all, "seq", split_axis=1, concat_axis=0, tiled=True)
    got_max = got_max.reshape(seq_count, req_local, slice_len, HEADS)
    got_sum = got_sum.reshape(seq_count, req_local, slice_len, HEADS)
    got_out = got_out.reshape(seq_count, req_local, slice_len, HEADS, HEAD)
    best_max = jnp.max(got_max, axis=0)
    factor = jnp.exp(got_max - best_max)
    total_sum = jnp.sum(got_sum * factor, axis=0)
    total_out = jnp.sum(got_out.astype(jnp.float32) * factor[..., None], axis=0)
    attended = (
        (total_out / total_sum[..., None])
        .reshape(req_local, slice_len, HEADS * HEAD)
        .astype(jnp.bfloat16)
    )
    return (attended, new_keys, new_values)


def solution(mesh):
    in_specs = (
        P("req", "seq", None),
        P(),
        P(("req", "seq"), None),
        P(("req", "seq"), None),
        P(("req", "seq"), None),
        P("req", "seq", None),
        P("req", "seq", None),
        P("req"),
    )
    out_specs = (P("req", "seq", None), P("req", "seq", None), P("req", "seq", None))
    return jax.shard_map(body, mesh=mesh, in_specs=in_specs, out_specs=out_specs, check_vma=False)
```

```python
import functools

import jax
import jax.numpy as jnp
from jax import lax
from jax.experimental import pallas as pl
from jax.experimental.pallas import tpu as pltpu
from jax.sharding import PartitionSpec as P

HEADS = 4
KV_HEADS = 2
HEAD = 256


EPSILON = 1e-06
THETA = 1000042.0
MASKED = -1e30


def tables(positions, head_size):
    half_size = head_size // 2
    frequency = THETA ** (-(jnp.arange(half_size, dtype=jnp.float32) * 2.0 / head_size))
    angles = positions.astype(jnp.float32)[..., None] * frequency
    return (jnp.cos(angles)[..., None, :], jnp.sin(angles)[..., None, :])


def rotate(values, cosine, sine_part):
    half_size = values.shape[-1] // 2
    first_half = values[..., :half_size]
    second_half = values[..., half_size:]
    return jnp.concatenate(
        [
            first_half * cosine - second_half * sine_part,
            second_half * cosine + first_half * sine_part,
        ],
        axis=-1,
    )


def attend(query_rows, key_rows, value_rows, live):
    span_len = query_rows.shape[0]
    group_size = HEADS // KV_HEADS
    query_view = query_rows.reshape(span_len, KV_HEADS, group_size, HEAD)
    key_view = key_rows.reshape(key_rows.shape[0], KV_HEADS, HEAD)
    value_view = value_rows.reshape(value_rows.shape[0], KV_HEADS, HEAD)
    scores = jnp.einsum(
        "cgeh,kgh->cgek", query_view, key_view, preferred_element_type=jnp.float32
    ) * HEAD ** (-0.5)
    mask_view = live[:, None, None, :]
    scores = jnp.where(mask_view, scores, MASKED)
    block_max = jnp.max(scores, axis=-1)
    weights = jnp.where(mask_view, jnp.exp(scores - block_max[..., None]), 0.0)
    block_sum = jnp.sum(weights, axis=-1)
    block_out = jnp.einsum(
        "cgek,kgh->cgeh",
        weights.astype(jnp.bfloat16),
        value_view,
        preferred_element_type=jnp.float32,
    )
    return (
        block_max.reshape(span_len, HEADS),
        block_sum.reshape(span_len, HEADS),
        block_out.reshape(span_len, HEADS * HEAD).astype(jnp.bfloat16),
    )


def attend_rows(query_rows, key_rows, value_rows, live):
    total_rows = query_rows.shape[0]
    row_block = min(512, total_rows)
    pieces = []
    for begin in range(0, total_rows, row_block):
        pieces.append(
            attend(
                query_rows[begin : begin + row_block],
                key_rows,
                value_rows,
                live[begin : begin + row_block],
            )
        )
    return tuple((jnp.concatenate([piece[slot] for piece in pieces], axis=0) for slot in range(3)))


def attention_kernel(scalar_ref, query_ref, key_ref, value_ref, stats_ref, out_ref, *, cache_len_dev, slice_len):
    request = pl.program_id(0)
    length = scalar_ref[request]
    seat = scalar_ref[scalar_ref.shape[0] - 1]
    span_len = query_ref.shape[1]
    key_rows = key_ref.shape[1]
    key_index = lax.broadcasted_iota(jnp.int32, (span_len, key_rows), 1)
    query_index = lax.broadcasted_iota(jnp.int32, (span_len, key_rows), 0)
    cache_live = seat * cache_len_dev + key_index < length
    new_live = seat * slice_len + (key_index - cache_len_dev) <= query_index
    in_cache = key_index < cache_len_dev
    in_new = jnp.logical_not(in_cache) & (key_index < cache_len_dev + slice_len)
    live = (in_cache & cache_live) | (in_new & new_live)
    lane = lax.broadcasted_iota(jnp.int32, (span_len, 128), 1)
    stats = jnp.zeros((span_len, 128), jnp.float32)
    group_size = HEADS // KV_HEADS
    for head in range(HEADS):
        group = head // group_size
        query_rows = query_ref[0, :, head * HEAD : (head + 1) * HEAD]
        key_rows_h = key_ref[0, :, group * HEAD : (group + 1) * HEAD]
        value_rows_h = value_ref[0, :, group * HEAD : (group + 1) * HEAD]
        scores = lax.dot_general(
            query_rows, key_rows_h, (((1,), (1,)), ((), ())), preferred_element_type=jnp.float32
        ) * HEAD ** (-0.5)
        scores = jnp.where(live, scores, MASKED)
        block_max = jnp.max(scores, axis=1, keepdims=True)
        weights = jnp.where(live, jnp.exp(scores - block_max), 0.0)
        block_sum = jnp.sum(weights, axis=1, keepdims=True)
        block_out = jnp.dot(
            weights.astype(jnp.bfloat16), value_rows_h, preferred_element_type=jnp.float32
        )
        out_ref[0, :, head * HEAD : (head + 1) * HEAD] = block_out.astype(jnp.bfloat16)
        stats = jnp.where(lane == head, block_max, stats)
        stats = jnp.where(lane == HEADS + head, block_sum, stats)
    stats_ref[0] = stats


def block_attention(all_queries, key_block, value_block, scalars, cache_len_dev, slice_len):
    req_local, span_len, query_width = all_queries.shape
    key_rows = key_block.shape[1]
    kv_width = key_block.shape[2]
    grid_spec = pltpu.PrefetchScalarGridSpec(
        num_scalar_prefetch=1,
        grid=(req_local,),
        in_specs=[
            pl.BlockSpec((1, span_len, query_width), lambda r, s: (r, 0, 0)),
            pl.BlockSpec((1, key_rows, kv_width), lambda r, s: (r, 0, 0)),
            pl.BlockSpec((1, key_rows, kv_width), lambda r, s: (r, 0, 0)),
        ],
        out_specs=[
            pl.BlockSpec((1, span_len, 128), lambda r, s: (r, 0, 0)),
            pl.BlockSpec((1, span_len, query_width), lambda r, s: (r, 0, 0)),
        ],
    )
    return pl.pallas_call(
        functools.partial(attention_kernel, cache_len_dev=cache_len_dev, slice_len=slice_len),
        grid_spec=grid_spec,
        out_shape=[
            jax.ShapeDtypeStruct((req_local, span_len, 128), jnp.float32),
            jax.ShapeDtypeStruct((req_local, span_len, query_width), jnp.bfloat16),
        ],
    )(scalars, all_queries, key_block, value_block)


def body(hidden_in, norm_gain, w_query, w_key, w_value, cache_keys, cache_values, cache_lengths):
    seq_count = lax.axis_size("seq")
    seq_seat = lax.axis_index("seq")
    req_local, slice_len, model_width = hidden_in.shape
    cache_len_dev = cache_keys.shape[1]
    span_len = slice_len * seq_count
    inputs = hidden_in.astype(jnp.float32)
    normed = (
        inputs * lax.rsqrt(jnp.mean(inputs * inputs, axis=-1, keepdims=True) + EPSILON) * norm_gain
    ).astype(jnp.bfloat16)
    flat_rows = normed.reshape(req_local * slice_len, model_width)
    req_count = lax.axis_size("req")
    row_local = w_query.shape[0]
    query_cols = w_query.shape[1]
    key_cols = w_key.shape[1]
    joined = jnp.concatenate([w_query, w_key, w_value], axis=1)
    joined = lax.all_gather(joined, "req", axis=0, tiled=True)
    joined = lax.all_gather(joined, "seq", axis=0, tiled=True)
    permuted_rows = (
        flat_rows.reshape(-1, req_count, seq_count, row_local)
        .transpose(0, 2, 1, 3)
        .reshape(-1, model_width)
    )
    projected = jnp.dot(permuted_rows, joined, preferred_element_type=jnp.float32)
    query_raw = projected[:, :query_cols]
    key_raw = projected[:, query_cols : query_cols + key_cols]
    value_raw = projected[:, query_cols + key_cols :]
    local_index = jnp.arange(slice_len, dtype=jnp.int32)
    positions = cache_lengths[:, None] + seq_seat * slice_len + local_index[None, :]
    cosine, sine_part = tables(positions, HEAD)
    queries = (
        rotate(query_raw.reshape(req_local, slice_len, HEADS, HEAD), cosine, sine_part)
        .reshape(req_local, slice_len, HEADS * HEAD)
        .astype(jnp.bfloat16)
    )
    new_keys = (
        rotate(key_raw.reshape(req_local, slice_len, KV_HEADS, HEAD), cosine, sine_part)
        .reshape(req_local, slice_len, KV_HEADS * HEAD)
        .astype(jnp.bfloat16)
    )
    new_values = value_raw.reshape(req_local, slice_len, KV_HEADS * HEAD).astype(jnp.bfloat16)
    all_queries = lax.all_gather(queries, "seq", axis=1, tiled=True)
    pad_rows = (-(cache_len_dev + slice_len)) % 128
    key_block = jnp.concatenate(
        [cache_keys, new_keys, jnp.zeros((req_local, pad_rows, KV_HEADS * HEAD), jnp.bfloat16)], axis=1
    )
    value_block = jnp.concatenate(
        [cache_values, new_values, jnp.zeros((req_local, pad_rows, KV_HEADS * HEAD), jnp.bfloat16)],
        axis=1,
    )
    scalars = jnp.concatenate([cache_lengths.astype(jnp.int32), seq_seat.astype(jnp.int32)[None]])
    stats, out_all = block_attention(all_queries, key_block, value_block, scalars, cache_len_dev, slice_len)
    stats = stats[:, :, : 2 * HEADS]
    got_stats = lax.all_to_all(stats, "seq", split_axis=1, concat_axis=0, tiled=True)
    got_out = lax.all_to_all(out_all, "seq", split_axis=1, concat_axis=0, tiled=True)
    got_stats = got_stats.reshape(seq_count, req_local, slice_len, 2 * HEADS)
    got_max = got_stats[..., :HEADS]
    got_sum = got_stats[..., HEADS:]
    got_out = got_out.reshape(seq_count, req_local, slice_len, HEADS, HEAD)
    best_max = jnp.max(got_max, axis=0)
    factor = jnp.exp(got_max - best_max)
    total_sum = jnp.sum(got_sum * factor, axis=0)
    total_out = jnp.sum(got_out.astype(jnp.float32) * factor[..., None], axis=0)
    attended = (
        (total_out / total_sum[..., None])
        .reshape(req_local, slice_len, HEADS * HEAD)
        .astype(jnp.bfloat16)
    )
    return (attended, new_keys, new_values)


def solution(mesh):
    in_specs = (
        P("req", "seq", None),
        P(),
        P(("req", "seq"), None),
        P(("req", "seq"), None),
        P(("req", "seq"), None),
        P("req", "seq", None),
        P("req", "seq", None),
        P("req"),
    )
    out_specs = (P("req", "seq", None), P("req", "seq", None), P("req", "seq", None))
    return jax.shard_map(body, mesh=mesh, in_specs=in_specs, out_specs=out_specs, check_vma=False)
```

```python
import functools

import jax
import jax.numpy as jnp
from jax import lax
from jax.experimental import pallas as pl
from jax.experimental.pallas import tpu as pltpu
from jax.sharding import PartitionSpec as P

HEADS = 4
KV_HEADS = 2
HEAD = 256


EPSILON = 1e-06
THETA = 1000042.0
MASKED = -1e30


def tables(positions, head_size):
    half_size = head_size // 2
    frequency = THETA ** (-(jnp.arange(half_size, dtype=jnp.float32) * 2.0 / head_size))
    angles = positions.astype(jnp.float32)[..., None] * frequency
    return (jnp.cos(angles)[..., None, :], jnp.sin(angles)[..., None, :])


def rotate(values, cosine, sine_part):
    half_size = values.shape[-1] // 2
    first_half = values[..., :half_size]
    second_half = values[..., half_size:]
    return jnp.concatenate(
        [
            first_half * cosine - second_half * sine_part,
            second_half * cosine + first_half * sine_part,
        ],
        axis=-1,
    )


def attention_kernel(scalar_ref, query_ref, key_ref, value_ref, stats_ref, out_ref, *, cache_len_dev, slice_len):
    request = pl.program_id(0)
    length = scalar_ref[request]
    seat = scalar_ref[scalar_ref.shape[0] - 1]
    span_len = query_ref.shape[1]
    key_rows = key_ref.shape[1]
    blocks = out_ref.shape[0]
    key_index = lax.broadcasted_iota(jnp.int32, (span_len, key_rows), 1)
    query_index = lax.broadcasted_iota(jnp.int32, (span_len, key_rows), 0)
    cache_live = seat * cache_len_dev + key_index < length
    new_live = seat * slice_len + (key_index - cache_len_dev) <= query_index
    in_cache = key_index < cache_len_dev
    in_new = jnp.logical_not(in_cache) & (key_index < cache_len_dev + slice_len)
    live = (in_cache & cache_live) | (in_new & new_live)
    lane = lax.broadcasted_iota(jnp.int32, (span_len, 128), 1)
    stats = jnp.zeros((span_len, 128), jnp.float32)
    group_size = HEADS // KV_HEADS
    for head in range(HEADS):
        group = head // group_size
        query_rows = query_ref[0, :, head * HEAD : (head + 1) * HEAD]
        key_rows_h = key_ref[0, :, group * HEAD : (group + 1) * HEAD]
        value_rows_h = value_ref[0, :, group * HEAD : (group + 1) * HEAD]
        scores = lax.dot_general(
            query_rows, key_rows_h, (((1,), (1,)), ((), ())), preferred_element_type=jnp.float32
        ) * HEAD ** (-0.5)
        scores = jnp.where(live, scores, MASKED)
        block_max = jnp.max(scores, axis=1, keepdims=True)
        weights = jnp.where(live, jnp.exp(scores - block_max), 0.0)
        block_sum = jnp.sum(weights, axis=1, keepdims=True)
        block_out = jnp.dot(
            weights.astype(jnp.bfloat16), value_rows_h, preferred_element_type=jnp.float32
        )
        out_ref[:, 0, :, head * HEAD : (head + 1) * HEAD] = block_out.astype(jnp.bfloat16).reshape(
            blocks, span_len // blocks, HEAD
        )
        stats = jnp.where(lane == head, block_max, stats)
        stats = jnp.where(lane == HEADS + head, block_sum, stats)
    stats_ref[:, 0] = stats[:, : stats_ref.shape[3]].reshape(blocks, span_len // blocks, stats_ref.shape[3])


def block_attention(all_queries, key_block, value_block, scalars, cache_len_dev, slice_len, blocks):
    req_local, span_len, query_width = all_queries.shape
    key_rows = key_block.shape[1]
    kv_width = key_block.shape[2]
    chunk = span_len // blocks
    grid_spec = pltpu.PrefetchScalarGridSpec(
        num_scalar_prefetch=1,
        grid=(req_local,),
        in_specs=[
            pl.BlockSpec((1, span_len, query_width), lambda r, s: (r, 0, 0)),
            pl.BlockSpec((1, key_rows, kv_width), lambda r, s: (r, 0, 0)),
            pl.BlockSpec((1, key_rows, kv_width), lambda r, s: (r, 0, 0)),
        ],
        out_specs=[
            pl.BlockSpec((blocks, 1, chunk, 2 * HEADS), lambda r, s: (0, r, 0, 0)),
            pl.BlockSpec((blocks, 1, chunk, query_width), lambda r, s: (0, r, 0, 0)),
        ],
    )
    return pl.pallas_call(
        functools.partial(attention_kernel, cache_len_dev=cache_len_dev, slice_len=slice_len),
        grid_spec=grid_spec,
        out_shape=[
            jax.ShapeDtypeStruct((blocks, req_local, chunk, 2 * HEADS), jnp.float32),
            jax.ShapeDtypeStruct((blocks, req_local, chunk, query_width), jnp.bfloat16),
        ],
    )(scalars, all_queries, key_block, value_block)


def combine_kernel(stats_ref, out_ref, result_ref):
    blocks, _, chunk, stat_width = stats_ref.shape
    width = out_ref.shape[3]
    top = stats_ref[0, 0]
    for block in range(1, blocks):
        top = jnp.maximum(top, stats_ref[block, 0])
    lane = lax.broadcasted_iota(jnp.int32, (chunk, stat_width), 1)

    def step(block, carry):
        summed, total = carry
        row_stats = stats_ref[block, 0]
        factor = jnp.exp(row_stats - top)
        rows = out_ref[block, 0].astype(jnp.float32)
        pieces = []
        new_total = []
        for head in range(HEADS):
            head_factor = jnp.sum(jnp.where(lane == head, factor, 0.0), axis=1, keepdims=True)
            head_sum = jnp.sum(jnp.where(lane == HEADS + head, row_stats, 0.0), axis=1, keepdims=True)
            pieces.append(summed[head] + rows[:, head * HEAD : (head + 1) * HEAD] * head_factor)
            new_total.append(total[head] + head_factor * head_sum)
        return (tuple(pieces), tuple(new_total))

    start = (
        tuple(jnp.zeros((chunk, HEAD), jnp.float32) for _ in range(HEADS)),
        tuple(jnp.zeros((chunk, 1), jnp.float32) for _ in range(HEADS)),
    )
    summed, total = lax.fori_loop(0, blocks, step, start)
    for head in range(HEADS):
        result_ref[0, :, head * HEAD : (head + 1) * HEAD] = (summed[head] / total[head]).astype(
            result_ref.dtype
        )


def combine(got_stats, got_out):
    blocks, req_local, chunk, stat_width = got_stats.shape
    width = got_out.shape[3]
    return pl.pallas_call(
        combine_kernel,
        grid=(req_local,),
        in_specs=[
            pl.BlockSpec((blocks, 1, chunk, stat_width), lambda r: (0, r, 0, 0)),
            pl.BlockSpec((blocks, 1, chunk, width), lambda r: (0, r, 0, 0)),
        ],
        out_specs=pl.BlockSpec((1, chunk, width), lambda r: (r, 0, 0)),
        out_shape=jax.ShapeDtypeStruct((req_local, chunk, width), jnp.bfloat16),
    )(got_stats, got_out)


def body(hidden_in, norm_gain, w_query, w_key, w_value, cache_keys, cache_values, cache_lengths):
    seq_count = lax.axis_size("seq")
    seq_seat = lax.axis_index("seq")
    req_local, slice_len, model_width = hidden_in.shape
    cache_len_dev = cache_keys.shape[1]
    span_len = slice_len * seq_count
    inputs = hidden_in.astype(jnp.float32)
    normed = (
        inputs * lax.rsqrt(jnp.mean(inputs * inputs, axis=-1, keepdims=True) + EPSILON) * norm_gain
    ).astype(jnp.bfloat16)
    flat_rows = normed.reshape(req_local * slice_len, model_width)
    req_count = lax.axis_size("req")
    row_local = w_query.shape[0]
    query_cols = w_query.shape[1]
    key_cols = w_key.shape[1]
    joined = jnp.concatenate([w_query, w_key, w_value], axis=1)
    joined = lax.all_gather(joined, "req", axis=0, tiled=True)
    joined = lax.all_gather(joined, "seq", axis=0, tiled=True)
    permuted_rows = (
        flat_rows.reshape(-1, req_count, seq_count, row_local)
        .transpose(0, 2, 1, 3)
        .reshape(-1, model_width)
    )
    projected = jnp.dot(permuted_rows, joined, preferred_element_type=jnp.float32)
    query_raw = projected[:, :query_cols]
    key_raw = projected[:, query_cols : query_cols + key_cols]
    value_raw = projected[:, query_cols + key_cols :]
    local_index = jnp.arange(slice_len, dtype=jnp.int32)
    positions = cache_lengths[:, None] + seq_seat * slice_len + local_index[None, :]
    cosine, sine_part = tables(positions, HEAD)
    queries = (
        rotate(query_raw.reshape(req_local, slice_len, HEADS, HEAD), cosine, sine_part)
        .reshape(req_local, slice_len, HEADS * HEAD)
        .astype(jnp.bfloat16)
    )
    new_keys = (
        rotate(key_raw.reshape(req_local, slice_len, KV_HEADS, HEAD), cosine, sine_part)
        .reshape(req_local, slice_len, KV_HEADS * HEAD)
        .astype(jnp.bfloat16)
    )
    new_values = value_raw.reshape(req_local, slice_len, KV_HEADS * HEAD).astype(jnp.bfloat16)
    all_queries = lax.all_gather(queries, "seq", axis=1, tiled=True)
    pad_rows = (-(cache_len_dev + slice_len)) % 128
    key_block = jnp.concatenate(
        [cache_keys, new_keys, jnp.zeros((req_local, pad_rows, KV_HEADS * HEAD), jnp.bfloat16)], axis=1
    )
    value_block = jnp.concatenate(
        [cache_values, new_values, jnp.zeros((req_local, pad_rows, KV_HEADS * HEAD), jnp.bfloat16)],
        axis=1,
    )
    scalars = jnp.concatenate([cache_lengths.astype(jnp.int32), seq_seat.astype(jnp.int32)[None]])
    stats, out_all = block_attention(
        all_queries, key_block, value_block, scalars, cache_len_dev, slice_len, seq_count
    )
    got_stats = lax.all_to_all(stats, "seq", split_axis=0, concat_axis=0, tiled=True)
    got_out = lax.all_to_all(out_all, "seq", split_axis=0, concat_axis=0, tiled=True)
    attended = combine(got_stats, got_out)
    return (attended, new_keys, new_values)


def solution(mesh):
    in_specs = (
        P("req", "seq", None),
        P(),
        P(("req", "seq"), None),
        P(("req", "seq"), None),
        P(("req", "seq"), None),
        P("req", "seq", None),
        P("req", "seq", None),
        P("req"),
    )
    out_specs = (P("req", "seq", None), P("req", "seq", None), P("req", "seq", None))
    return jax.shard_map(body, mesh=mesh, in_specs=in_specs, out_specs=out_specs, check_vma=False)
```

```python
import functools

import jax
import jax.numpy as jnp
from jax import lax
from jax.experimental import pallas as pl
from jax.experimental.pallas import tpu as pltpu
from jax.sharding import PartitionSpec as P

HEADS = 4
KV_HEADS = 2
HEAD = 256


EPSILON = 1e-06
THETA = 1000042.0
MASKED = -1e30


def tables(positions, head_size):
    half_size = head_size // 2
    frequency = THETA ** (-(jnp.arange(half_size, dtype=jnp.float32) * 2.0 / head_size))
    angles = positions.astype(jnp.float32)[..., None] * frequency
    return (jnp.cos(angles)[..., None, :], jnp.sin(angles)[..., None, :])


def rotate(values, cosine, sine_part):
    half_size = values.shape[-1] // 2
    first_half = values[..., :half_size]
    second_half = values[..., half_size:]
    return jnp.concatenate(
        [
            first_half * cosine - second_half * sine_part,
            second_half * cosine + first_half * sine_part,
        ],
        axis=-1,
    )


def attention_kernel(scalar_ref, query_ref, key_ref, value_ref, stats_ref, out_ref, *, cache_len_dev, slice_len):
    request = pl.program_id(0)
    length = scalar_ref[request]
    seat = scalar_ref[scalar_ref.shape[0] - 1]
    span_len = query_ref.shape[1]
    key_rows = key_ref.shape[1]
    blocks = out_ref.shape[0]
    key_index = lax.broadcasted_iota(jnp.int32, (span_len, key_rows), 1)
    query_index = lax.broadcasted_iota(jnp.int32, (span_len, key_rows), 0)
    cache_live = seat * cache_len_dev + key_index < length
    new_live = seat * slice_len + (key_index - cache_len_dev) <= query_index
    in_cache = key_index < cache_len_dev
    in_new = jnp.logical_not(in_cache) & (key_index < cache_len_dev + slice_len)
    live = (in_cache & cache_live) | (in_new & new_live)
    lane = lax.broadcasted_iota(jnp.int32, (span_len, 128), 1)
    stats = jnp.zeros((span_len, 128), jnp.float32)
    group_size = HEADS // KV_HEADS
    for head in range(HEADS):
        group = head // group_size
        query_rows = query_ref[0, :, head * HEAD : (head + 1) * HEAD]
        key_rows_h = key_ref[0, :, group * HEAD : (group + 1) * HEAD]
        value_rows_h = value_ref[0, :, group * HEAD : (group + 1) * HEAD]
        scores = lax.dot_general(
            query_rows, key_rows_h, (((1,), (1,)), ((), ())), preferred_element_type=jnp.float32
        ) * HEAD ** (-0.5)
        scores = jnp.where(live, scores, MASKED)
        block_max = jnp.max(scores, axis=1, keepdims=True)
        weights = jnp.where(live, jnp.exp(scores - block_max), 0.0)
        block_sum = jnp.sum(weights, axis=1, keepdims=True)
        block_out = jnp.dot(
            weights.astype(jnp.bfloat16), value_rows_h, preferred_element_type=jnp.float32
        )
        out_ref[:, 0, :, head * HEAD : (head + 1) * HEAD] = block_out.astype(jnp.bfloat16).reshape(
            blocks, span_len // blocks, HEAD
        )
        stats = jnp.where(lane == head, block_max, stats)
        stats = jnp.where(lane == HEADS + head, block_sum, stats)
    stats_ref[:, 0] = stats[:, : stats_ref.shape[3]].reshape(blocks, span_len // blocks, stats_ref.shape[3])


def block_attention(all_queries, key_block, value_block, scalars, cache_len_dev, slice_len, blocks):
    req_local, span_len, query_width = all_queries.shape
    key_rows = key_block.shape[1]
    kv_width = key_block.shape[2]
    chunk = span_len // blocks
    grid_spec = pltpu.PrefetchScalarGridSpec(
        num_scalar_prefetch=1,
        grid=(req_local,),
        in_specs=[
            pl.BlockSpec((1, span_len, query_width), lambda r, s: (r, 0, 0)),
            pl.BlockSpec((1, key_rows, kv_width), lambda r, s: (r, 0, 0)),
            pl.BlockSpec((1, key_rows, kv_width), lambda r, s: (r, 0, 0)),
        ],
        out_specs=[
            pl.BlockSpec((blocks, 1, chunk, 2 * HEADS), lambda r, s: (0, r, 0, 0)),
            pl.BlockSpec((blocks, 1, chunk, query_width), lambda r, s: (0, r, 0, 0)),
        ],
    )
    return pl.pallas_call(
        functools.partial(attention_kernel, cache_len_dev=cache_len_dev, slice_len=slice_len),
        grid_spec=grid_spec,
        out_shape=[
            jax.ShapeDtypeStruct((blocks, req_local, chunk, 2 * HEADS), jnp.float32),
            jax.ShapeDtypeStruct((blocks, req_local, chunk, query_width), jnp.bfloat16),
        ],
    )(scalars, all_queries, key_block, value_block)


def combine_kernel(stats_ref, out_ref, result_ref):
    blocks, _, chunk, stat_width = stats_ref.shape
    width = out_ref.shape[3]
    top = stats_ref[0, 0]
    for block in range(1, blocks):
        top = jnp.maximum(top, stats_ref[block, 0])
    lane = lax.broadcasted_iota(jnp.int32, (chunk, stat_width), 1)

    def step(block, carry):
        summed, total = carry
        row_stats = stats_ref[block, 0]
        factor = jnp.exp(row_stats - top)
        rows = out_ref[block, 0].astype(jnp.float32)
        pieces = []
        new_total = []
        for head in range(HEADS):
            head_factor = jnp.sum(jnp.where(lane == head, factor, 0.0), axis=1, keepdims=True)
            head_sum = jnp.sum(jnp.where(lane == HEADS + head, row_stats, 0.0), axis=1, keepdims=True)
            pieces.append(summed[head] + rows[:, head * HEAD : (head + 1) * HEAD] * head_factor)
            new_total.append(total[head] + head_factor * head_sum)
        return (tuple(pieces), tuple(new_total))

    start = (
        tuple(jnp.zeros((chunk, HEAD), jnp.float32) for _ in range(HEADS)),
        tuple(jnp.zeros((chunk, 1), jnp.float32) for _ in range(HEADS)),
    )
    summed, total = lax.fori_loop(0, blocks, step, start)
    for head in range(HEADS):
        result_ref[0, :, head * HEAD : (head + 1) * HEAD] = (summed[head] / total[head]).astype(
            result_ref.dtype
        )


def combine(got_stats, got_out):
    blocks, req_local, chunk, stat_width = got_stats.shape
    width = got_out.shape[3]
    return pl.pallas_call(
        combine_kernel,
        grid=(req_local,),
        in_specs=[
            pl.BlockSpec((blocks, 1, chunk, stat_width), lambda r: (0, r, 0, 0)),
            pl.BlockSpec((blocks, 1, chunk, width), lambda r: (0, r, 0, 0)),
        ],
        out_specs=pl.BlockSpec((1, chunk, width), lambda r: (r, 0, 0)),
        out_shape=jax.ShapeDtypeStruct((req_local, chunk, width), jnp.bfloat16),
    )(got_stats, got_out)


def gather_by_doubling(rows, axis_name, count):
    seat = lax.axis_index(axis_name)
    distance = 1
    while distance < count:
        pairs = [(source, source ^ distance) for source in range(count)]
        other = lax.ppermute(rows, axis_name, pairs)
        low_first = jnp.concatenate([rows, other], axis=0)
        high_first = jnp.concatenate([other, rows], axis=0)
        rows = jnp.where((seat & distance) == 0, low_first, high_first)
        distance *= 2
    return rows


def body(hidden_in, norm_gain, w_query, w_key, w_value, cache_keys, cache_values, cache_lengths):
    seq_count = lax.axis_size("seq")
    seq_seat = lax.axis_index("seq")
    req_local, slice_len, model_width = hidden_in.shape
    cache_len_dev = cache_keys.shape[1]
    span_len = slice_len * seq_count
    inputs = hidden_in.astype(jnp.float32)
    normed = (
        inputs * lax.rsqrt(jnp.mean(inputs * inputs, axis=-1, keepdims=True) + EPSILON) * norm_gain
    ).astype(jnp.bfloat16)
    flat_rows = normed.reshape(req_local * slice_len, model_width)
    req_count = lax.axis_size("req")
    row_local = w_query.shape[0]
    query_cols = w_query.shape[1]
    key_cols = w_key.shape[1]
    joined = jnp.concatenate([w_query, w_key, w_value], axis=1)
    joined = gather_by_doubling(joined, "req", req_count)
    joined = lax.all_gather(joined, "seq", axis=0, tiled=True)
    permuted_rows = (
        flat_rows.reshape(-1, req_count, seq_count, row_local)
        .transpose(0, 2, 1, 3)
        .reshape(-1, model_width)
    )
    projected = jnp.dot(permuted_rows, joined, preferred_element_type=jnp.float32)
    query_raw = projected[:, :query_cols]
    key_raw = projected[:, query_cols : query_cols + key_cols]
    value_raw = projected[:, query_cols + key_cols :]
    local_index = jnp.arange(slice_len, dtype=jnp.int32)
    positions = cache_lengths[:, None] + seq_seat * slice_len + local_index[None, :]
    cosine, sine_part = tables(positions, HEAD)
    queries = (
        rotate(query_raw.reshape(req_local, slice_len, HEADS, HEAD), cosine, sine_part)
        .reshape(req_local, slice_len, HEADS * HEAD)
        .astype(jnp.bfloat16)
    )
    new_keys = (
        rotate(key_raw.reshape(req_local, slice_len, KV_HEADS, HEAD), cosine, sine_part)
        .reshape(req_local, slice_len, KV_HEADS * HEAD)
        .astype(jnp.bfloat16)
    )
    new_values = value_raw.reshape(req_local, slice_len, KV_HEADS * HEAD).astype(jnp.bfloat16)
    all_queries = lax.all_gather(queries, "seq", axis=1, tiled=True)
    pad_rows = (-(cache_len_dev + slice_len)) % 128
    key_block = jnp.concatenate(
        [cache_keys, new_keys, jnp.zeros((req_local, pad_rows, KV_HEADS * HEAD), jnp.bfloat16)], axis=1
    )
    value_block = jnp.concatenate(
        [cache_values, new_values, jnp.zeros((req_local, pad_rows, KV_HEADS * HEAD), jnp.bfloat16)],
        axis=1,
    )
    scalars = jnp.concatenate([cache_lengths.astype(jnp.int32), seq_seat.astype(jnp.int32)[None]])
    stats, out_all = block_attention(
        all_queries, key_block, value_block, scalars, cache_len_dev, slice_len, seq_count
    )
    got_stats = lax.all_to_all(stats, "seq", split_axis=0, concat_axis=0, tiled=True)
    got_out = lax.all_to_all(out_all, "seq", split_axis=0, concat_axis=0, tiled=True)
    attended = combine(got_stats, got_out)
    return (attended, new_keys, new_values)


def solution(mesh):
    in_specs = (
        P("req", "seq", None),
        P(),
        P(("req", "seq"), None),
        P(("req", "seq"), None),
        P(("req", "seq"), None),
        P("req", "seq", None),
        P("req", "seq", None),
        P("req"),
    )
    out_specs = (P("req", "seq", None), P("req", "seq", None), P("req", "seq", None))
    return jax.shard_map(body, mesh=mesh, in_specs=in_specs, out_specs=out_specs, check_vma=False)
```

```python
import functools

import jax
import jax.numpy as jnp
from jax import lax
from jax.experimental import pallas as pl
from jax.experimental.pallas import tpu as pltpu
from jax.sharding import PartitionSpec as P

HEADS = 4
KV_HEADS = 2
HEAD = 256


EPSILON = 1e-06
THETA = 1000042.0
MASKED = -1e30


def tables(positions, head_size):
    half_size = head_size // 2
    frequency = THETA ** (-(jnp.arange(half_size, dtype=jnp.float32) * 2.0 / head_size))
    angles = positions.astype(jnp.float32)[..., None] * frequency
    return (jnp.cos(angles)[..., None, :], jnp.sin(angles)[..., None, :])


def rotate(values, cosine, sine_part):
    half_size = values.shape[-1] // 2
    first_half = values[..., :half_size]
    second_half = values[..., half_size:]
    return jnp.concatenate(
        [
            first_half * cosine - second_half * sine_part,
            second_half * cosine + first_half * sine_part,
        ],
        axis=-1,
    )


def attention_kernel(scalar_ref, query_ref, key_ref, value_ref, out_ref, *, cache_len_dev, slice_len):
    request = pl.program_id(0)
    length = scalar_ref[request]
    seat = scalar_ref[scalar_ref.shape[0] - 1]
    span_len = query_ref.shape[1]
    key_rows = key_ref.shape[1]
    blocks = out_ref.shape[0]
    key_index = lax.broadcasted_iota(jnp.int32, (span_len, key_rows), 1)
    query_index = lax.broadcasted_iota(jnp.int32, (span_len, key_rows), 0)
    cache_live = seat * cache_len_dev + key_index < length
    new_live = seat * slice_len + (key_index - cache_len_dev) <= query_index
    in_cache = key_index < cache_len_dev
    in_new = jnp.logical_not(in_cache) & (key_index < cache_len_dev + slice_len)
    live = (in_cache & cache_live) | (in_new & new_live)
    lane = lax.broadcasted_iota(jnp.int32, (span_len, 128), 1)
    stats = jnp.zeros((span_len, 128), jnp.float32)
    group_size = HEADS // KV_HEADS
    for head in range(HEADS):
        group = head // group_size
        query_rows = query_ref[0, :, head * HEAD : (head + 1) * HEAD]
        key_rows_h = key_ref[0, :, group * HEAD : (group + 1) * HEAD]
        value_rows_h = value_ref[0, :, group * HEAD : (group + 1) * HEAD]
        scores = lax.dot_general(
            query_rows, key_rows_h, (((1,), (1,)), ((), ())), preferred_element_type=jnp.float32
        ) * HEAD ** (-0.5)
        scores = jnp.where(live, scores, MASKED)
        block_max = jnp.max(scores, axis=1, keepdims=True)
        weights = jnp.where(live, jnp.exp(scores - block_max), 0.0)
        block_sum = jnp.sum(weights, axis=1, keepdims=True)
        block_out = jnp.dot(
            weights.astype(jnp.bfloat16), value_rows_h, preferred_element_type=jnp.float32
        )
        out_ref[:, 0, :, head * HEAD : (head + 1) * HEAD] = block_out.astype(jnp.bfloat16).reshape(
            blocks, span_len // blocks, HEAD
        )
        stats = jnp.where(lane == head, block_max, stats)
        stats = jnp.where(lane == HEADS + head, block_sum, stats)
    first = stats.astype(jnp.bfloat16).astype(jnp.float32)
    rest = stats - first
    second = rest.astype(jnp.bfloat16).astype(jnp.float32)
    third = (rest - second).astype(jnp.bfloat16).astype(jnp.float32)
    width = 2 * HEADS
    packed = jnp.where(
        lane < width,
        first,
        jnp.where(
            lane < 2 * width,
            pltpu.roll(second, width, 1),
            jnp.where(lane < 3 * width, pltpu.roll(third, 2 * width, 1), 0.0),
        ),
    )
    out_ref[:, 0, :, HEADS * HEAD :] = packed.astype(jnp.bfloat16).reshape(
        blocks, span_len // blocks, 128
    )


def block_attention(all_queries, key_block, value_block, scalars, cache_len_dev, slice_len, blocks):
    req_local, span_len, query_width = all_queries.shape
    key_rows = key_block.shape[1]
    kv_width = key_block.shape[2]
    chunk = span_len // blocks
    grid_spec = pltpu.PrefetchScalarGridSpec(
        num_scalar_prefetch=1,
        grid=(req_local,),
        in_specs=[
            pl.BlockSpec((1, span_len, query_width), lambda r, s: (r, 0, 0)),
            pl.BlockSpec((1, key_rows, kv_width), lambda r, s: (r, 0, 0)),
            pl.BlockSpec((1, key_rows, kv_width), lambda r, s: (r, 0, 0)),
        ],
        out_specs=pl.BlockSpec((blocks, 1, chunk, query_width + 128), lambda r, s: (0, r, 0, 0)),
    )
    return pl.pallas_call(
        functools.partial(attention_kernel, cache_len_dev=cache_len_dev, slice_len=slice_len),
        grid_spec=grid_spec,
        out_shape=jax.ShapeDtypeStruct((blocks, req_local, chunk, query_width + 128), jnp.bfloat16),
    )(scalars, all_queries, key_block, value_block)


def combine_kernel(out_ref, result_ref):
    blocks, _, chunk, padded = out_ref.shape
    width = HEADS * HEAD
    stat_width = 2 * HEADS
    lane = lax.broadcasted_iota(jnp.int32, (chunk, 128), 1)

    def block_stats(block):
        packed = out_ref[block, 0, :, width:].astype(jnp.float32)
        return (packed + pltpu.roll(packed, 128 - stat_width, 1)) + pltpu.roll(packed, 128 - 2 * stat_width, 1)

    top = block_stats(0)
    for block in range(1, blocks):
        top = jnp.maximum(top, block_stats(block))
    top = jnp.where(lane < HEADS, top, 0.0)

    def step(block, carry):
        summed, total = carry
        row_stats = block_stats(block)
        factor = jnp.exp(jnp.where(lane < HEADS, row_stats, 0.0) - top)
        pieces = []
        new_total = []
        for head in range(HEADS):
            head_factor = jnp.sum(jnp.where(lane == head, factor, 0.0), axis=1, keepdims=True)
            head_sum = jnp.sum(jnp.where(lane == HEADS + head, row_stats, 0.0), axis=1, keepdims=True)
            rows = out_ref[block, 0, :, head * HEAD : (head + 1) * HEAD].astype(jnp.float32)
            pieces.append(summed[head] + rows * head_factor)
            new_total.append(total[head] + head_factor * head_sum)
        return (tuple(pieces), tuple(new_total))

    start = (
        tuple(jnp.zeros((chunk, HEAD), jnp.float32) for _ in range(HEADS)),
        tuple(jnp.zeros((chunk, 1), jnp.float32) for _ in range(HEADS)),
    )
    summed, total = lax.fori_loop(0, blocks, step, start)
    for head in range(HEADS):
        result_ref[0, :, head * HEAD : (head + 1) * HEAD] = (summed[head] / total[head]).astype(
            result_ref.dtype
        )


def combine(got_out):
    blocks, req_local, chunk, padded = got_out.shape
    width = HEADS * HEAD
    return pl.pallas_call(
        combine_kernel,
        grid=(req_local,),
        in_specs=[pl.BlockSpec((blocks, 1, chunk, padded), lambda r: (0, r, 0, 0))],
        out_specs=pl.BlockSpec((1, chunk, width), lambda r: (r, 0, 0)),
        out_shape=jax.ShapeDtypeStruct((req_local, chunk, width), jnp.bfloat16),
    )(got_out)


def gather_by_doubling(rows, axis_name, count):
    seat = lax.axis_index(axis_name)
    distance = 1
    while distance < count:
        pairs = [(source, source ^ distance) for source in range(count)]
        other = lax.ppermute(rows, axis_name, pairs)
        low_first = jnp.concatenate([rows, other], axis=0)
        high_first = jnp.concatenate([other, rows], axis=0)
        rows = jnp.where((seat & distance) == 0, low_first, high_first)
        distance *= 2
    return rows


def body(hidden_in, norm_gain, w_query, w_key, w_value, cache_keys, cache_values, cache_lengths):
    seq_count = lax.axis_size("seq")
    seq_seat = lax.axis_index("seq")
    req_local, slice_len, model_width = hidden_in.shape
    cache_len_dev = cache_keys.shape[1]
    span_len = slice_len * seq_count
    inputs = hidden_in.astype(jnp.float32)
    normed = (
        inputs * lax.rsqrt(jnp.mean(inputs * inputs, axis=-1, keepdims=True) + EPSILON) * norm_gain
    ).astype(jnp.bfloat16)
    flat_rows = normed.reshape(req_local * slice_len, model_width)
    req_count = lax.axis_size("req")
    row_local = w_query.shape[0]
    query_cols = w_query.shape[1]
    key_cols = w_key.shape[1]
    joined = jnp.concatenate([w_query, w_key, w_value], axis=1)
    joined = gather_by_doubling(joined, "req", req_count)
    joined = lax.all_gather(joined, "seq", axis=0, tiled=True)
    permuted_rows = (
        flat_rows.reshape(-1, req_count, seq_count, row_local)
        .transpose(0, 2, 1, 3)
        .reshape(-1, model_width)
    )
    projected = jnp.dot(permuted_rows, joined, preferred_element_type=jnp.float32)
    query_raw = projected[:, :query_cols]
    key_raw = projected[:, query_cols : query_cols + key_cols]
    value_raw = projected[:, query_cols + key_cols :]
    local_index = jnp.arange(slice_len, dtype=jnp.int32)
    positions = cache_lengths[:, None] + seq_seat * slice_len + local_index[None, :]
    cosine, sine_part = tables(positions, HEAD)
    queries = (
        rotate(query_raw.reshape(req_local, slice_len, HEADS, HEAD), cosine, sine_part)
        .reshape(req_local, slice_len, HEADS * HEAD)
        .astype(jnp.bfloat16)
    )
    new_keys = (
        rotate(key_raw.reshape(req_local, slice_len, KV_HEADS, HEAD), cosine, sine_part)
        .reshape(req_local, slice_len, KV_HEADS * HEAD)
        .astype(jnp.bfloat16)
    )
    new_values = value_raw.reshape(req_local, slice_len, KV_HEADS * HEAD).astype(jnp.bfloat16)
    all_queries = lax.all_gather(queries, "seq", axis=1, tiled=True)
    pad_rows = (-(cache_len_dev + slice_len)) % 128
    key_block = jnp.concatenate(
        [cache_keys, new_keys, jnp.zeros((req_local, pad_rows, KV_HEADS * HEAD), jnp.bfloat16)], axis=1
    )
    value_block = jnp.concatenate(
        [cache_values, new_values, jnp.zeros((req_local, pad_rows, KV_HEADS * HEAD), jnp.bfloat16)],
        axis=1,
    )
    scalars = jnp.concatenate([cache_lengths.astype(jnp.int32), seq_seat.astype(jnp.int32)[None]])
    out_all = block_attention(
        all_queries, key_block, value_block, scalars, cache_len_dev, slice_len, seq_count
    )
    got_out = lax.all_to_all(out_all, "seq", split_axis=0, concat_axis=0, tiled=True)
    attended = combine(got_out)
    return (attended, new_keys, new_values)


def solution(mesh):
    in_specs = (
        P("req", "seq", None),
        P(),
        P(("req", "seq"), None),
        P(("req", "seq"), None),
        P(("req", "seq"), None),
        P("req", "seq", None),
        P("req", "seq", None),
        P("req"),
    )
    out_specs = (P("req", "seq", None), P("req", "seq", None), P("req", "seq", None))
    return jax.shard_map(body, mesh=mesh, in_specs=in_specs, out_specs=out_specs, check_vma=False)
```

```python
import functools

import jax
import jax.numpy as jnp
from jax import lax
from jax.experimental import pallas as pl
from jax.experimental.pallas import tpu as pltpu
from jax.sharding import PartitionSpec as P

HEADS = 4
KV_HEADS = 2
HEAD = 256


EPSILON = 1e-06
THETA = 1000042.0
MASKED = -1e30


def tables(positions, head_size):
    half_size = head_size // 2
    frequency = THETA ** (-(jnp.arange(half_size, dtype=jnp.float32) * 2.0 / head_size))
    angles = positions.astype(jnp.float32)[..., None] * frequency
    return (jnp.cos(angles)[..., None, :], jnp.sin(angles)[..., None, :])


def rotate(values, cosine, sine_part):
    half_size = values.shape[-1] // 2
    first_half = values[..., :half_size]
    second_half = values[..., half_size:]
    return jnp.concatenate(
        [
            first_half * cosine - second_half * sine_part,
            second_half * cosine + first_half * sine_part,
        ],
        axis=-1,
    )


def attention_kernel(scalar_ref, query_ref, key_ref, value_ref, out_ref, *, cache_len_dev, slice_len):
    request = pl.program_id(0)
    length = scalar_ref[request]
    seat = scalar_ref[scalar_ref.shape[0] - 1]
    span_len = query_ref.shape[1]
    key_rows = key_ref.shape[1]
    blocks = out_ref.shape[0]
    key_index = lax.broadcasted_iota(jnp.int32, (span_len, key_rows), 1)
    query_index = lax.broadcasted_iota(jnp.int32, (span_len, key_rows), 0)
    cache_live = seat * cache_len_dev + key_index < length
    new_live = seat * slice_len + (key_index - cache_len_dev) <= query_index
    in_cache = key_index < cache_len_dev
    in_new = jnp.logical_not(in_cache) & (key_index < cache_len_dev + slice_len)
    live = (in_cache & cache_live) | (in_new & new_live)
    lane = lax.broadcasted_iota(jnp.int32, (span_len, 128), 1)
    stats = jnp.zeros((span_len, 128), jnp.float32)
    group_size = HEADS // KV_HEADS
    for head in range(HEADS):
        group = head // group_size
        query_rows = query_ref[0, :, head * HEAD : (head + 1) * HEAD]
        key_rows_h = key_ref[0, :, group * HEAD : (group + 1) * HEAD]
        value_rows_h = value_ref[0, :, group * HEAD : (group + 1) * HEAD]
        scores = lax.dot_general(
            query_rows, key_rows_h, (((1,), (1,)), ((), ())), preferred_element_type=jnp.float32
        ) * HEAD ** (-0.5)
        scores = jnp.where(live, scores, MASKED)
        block_max = jnp.max(scores, axis=1, keepdims=True)
        weights = jnp.where(live, jnp.exp(scores - block_max), 0.0)
        block_sum = jnp.sum(weights, axis=1, keepdims=True)
        block_out = jnp.dot(
            weights.astype(jnp.bfloat16), value_rows_h, preferred_element_type=jnp.float32
        )
        out_ref[:, 0, :, head * HEAD : (head + 1) * HEAD] = block_out.astype(jnp.bfloat16).reshape(
            blocks, span_len // blocks, HEAD
        )
        stats = jnp.where(lane == head, block_max, stats)
        stats = jnp.where(lane == HEADS + head, block_sum, stats)
    first = stats.astype(jnp.bfloat16).astype(jnp.float32)
    rest = stats - first
    second = rest.astype(jnp.bfloat16).astype(jnp.float32)
    third = (rest - second).astype(jnp.bfloat16).astype(jnp.float32)
    width = 2 * HEADS
    packed = jnp.where(
        lane < width,
        first,
        jnp.where(
            lane < 2 * width,
            pltpu.roll(second, width, 1),
            jnp.where(lane < 3 * width, pltpu.roll(third, 2 * width, 1), 0.0),
        ),
    )
    out_ref[:, 0, :, HEADS * HEAD :] = packed.astype(jnp.bfloat16).reshape(
        blocks, span_len // blocks, 128
    )


def block_attention(all_queries, key_block, value_block, scalars, cache_len_dev, slice_len, blocks):
    req_local, span_len, query_width = all_queries.shape
    key_rows = key_block.shape[1]
    kv_width = key_block.shape[2]
    chunk = span_len // blocks
    grid_spec = pltpu.PrefetchScalarGridSpec(
        num_scalar_prefetch=1,
        grid=(req_local,),
        in_specs=[
            pl.BlockSpec((1, span_len, query_width), lambda r, s: (r, 0, 0)),
            pl.BlockSpec((1, key_rows, kv_width), lambda r, s: (r, 0, 0)),
            pl.BlockSpec((1, key_rows, kv_width), lambda r, s: (r, 0, 0)),
        ],
        out_specs=pl.BlockSpec((blocks, 1, chunk, query_width + 128), lambda r, s: (0, r, 0, 0)),
    )
    return pl.pallas_call(
        functools.partial(attention_kernel, cache_len_dev=cache_len_dev, slice_len=slice_len),
        grid_spec=grid_spec,
        out_shape=jax.ShapeDtypeStruct((blocks, req_local, chunk, query_width + 128), jnp.bfloat16),
    )(scalars, all_queries, key_block, value_block)


def combine_kernel(out_ref, result_ref):
    blocks, _, chunk, padded = out_ref.shape
    width = HEADS * HEAD
    stat_width = 2 * HEADS
    lane = lax.broadcasted_iota(jnp.int32, (chunk, 128), 1)

    def block_stats(block):
        packed = out_ref[block, 0, :, width:].astype(jnp.float32)
        return (packed + pltpu.roll(packed, 128 - stat_width, 1)) + pltpu.roll(packed, 128 - 2 * stat_width, 1)

    top = block_stats(0)
    for block in range(1, blocks):
        top = jnp.maximum(top, block_stats(block))
    top = jnp.where(lane < HEADS, top, 0.0)

    def step(block, carry):
        summed, total = carry
        row_stats = block_stats(block)
        factor = jnp.exp(jnp.where(lane < HEADS, row_stats, 0.0) - top)
        pieces = []
        new_total = []
        for head in range(HEADS):
            head_factor = jnp.sum(jnp.where(lane == head, factor, 0.0), axis=1, keepdims=True)
            head_sum = jnp.sum(jnp.where(lane == HEADS + head, row_stats, 0.0), axis=1, keepdims=True)
            rows = out_ref[block, 0, :, head * HEAD : (head + 1) * HEAD].astype(jnp.float32)
            pieces.append(summed[head] + rows * head_factor)
            new_total.append(total[head] + head_factor * head_sum)
        return (tuple(pieces), tuple(new_total))

    start = (
        tuple(jnp.zeros((chunk, HEAD), jnp.float32) for _ in range(HEADS)),
        tuple(jnp.zeros((chunk, 1), jnp.float32) for _ in range(HEADS)),
    )
    summed, total = lax.fori_loop(0, blocks, step, start, unroll=4)
    for head in range(HEADS):
        result_ref[0, :, head * HEAD : (head + 1) * HEAD] = (summed[head] / total[head]).astype(
            result_ref.dtype
        )


def combine(got_out):
    blocks, req_local, chunk, padded = got_out.shape
    width = HEADS * HEAD
    return pl.pallas_call(
        combine_kernel,
        grid=(req_local,),
        in_specs=[pl.BlockSpec((blocks, 1, chunk, padded), lambda r: (0, r, 0, 0))],
        out_specs=pl.BlockSpec((1, chunk, width), lambda r: (r, 0, 0)),
        out_shape=jax.ShapeDtypeStruct((req_local, chunk, width), jnp.bfloat16),
    )(got_out)


def gather_by_shifts(rows, axis_name, count):
    seat = lax.axis_index(axis_name)
    shifted = [rows]
    for distance in range(1, count):
        pairs = [(source, (source + distance) % count) for source in range(count)]
        shifted.append(lax.ppermute(rows, axis_name, pairs))
    stacked = jnp.stack(shifted)
    order = (seat - jnp.arange(count, dtype=jnp.int32)) % count
    return jnp.take(stacked, order, axis=0).reshape(count * rows.shape[0], rows.shape[1])


def body(hidden_in, norm_gain, w_query, w_key, w_value, cache_keys, cache_values, cache_lengths):
    seq_count = lax.axis_size("seq")
    seq_seat = lax.axis_index("seq")
    req_local, slice_len, model_width = hidden_in.shape
    cache_len_dev = cache_keys.shape[1]
    span_len = slice_len * seq_count
    inputs = hidden_in.astype(jnp.float32)
    normed = (
        inputs * lax.rsqrt(jnp.mean(inputs * inputs, axis=-1, keepdims=True) + EPSILON) * norm_gain
    ).astype(jnp.bfloat16)
    flat_rows = normed.reshape(req_local * slice_len, model_width)
    req_count = lax.axis_size("req")
    row_local = w_query.shape[0]
    query_cols = w_query.shape[1]
    key_cols = w_key.shape[1]
    joined = jnp.concatenate([w_query, w_key, w_value], axis=1)
    joined = gather_by_shifts(joined, "req", req_count)
    joined = lax.all_gather(joined, "seq", axis=0, tiled=True)
    permuted_rows = (
        flat_rows.reshape(-1, req_count, seq_count, row_local)
        .transpose(0, 2, 1, 3)
        .reshape(-1, model_width)
    )
    projected = jnp.dot(permuted_rows, joined, preferred_element_type=jnp.float32)
    query_raw = projected[:, :query_cols]
    key_raw = projected[:, query_cols : query_cols + key_cols]
    value_raw = projected[:, query_cols + key_cols :]
    local_index = jnp.arange(slice_len, dtype=jnp.int32)
    positions = cache_lengths[:, None] + seq_seat * slice_len + local_index[None, :]
    cosine, sine_part = tables(positions, HEAD)
    queries = (
        rotate(query_raw.reshape(req_local, slice_len, HEADS, HEAD), cosine, sine_part)
        .reshape(req_local, slice_len, HEADS * HEAD)
        .astype(jnp.bfloat16)
    )
    new_keys = (
        rotate(key_raw.reshape(req_local, slice_len, KV_HEADS, HEAD), cosine, sine_part)
        .reshape(req_local, slice_len, KV_HEADS * HEAD)
        .astype(jnp.bfloat16)
    )
    new_values = value_raw.reshape(req_local, slice_len, KV_HEADS * HEAD).astype(jnp.bfloat16)
    all_queries = lax.all_gather(queries, "seq", axis=1, tiled=True)
    pad_rows = (-(cache_len_dev + slice_len)) % 128
    key_block = jnp.concatenate(
        [cache_keys, new_keys, jnp.zeros((req_local, pad_rows, KV_HEADS * HEAD), jnp.bfloat16)], axis=1
    )
    value_block = jnp.concatenate(
        [cache_values, new_values, jnp.zeros((req_local, pad_rows, KV_HEADS * HEAD), jnp.bfloat16)],
        axis=1,
    )
    scalars = jnp.concatenate([cache_lengths.astype(jnp.int32), seq_seat.astype(jnp.int32)[None]])
    out_all = block_attention(
        all_queries, key_block, value_block, scalars, cache_len_dev, slice_len, seq_count
    )
    got_out = lax.all_to_all(out_all, "seq", split_axis=0, concat_axis=0, tiled=True)
    attended = combine(got_out)
    return (attended, new_keys, new_values)


def solution(mesh):
    in_specs = (
        P("req", "seq", None),
        P(),
        P(("req", "seq"), None),
        P(("req", "seq"), None),
        P(("req", "seq"), None),
        P("req", "seq", None),
        P("req", "seq", None),
        P("req"),
    )
    out_specs = (P("req", "seq", None), P("req", "seq", None), P("req", "seq", None))
    return jax.shard_map(body, mesh=mesh, in_specs=in_specs, out_specs=out_specs, check_vma=False)
```

```python
import functools

import jax
import jax.numpy as jnp
from jax import lax
from jax.experimental import pallas as pl
from jax.experimental.pallas import tpu as pltpu
from jax.sharding import Mesh
from jax.sharding import PartitionSpec as P

HEADS = 4
KV_HEADS = 2
HEAD = 256


EPSILON = 1e-06
THETA = 1000042.0
MASKED = -1e30
SEQ = ("sq", "core")


def tables(positions, head_size):
    half_size = head_size // 2
    frequency = THETA ** (-(jnp.arange(half_size, dtype=jnp.float32) * 2.0 / head_size))
    angles = positions.astype(jnp.float32)[..., None] * frequency
    return (jnp.cos(angles)[..., None, :], jnp.sin(angles)[..., None, :])


def rotate(values, cosine, sine_part):
    half_size = values.shape[-1] // 2
    first_half = values[..., :half_size]
    second_half = values[..., half_size:]
    return jnp.concatenate(
        [
            first_half * cosine - second_half * sine_part,
            second_half * cosine + first_half * sine_part,
        ],
        axis=-1,
    )


def pack_stats(stats, lane):
    width = 2 * HEADS
    first = stats.astype(jnp.bfloat16).astype(jnp.float32)
    rest = stats - first
    second = rest.astype(jnp.bfloat16).astype(jnp.float32)
    third = (rest - second).astype(jnp.bfloat16).astype(jnp.float32)
    return jnp.where(
        lane < width,
        first,
        jnp.where(
            lane < 2 * width,
            pltpu.roll(second, width, 1),
            jnp.where(lane < 3 * width, pltpu.roll(third, 2 * width, 1), 0.0),
        ),
    )


def unpack_stats(packed):
    width = 2 * HEADS
    return (packed + pltpu.roll(packed, 128 - width, 1)) + pltpu.roll(packed, 128 - 2 * width, 1)


def attention_kernel(scalar_ref, query_ref, key_ref, value_ref, out_ref, *, cache_len_dev, slice_len):
    request = pl.program_id(0)
    length = scalar_ref[request]
    seat = scalar_ref[scalar_ref.shape[0] - 1]
    span_len = query_ref.shape[1]
    key_rows = key_ref.shape[1]
    blocks = out_ref.shape[0]
    key_index = lax.broadcasted_iota(jnp.int32, (span_len, key_rows), 1)
    query_index = lax.broadcasted_iota(jnp.int32, (span_len, key_rows), 0)
    cache_live = seat * cache_len_dev + key_index < length
    new_live = seat * slice_len + (key_index - cache_len_dev) <= query_index
    in_cache = key_index < cache_len_dev
    in_new = jnp.logical_not(in_cache) & (key_index < cache_len_dev + slice_len)
    live = (in_cache & cache_live) | (in_new & new_live)
    lane = lax.broadcasted_iota(jnp.int32, (span_len, 128), 1)
    stats = jnp.zeros((span_len, 128), jnp.float32)
    group_size = HEADS // KV_HEADS
    for head in range(HEADS):
        group = head // group_size
        query_rows = query_ref[0, :, head * HEAD : (head + 1) * HEAD]
        key_rows_h = key_ref[0, :, group * HEAD : (group + 1) * HEAD]
        value_rows_h = value_ref[0, :, group * HEAD : (group + 1) * HEAD]
        scores = lax.dot_general(
            query_rows, key_rows_h, (((1,), (1,)), ((), ())), preferred_element_type=jnp.float32
        ) * HEAD ** (-0.5)
        scores = jnp.where(live, scores, MASKED)
        block_max = jnp.max(scores, axis=1, keepdims=True)
        weights = jnp.where(live, jnp.exp(scores - block_max), 0.0)
        block_sum = jnp.sum(weights, axis=1, keepdims=True)
        block_out = jnp.dot(
            weights.astype(jnp.bfloat16), value_rows_h, preferred_element_type=jnp.float32
        )
        out_ref[:, 0, :, head * HEAD : (head + 1) * HEAD] = block_out.astype(jnp.bfloat16).reshape(
            blocks, span_len // blocks, HEAD
        )
        stats = jnp.where(lane == head, block_max, stats)
        stats = jnp.where(lane == HEADS + head, block_sum, stats)
    packed = pack_stats(stats, lane)
    out_ref[:, 0, :, HEADS * HEAD :] = packed.astype(jnp.bfloat16).reshape(
        blocks, span_len // blocks, 128
    )


def block_attention(all_queries, key_block, value_block, scalars, cache_len_dev, slice_len, blocks):
    req_local, span_len, query_width = all_queries.shape
    key_rows = key_block.shape[1]
    kv_width = key_block.shape[2]
    chunk = span_len // blocks
    grid_spec = pltpu.PrefetchScalarGridSpec(
        num_scalar_prefetch=1,
        grid=(req_local,),
        in_specs=[
            pl.BlockSpec((1, span_len, query_width), lambda r, s: (r, 0, 0)),
            pl.BlockSpec((1, key_rows, kv_width), lambda r, s: (r, 0, 0)),
            pl.BlockSpec((1, key_rows, kv_width), lambda r, s: (r, 0, 0)),
        ],
        out_specs=pl.BlockSpec((blocks, 1, chunk, query_width + 128), lambda r, s: (0, r, 0, 0)),
    )
    return pl.pallas_call(
        functools.partial(attention_kernel, cache_len_dev=cache_len_dev, slice_len=slice_len),
        grid_spec=grid_spec,
        out_shape=jax.ShapeDtypeStruct((blocks, req_local, chunk, query_width + 128), jnp.bfloat16),
    )(scalars, all_queries, key_block, value_block)


def combine_kernel(out_ref, result_ref):
    blocks, _, chunk, padded = out_ref.shape
    width = HEADS * HEAD
    stat_width = 2 * HEADS
    lane = lax.broadcasted_iota(jnp.int32, (chunk, 128), 1)

    def block_stats(block):
        return unpack_stats(out_ref[block, 0, :, width:].astype(jnp.float32))

    top = block_stats(0)
    for block in range(1, blocks):
        top = jnp.maximum(top, block_stats(block))
    top = jnp.where(lane < HEADS, top, 0.0)

    def step(block, carry):
        summed, total = carry
        row_stats = block_stats(block)
        factor = jnp.exp(jnp.where(lane < HEADS, row_stats, 0.0) - top)
        pieces = []
        new_total = []
        for head in range(HEADS):
            head_factor = jnp.sum(jnp.where(lane == head, factor, 0.0), axis=1, keepdims=True)
            head_sum = jnp.sum(jnp.where(lane == HEADS + head, row_stats, 0.0), axis=1, keepdims=True)
            rows = out_ref[block, 0, :, head * HEAD : (head + 1) * HEAD].astype(jnp.float32)
            pieces.append(summed[head] + rows * head_factor)
            new_total.append(total[head] + head_factor * head_sum)
        return (tuple(pieces), tuple(new_total))

    start = (
        tuple(jnp.zeros((chunk, HEAD), jnp.float32) for _ in range(HEADS)),
        tuple(jnp.zeros((chunk, 1), jnp.float32) for _ in range(HEADS)),
    )
    summed, total = lax.fori_loop(0, blocks, step, start, unroll=4)
    for head in range(HEADS):
        result_ref[0, :, head * HEAD : (head + 1) * HEAD] = (summed[head] / total[head]).astype(
            result_ref.dtype
        )


def combine(got_out):
    blocks, req_local, chunk, padded = got_out.shape
    width = HEADS * HEAD
    return pl.pallas_call(
        combine_kernel,
        grid=(req_local,),
        in_specs=[pl.BlockSpec((blocks, 1, chunk, padded), lambda r: (0, r, 0, 0))],
        out_specs=pl.BlockSpec((1, chunk, width), lambda r: (r, 0, 0)),
        out_shape=jax.ShapeDtypeStruct((req_local, chunk, width), jnp.bfloat16),
    )(got_out)


def merge_kernel(pair_ref, merged_ref):
    dests, _, _, chunk, padded = pair_ref.shape
    width = HEADS * HEAD
    lane = lax.broadcasted_iota(jnp.int32, (chunk, 128), 1)

    def step(dest, carry):
        first = unpack_stats(pair_ref[dest, 0, 0, :, width:].astype(jnp.float32))
        second = unpack_stats(pair_ref[dest, 1, 0, :, width:].astype(jnp.float32))
        first_max = jnp.where(lane < HEADS, first, 0.0)
        second_max = jnp.where(lane < HEADS, second, 0.0)
        best = jnp.maximum(first_max, second_max)
        first_factor = jnp.exp(first_max - best)
        second_factor = jnp.exp(second_max - best)
        stats = best
        for head in range(HEADS):
            pick = lane == head
            first_head = jnp.sum(jnp.where(pick, first_factor, 0.0), axis=1, keepdims=True)
            second_head = jnp.sum(jnp.where(pick, second_factor, 0.0), axis=1, keepdims=True)
            take = lane == HEADS + head
            first_sum = jnp.sum(jnp.where(take, first, 0.0), axis=1, keepdims=True)
            second_sum = jnp.sum(jnp.where(take, second, 0.0), axis=1, keepdims=True)
            stats = jnp.where(take, first_head * first_sum + second_head * second_sum, stats)
            columns = slice(head * HEAD, (head + 1) * HEAD)
            partial = (
                pair_ref[dest, 0, 0, :, columns].astype(jnp.float32) * first_head
                + pair_ref[dest, 1, 0, :, columns].astype(jnp.float32) * second_head
            )
            merged_ref[dest, 0, :, columns] = partial.astype(merged_ref.dtype)
        merged_ref[dest, 0, :, width:] = pack_stats(stats, lane).astype(merged_ref.dtype)
        return carry

    lax.fori_loop(0, dests, step, 0, unroll=4)


def merge_pairs(pair):
    dests, sources, req_local, chunk, padded = pair.shape
    return pl.pallas_call(
        merge_kernel,
        grid=(req_local,),
        in_specs=[pl.BlockSpec((dests, sources, 1, chunk, padded), lambda r: (0, 0, r, 0, 0))],
        out_specs=pl.BlockSpec((dests, 1, chunk, padded), lambda r: (0, r, 0, 0)),
        out_shape=jax.ShapeDtypeStruct((dests, req_local, chunk, padded), jnp.bfloat16),
    )(pair)


def gather_by_shifts(rows, axis_name, count):
    seat = lax.axis_index(axis_name)
    shifted = [rows]
    for distance in range(1, count):
        pairs = [(source, (source + distance) % count) for source in range(count)]
        shifted.append(lax.ppermute(rows, axis_name, pairs))
    stacked = jnp.stack(shifted)
    order = (seat - jnp.arange(count, dtype=jnp.int32)) % count
    return jnp.take(stacked, order, axis=0).reshape(count * rows.shape[0], rows.shape[1])


def body(hidden_in, norm_gain, w_query, w_key, w_value, cache_keys, cache_values, cache_lengths):
    core_count = lax.axis_size("core")
    seq_count = lax.axis_size("sq") * core_count
    seq_seat = lax.axis_index("sq") * core_count + lax.axis_index("core")
    req_local, slice_len, model_width = hidden_in.shape
    cache_len_dev = cache_keys.shape[1]
    span_len = slice_len * seq_count
    inputs = hidden_in.astype(jnp.float32)
    normed = (
        inputs * lax.rsqrt(jnp.mean(inputs * inputs, axis=-1, keepdims=True) + EPSILON) * norm_gain
    ).astype(jnp.bfloat16)
    flat_rows = normed.reshape(req_local * slice_len, model_width)
    req_count = lax.axis_size("req")
    row_local = w_query.shape[0]
    query_cols = w_query.shape[1]
    key_cols = w_key.shape[1]
    joined = jnp.concatenate([w_query, w_key, w_value], axis=1)
    joined = gather_by_shifts(joined, "req", req_count)
    joined = lax.all_gather(joined, SEQ, axis=0, tiled=True)
    permuted_rows = (
        flat_rows.reshape(-1, req_count, seq_count, row_local)
        .transpose(0, 2, 1, 3)
        .reshape(-1, model_width)
    )
    projected = jnp.dot(permuted_rows, joined, preferred_element_type=jnp.float32)
    query_raw = projected[:, :query_cols]
    key_raw = projected[:, query_cols : query_cols + key_cols]
    value_raw = projected[:, query_cols + key_cols :]
    local_index = jnp.arange(slice_len, dtype=jnp.int32)
    positions = cache_lengths[:, None] + seq_seat * slice_len + local_index[None, :]
    cosine, sine_part = tables(positions, HEAD)
    queries = (
        rotate(query_raw.reshape(req_local, slice_len, HEADS, HEAD), cosine, sine_part)
        .reshape(req_local, slice_len, HEADS * HEAD)
        .astype(jnp.bfloat16)
    )
    new_keys = (
        rotate(key_raw.reshape(req_local, slice_len, KV_HEADS, HEAD), cosine, sine_part)
        .reshape(req_local, slice_len, KV_HEADS * HEAD)
        .astype(jnp.bfloat16)
    )
    new_values = value_raw.reshape(req_local, slice_len, KV_HEADS * HEAD).astype(jnp.bfloat16)
    all_queries = lax.all_gather(queries, SEQ, axis=1, tiled=True)
    pad_rows = (-(cache_len_dev + slice_len)) % 128
    key_block = jnp.concatenate(
        [cache_keys, new_keys, jnp.zeros((req_local, pad_rows, KV_HEADS * HEAD), jnp.bfloat16)], axis=1
    )
    value_block = jnp.concatenate(
        [cache_values, new_values, jnp.zeros((req_local, pad_rows, KV_HEADS * HEAD), jnp.bfloat16)],
        axis=1,
    )
    scalars = jnp.concatenate([cache_lengths.astype(jnp.int32), seq_seat.astype(jnp.int32)[None]])
    out_all = block_attention(
        all_queries, key_block, value_block, scalars, cache_len_dev, slice_len, seq_count
    )
    pair = out_all.reshape((seq_count // core_count, core_count) + out_all.shape[1:])
    pair = lax.all_to_all(pair, "core", split_axis=1, concat_axis=1, tiled=True)
    merged = merge_pairs(pair)
    got_out = lax.all_to_all(merged, "sq", split_axis=0, concat_axis=0, tiled=True)
    attended = combine(got_out)
    return (attended, new_keys, new_values)


def solution(mesh):
    core_count = 2
    req_count, seq_count = mesh.devices.shape
    split_mesh = Mesh(
        mesh.devices.reshape(req_count, seq_count // core_count, core_count), ("req", "sq", "core")
    )
    in_specs = (
        P("req", SEQ, None),
        P(),
        P(("req",) + SEQ, None),
        P(("req",) + SEQ, None),
        P(("req",) + SEQ, None),
        P("req", SEQ, None),
        P("req", SEQ, None),
        P("req"),
    )
    out_specs = (P("req", SEQ, None), P("req", SEQ, None), P("req", SEQ, None))
    return jax.shard_map(body, mesh=split_mesh, in_specs=in_specs, out_specs=out_specs, check_vma=False)
```

```python
import functools

import jax
import jax.numpy as jnp
from jax import lax
from jax.experimental import pallas as pl
from jax.experimental.pallas import tpu as pltpu
from jax.sharding import Mesh
from jax.sharding import PartitionSpec as P

HEADS = 4
KV_HEADS = 2
HEAD = 256


EPSILON = 1e-06
THETA = 1000042.0
MASKED = -1e30
SEQ = ("sq", "core")


def tables(positions, head_size):
    half_size = head_size // 2
    frequency = THETA ** (-(jnp.arange(half_size, dtype=jnp.float32) * 2.0 / head_size))
    angles = positions.astype(jnp.float32)[..., None] * frequency
    return (jnp.cos(angles)[..., None, :], jnp.sin(angles)[..., None, :])


def rotate(values, cosine, sine_part):
    half_size = values.shape[-1] // 2
    first_half = values[..., :half_size]
    second_half = values[..., half_size:]
    return jnp.concatenate(
        [
            first_half * cosine - second_half * sine_part,
            second_half * cosine + first_half * sine_part,
        ],
        axis=-1,
    )


def pack_stats(stats, lane):
    width = 2 * HEADS
    first = stats.astype(jnp.bfloat16).astype(jnp.float32)
    rest = stats - first
    second = rest.astype(jnp.bfloat16).astype(jnp.float32)
    third = (rest - second).astype(jnp.bfloat16).astype(jnp.float32)
    return jnp.where(
        lane < width,
        first,
        jnp.where(
            lane < 2 * width,
            pltpu.roll(second, width, 1),
            jnp.where(lane < 3 * width, pltpu.roll(third, 2 * width, 1), 0.0),
        ),
    )


def unpack_stats(packed):
    width = 2 * HEADS
    return (packed + pltpu.roll(packed, 128 - width, 1)) + pltpu.roll(packed, 128 - 2 * width, 1)


def attention_kernel(scalar_ref, query_ref, key_ref, value_ref, out_ref, *, cache_len_dev, slice_len):
    request = pl.program_id(0)
    length = scalar_ref[request]
    seat = scalar_ref[scalar_ref.shape[0] - 1]
    span_len = query_ref.shape[1]
    key_rows = key_ref.shape[1]
    cores = out_ref.shape[0]
    blocks = cores * out_ref.shape[1]
    key_index = lax.broadcasted_iota(jnp.int32, (span_len, key_rows), 1)
    query_index = lax.broadcasted_iota(jnp.int32, (span_len, key_rows), 0)
    cache_live = seat * cache_len_dev + key_index < length
    new_live = seat * slice_len + (key_index - cache_len_dev) <= query_index
    in_cache = key_index < cache_len_dev
    in_new = jnp.logical_not(in_cache) & (key_index < cache_len_dev + slice_len)
    live = (in_cache & cache_live) | (in_new & new_live)
    lane = lax.broadcasted_iota(jnp.int32, (span_len, 128), 1)
    stats = jnp.zeros((span_len, 128), jnp.float32)
    group_size = HEADS // KV_HEADS
    for head in range(HEADS):
        group = head // group_size
        query_rows = query_ref[0, :, head * HEAD : (head + 1) * HEAD]
        key_rows_h = key_ref[0, :, group * HEAD : (group + 1) * HEAD]
        value_rows_h = value_ref[0, :, group * HEAD : (group + 1) * HEAD]
        scores = lax.dot_general(
            query_rows, key_rows_h, (((1,), (1,)), ((), ())), preferred_element_type=jnp.float32
        ) * HEAD ** (-0.5)
        scores = jnp.where(live, scores, MASKED)
        block_max = jnp.max(scores, axis=1, keepdims=True)
        weights = jnp.where(live, jnp.exp(scores - block_max), 0.0)
        block_sum = jnp.sum(weights, axis=1, keepdims=True)
        block_out = jnp.dot(
            weights.astype(jnp.bfloat16), value_rows_h, preferred_element_type=jnp.float32
        )
        by_dest = block_out.astype(jnp.bfloat16).reshape(blocks // cores, cores, span_len // blocks, HEAD)
        for core in range(cores):
            out_ref[core, :, 0, :, head * HEAD : (head + 1) * HEAD] = by_dest[:, core]
        stats = jnp.where(lane == head, block_max, stats)
        stats = jnp.where(lane == HEADS + head, block_sum, stats)
    packed = pack_stats(stats, lane)
    by_dest = packed.astype(jnp.bfloat16).reshape(blocks // cores, cores, span_len // blocks, 128)
    for core in range(cores):
        out_ref[core, :, 0, :, HEADS * HEAD :] = by_dest[:, core]


def block_attention(all_queries, key_block, value_block, scalars, cache_len_dev, slice_len, blocks, cores):
    req_local, span_len, query_width = all_queries.shape
    key_rows = key_block.shape[1]
    kv_width = key_block.shape[2]
    chunk = span_len // blocks
    grid_spec = pltpu.PrefetchScalarGridSpec(
        num_scalar_prefetch=1,
        grid=(req_local,),
        in_specs=[
            pl.BlockSpec((1, span_len, query_width), lambda r, s: (r, 0, 0)),
            pl.BlockSpec((1, key_rows, kv_width), lambda r, s: (r, 0, 0)),
            pl.BlockSpec((1, key_rows, kv_width), lambda r, s: (r, 0, 0)),
        ],
        out_specs=pl.BlockSpec(
            (cores, blocks // cores, 1, chunk, query_width + 128), lambda r, s: (0, 0, r, 0, 0)
        ),
    )
    return pl.pallas_call(
        functools.partial(attention_kernel, cache_len_dev=cache_len_dev, slice_len=slice_len),
        grid_spec=grid_spec,
        out_shape=jax.ShapeDtypeStruct(
            (cores, blocks // cores, req_local, chunk, query_width + 128), jnp.bfloat16
        ),
    )(scalars, all_queries, key_block, value_block)


def combine_kernel(out_ref, result_ref):
    blocks, _, chunk, padded = out_ref.shape
    width = HEADS * HEAD
    stat_width = 2 * HEADS
    lane = lax.broadcasted_iota(jnp.int32, (chunk, 128), 1)

    def block_stats(block):
        return unpack_stats(out_ref[block, 0, :, width:].astype(jnp.float32))

    top = block_stats(0)
    for block in range(1, blocks):
        top = jnp.maximum(top, block_stats(block))
    top = jnp.where(lane < HEADS, top, 0.0)

    def step(block, carry):
        summed, total = carry
        row_stats = block_stats(block)
        factor = jnp.exp(jnp.where(lane < HEADS, row_stats, 0.0) - top)
        pieces = []
        new_total = []
        total = total + factor * pltpu.roll(row_stats, 128 - HEADS, 1)
        for head in range(HEADS):
            head_factor = jnp.broadcast_to(factor[:, head : head + 1], (chunk, HEAD))
            rows = out_ref[block, 0, :, head * HEAD : (head + 1) * HEAD].astype(jnp.float32)
            pieces.append(summed[head] + rows * head_factor)
        return (tuple(pieces), total)

    start = (
        tuple(jnp.zeros((chunk, HEAD), jnp.float32) for _ in range(HEADS)),
        jnp.zeros((chunk, 128), jnp.float32),
    )
    summed, total = lax.fori_loop(0, blocks, step, start, unroll=4)
    for head in range(HEADS):
        head_total = jnp.broadcast_to(total[:, head : head + 1], (chunk, HEAD))
        result_ref[0, :, head * HEAD : (head + 1) * HEAD] = (summed[head] / head_total).astype(
            result_ref.dtype
        )


def combine(got_out):
    blocks, req_local, chunk, padded = got_out.shape
    width = HEADS * HEAD
    return pl.pallas_call(
        combine_kernel,
        grid=(req_local,),
        in_specs=[pl.BlockSpec((blocks, 1, chunk, padded), lambda r: (0, r, 0, 0))],
        out_specs=pl.BlockSpec((1, chunk, width), lambda r: (r, 0, 0)),
        out_shape=jax.ShapeDtypeStruct((req_local, chunk, width), jnp.bfloat16),
    )(got_out)


def merge_kernel(pair_ref, merged_ref):
    _, dests, _, chunk, padded = pair_ref.shape
    width = HEADS * HEAD
    lane = lax.broadcasted_iota(jnp.int32, (chunk, 128), 1)

    def step(dest, carry):
        first = unpack_stats(pair_ref[0, dest, 0, :, width:].astype(jnp.float32))
        second = unpack_stats(pair_ref[1, dest, 0, :, width:].astype(jnp.float32))
        first_max = jnp.where(lane < HEADS, first, 0.0)
        second_max = jnp.where(lane < HEADS, second, 0.0)
        best = jnp.maximum(first_max, second_max)
        first_factor = jnp.exp(first_max - best)
        second_factor = jnp.exp(second_max - best)
        first_sums = pltpu.roll(first, 128 - HEADS, 1)
        second_sums = pltpu.roll(second, 128 - HEADS, 1)
        sums = first_factor * first_sums + second_factor * second_sums
        stats = jnp.where(lane < HEADS, best, jnp.where(lane < 2 * HEADS, pltpu.roll(sums, HEADS, 1), 0.0))
        for head in range(HEADS):
            columns = slice(head * HEAD, (head + 1) * HEAD)
            first_head = jnp.broadcast_to(first_factor[:, head : head + 1], (chunk, HEAD))
            second_head = jnp.broadcast_to(second_factor[:, head : head + 1], (chunk, HEAD))
            partial = (
                pair_ref[0, dest, 0, :, columns].astype(jnp.float32) * first_head
                + pair_ref[1, dest, 0, :, columns].astype(jnp.float32) * second_head
            )
            merged_ref[dest, 0, :, columns] = partial.astype(merged_ref.dtype)
        merged_ref[dest, 0, :, width:] = pack_stats(stats, lane).astype(merged_ref.dtype)
        return carry

    lax.fori_loop(0, dests, step, 0, unroll=4)


def merge_pairs(pair):
    sources, dests, req_local, chunk, padded = pair.shape
    return pl.pallas_call(
        merge_kernel,
        grid=(req_local,),
        in_specs=[pl.BlockSpec((sources, dests, 1, chunk, padded), lambda r: (0, 0, r, 0, 0))],
        out_specs=pl.BlockSpec((dests, 1, chunk, padded), lambda r: (0, r, 0, 0)),
        out_shape=jax.ShapeDtypeStruct((dests, req_local, chunk, padded), jnp.bfloat16),
    )(pair)


def gather_by_shifts(rows, axis_name, count):
    seat = lax.axis_index(axis_name)
    shifted = [rows]
    for distance in range(1, count):
        pairs = [(source, (source + distance) % count) for source in range(count)]
        shifted.append(lax.ppermute(rows, axis_name, pairs))
    stacked = jnp.stack(shifted)
    order = (seat - jnp.arange(count, dtype=jnp.int32)) % count
    return jnp.take(stacked, order, axis=0).reshape(count * rows.shape[0], rows.shape[1])


def body(hidden_in, norm_gain, w_query, w_key, w_value, cache_keys, cache_values, cache_lengths):
    core_count = lax.axis_size("core")
    seq_count = lax.axis_size("sq") * core_count
    seq_seat = lax.axis_index("sq") * core_count + lax.axis_index("core")
    req_local, slice_len, model_width = hidden_in.shape
    cache_len_dev = cache_keys.shape[1]
    span_len = slice_len * seq_count
    inputs = hidden_in.astype(jnp.float32)
    normed = (
        inputs * lax.rsqrt(jnp.mean(inputs * inputs, axis=-1, keepdims=True) + EPSILON) * norm_gain
    ).astype(jnp.bfloat16)
    flat_rows = normed.reshape(req_local * slice_len, model_width)
    req_count = lax.axis_size("req")
    row_local = w_query.shape[0]
    query_cols = w_query.shape[1]
    key_cols = w_key.shape[1]
    joined = jnp.concatenate([w_query, w_key, w_value], axis=1)
    joined = gather_by_shifts(joined, "req", req_count)
    joined = lax.all_gather(joined, SEQ, axis=0, tiled=True)
    permuted_rows = (
        flat_rows.reshape(-1, req_count, seq_count, row_local)
        .transpose(0, 2, 1, 3)
        .reshape(-1, model_width)
    )
    projected = jnp.dot(permuted_rows, joined, preferred_element_type=jnp.float32)
    query_raw = projected[:, :query_cols]
    key_raw = projected[:, query_cols : query_cols + key_cols]
    value_raw = projected[:, query_cols + key_cols :]
    local_index = jnp.arange(slice_len, dtype=jnp.int32)
    positions = cache_lengths[:, None] + seq_seat * slice_len + local_index[None, :]
    cosine, sine_part = tables(positions, HEAD)
    queries = (
        rotate(query_raw.reshape(req_local, slice_len, HEADS, HEAD), cosine, sine_part)
        .reshape(req_local, slice_len, HEADS * HEAD)
        .astype(jnp.bfloat16)
    )
    new_keys = (
        rotate(key_raw.reshape(req_local, slice_len, KV_HEADS, HEAD), cosine, sine_part)
        .reshape(req_local, slice_len, KV_HEADS * HEAD)
        .astype(jnp.bfloat16)
    )
    new_values = value_raw.reshape(req_local, slice_len, KV_HEADS * HEAD).astype(jnp.bfloat16)
    all_queries = lax.all_gather(queries, SEQ, axis=1, tiled=True)
    pad_rows = (-(cache_len_dev + slice_len)) % 128
    key_block = jnp.concatenate(
        [cache_keys, new_keys, jnp.zeros((req_local, pad_rows, KV_HEADS * HEAD), jnp.bfloat16)], axis=1
    )
    value_block = jnp.concatenate(
        [cache_values, new_values, jnp.zeros((req_local, pad_rows, KV_HEADS * HEAD), jnp.bfloat16)],
        axis=1,
    )
    scalars = jnp.concatenate([cache_lengths.astype(jnp.int32), seq_seat.astype(jnp.int32)[None]])
    out_all = block_attention(
        all_queries, key_block, value_block, scalars, cache_len_dev, slice_len, seq_count, core_count
    )
    pair = lax.all_to_all(out_all, "core", split_axis=0, concat_axis=0, tiled=True)
    merged = merge_pairs(pair)
    got_out = lax.all_to_all(merged, "sq", split_axis=0, concat_axis=0, tiled=True)
    attended = combine(got_out)
    return (attended, new_keys, new_values)


def solution(mesh):
    core_count = 2
    req_count, seq_count = mesh.devices.shape
    split_mesh = Mesh(
        mesh.devices.reshape(req_count, seq_count // core_count, core_count), ("req", "sq", "core")
    )
    in_specs = (
        P("req", SEQ, None),
        P(),
        P(("req",) + SEQ, None),
        P(("req",) + SEQ, None),
        P(("req",) + SEQ, None),
        P("req", SEQ, None),
        P("req", SEQ, None),
        P("req"),
    )
    out_specs = (P("req", SEQ, None), P("req", SEQ, None), P("req", SEQ, None))
    return jax.shard_map(body, mesh=split_mesh, in_specs=in_specs, out_specs=out_specs, check_vma=False)
```

```python
import functools

import jax
import jax.numpy as jnp
from jax import lax
from jax.experimental import pallas as pl
from jax.experimental.pallas import tpu as pltpu
from jax.sharding import Mesh
from jax.sharding import PartitionSpec as P

HEADS = 4
KV_HEADS = 2
HEAD = 256


EPSILON = 1e-06
THETA = 1000042.0
MASKED = -1e30
SEQ = ("sq", "core")


def tables(positions, head_size):
    half_size = head_size // 2
    frequency = THETA ** (-(jnp.arange(half_size, dtype=jnp.float32) * 2.0 / head_size))
    angles = positions.astype(jnp.float32)[..., None] * frequency
    return (jnp.cos(angles)[..., None, :], jnp.sin(angles)[..., None, :])


def rotate(values, cosine, sine_part):
    half_size = values.shape[-1] // 2
    first_half = values[..., :half_size]
    second_half = values[..., half_size:]
    return jnp.concatenate(
        [
            first_half * cosine - second_half * sine_part,
            second_half * cosine + first_half * sine_part,
        ],
        axis=-1,
    )


def pack_stats(stats, lane):
    width = 2 * HEADS
    first = stats.astype(jnp.bfloat16).astype(jnp.float32)
    rest = stats - first
    second = rest.astype(jnp.bfloat16).astype(jnp.float32)
    third = (rest - second).astype(jnp.bfloat16).astype(jnp.float32)
    return jnp.where(
        lane < width,
        first,
        jnp.where(
            lane < 2 * width,
            pltpu.roll(second, width, 1),
            jnp.where(lane < 3 * width, pltpu.roll(third, 2 * width, 1), 0.0),
        ),
    )


def unpack_stats(packed):
    width = 2 * HEADS
    return (packed + pltpu.roll(packed, 128 - width, 1)) + pltpu.roll(packed, 128 - 2 * width, 1)


def attention_kernel(scalar_ref, query_ref, key_ref, value_ref, out_ref, *, cache_len_dev, slice_len):
    request = pl.program_id(0)
    length = scalar_ref[request]
    seat = scalar_ref[scalar_ref.shape[0] - 1]
    span_len = query_ref.shape[0]
    key_rows = key_ref.shape[1]
    cores = out_ref.shape[0]
    blocks = cores * out_ref.shape[1]
    key_index = lax.broadcasted_iota(jnp.int32, (span_len, key_rows), 1)
    query_index = lax.broadcasted_iota(jnp.int32, (span_len, key_rows), 0)
    cache_live = seat * cache_len_dev + key_index < length
    new_live = seat * slice_len + (key_index - cache_len_dev) <= query_index
    in_cache = key_index < cache_len_dev
    in_new = jnp.logical_not(in_cache) & (key_index < cache_len_dev + slice_len)
    live = (in_cache & cache_live) | (in_new & new_live)
    lane = lax.broadcasted_iota(jnp.int32, (span_len, 128), 1)
    stats = jnp.zeros((span_len, 128), jnp.float32)
    group_size = HEADS // KV_HEADS
    for head in range(HEADS):
        group = head // group_size
        query_rows = query_ref[:, head * HEAD : (head + 1) * HEAD]
        key_rows_h = key_ref[0, :, group * HEAD : (group + 1) * HEAD]
        value_rows_h = value_ref[0, :, group * HEAD : (group + 1) * HEAD]
        scores = lax.dot_general(
            query_rows, key_rows_h, (((1,), (1,)), ((), ())), preferred_element_type=jnp.float32
        ) * HEAD ** (-0.5)
        scores = jnp.where(live, scores, MASKED)
        block_max = jnp.max(scores, axis=1, keepdims=True)
        weights = jnp.where(live, jnp.exp(scores - block_max), 0.0)
        block_sum = jnp.sum(weights, axis=1, keepdims=True)
        block_out = jnp.dot(
            weights.astype(jnp.bfloat16), value_rows_h, preferred_element_type=jnp.float32
        )
        by_dest = block_out.astype(jnp.bfloat16).reshape(blocks // cores, cores, span_len // blocks, HEAD)
        for core in range(cores):
            out_ref[core, :, 0, :, head * HEAD : (head + 1) * HEAD] = by_dest[:, core]
        stats = jnp.where(lane == head, block_max, stats)
        stats = jnp.where(lane == HEADS + head, block_sum, stats)
    packed = pack_stats(stats, lane)
    by_dest = packed.astype(jnp.bfloat16).reshape(blocks // cores, cores, span_len // blocks, 128)
    for core in range(cores):
        out_ref[core, :, 0, :, HEADS * HEAD :] = by_dest[:, core]


def block_attention(all_queries, key_block, value_block, scalars, cache_len_dev, slice_len, blocks, cores):
    req_local = key_block.shape[0]
    span_len = all_queries.shape[0]
    query_width = all_queries.shape[1] // req_local
    key_rows = key_block.shape[1]
    kv_width = key_block.shape[2]
    chunk = span_len // blocks
    grid_spec = pltpu.PrefetchScalarGridSpec(
        num_scalar_prefetch=1,
        grid=(req_local,),
        in_specs=[
            pl.BlockSpec((span_len, query_width), lambda r, s: (0, r)),
            pl.BlockSpec((1, key_rows, kv_width), lambda r, s: (r, 0, 0)),
            pl.BlockSpec((1, key_rows, kv_width), lambda r, s: (r, 0, 0)),
        ],
        out_specs=pl.BlockSpec(
            (cores, blocks // cores, 1, chunk, query_width + 128), lambda r, s: (0, 0, r, 0, 0)
        ),
    )
    return pl.pallas_call(
        functools.partial(attention_kernel, cache_len_dev=cache_len_dev, slice_len=slice_len),
        grid_spec=grid_spec,
        out_shape=jax.ShapeDtypeStruct(
            (cores, blocks // cores, req_local, chunk, query_width + 128), jnp.bfloat16
        ),
    )(scalars, all_queries, key_block, value_block)


def combine_kernel(out_ref, result_ref):
    blocks, _, chunk, padded = out_ref.shape
    width = HEADS * HEAD
    stat_width = 2 * HEADS
    lane = lax.broadcasted_iota(jnp.int32, (chunk, 128), 1)

    def block_stats(block):
        return unpack_stats(out_ref[block, 0, :, width:].astype(jnp.float32))

    top = block_stats(0)
    for block in range(1, blocks):
        top = jnp.maximum(top, block_stats(block))
    top = jnp.where(lane < HEADS, top, 0.0)

    def step(block, carry):
        summed, total = carry
        row_stats = block_stats(block)
        factor = jnp.exp(jnp.where(lane < HEADS, row_stats, 0.0) - top)
        pieces = []
        new_total = []
        total = total + factor * pltpu.roll(row_stats, 128 - HEADS, 1)
        for head in range(HEADS):
            head_factor = jnp.broadcast_to(factor[:, head : head + 1], (chunk, HEAD))
            rows = out_ref[block, 0, :, head * HEAD : (head + 1) * HEAD].astype(jnp.float32)
            pieces.append(summed[head] + rows * head_factor)
        return (tuple(pieces), total)

    start = (
        tuple(jnp.zeros((chunk, HEAD), jnp.float32) for _ in range(HEADS)),
        jnp.zeros((chunk, 128), jnp.float32),
    )
    summed, total = lax.fori_loop(0, blocks, step, start, unroll=4)
    for head in range(HEADS):
        head_total = jnp.broadcast_to(total[:, head : head + 1], (chunk, HEAD))
        result_ref[0, :, head * HEAD : (head + 1) * HEAD] = (summed[head] / head_total).astype(
            result_ref.dtype
        )


def combine(got_out):
    blocks, req_local, chunk, padded = got_out.shape
    width = HEADS * HEAD
    return pl.pallas_call(
        combine_kernel,
        grid=(req_local,),
        in_specs=[pl.BlockSpec((blocks, 1, chunk, padded), lambda r: (0, r, 0, 0))],
        out_specs=pl.BlockSpec((1, chunk, width), lambda r: (r, 0, 0)),
        out_shape=jax.ShapeDtypeStruct((req_local, chunk, width), jnp.bfloat16),
    )(got_out)


def merge_kernel(pair_ref, merged_ref):
    _, dests, _, chunk, padded = pair_ref.shape
    width = HEADS * HEAD
    lane = lax.broadcasted_iota(jnp.int32, (chunk, 128), 1)

    def step(dest, carry):
        first = unpack_stats(pair_ref[0, dest, 0, :, width:].astype(jnp.float32))
        second = unpack_stats(pair_ref[1, dest, 0, :, width:].astype(jnp.float32))
        first_max = jnp.where(lane < HEADS, first, 0.0)
        second_max = jnp.where(lane < HEADS, second, 0.0)
        best = jnp.maximum(first_max, second_max)
        first_factor = jnp.exp(first_max - best)
        second_factor = jnp.exp(second_max - best)
        first_sums = pltpu.roll(first, 128 - HEADS, 1)
        second_sums = pltpu.roll(second, 128 - HEADS, 1)
        sums = first_factor * first_sums + second_factor * second_sums
        stats = jnp.where(lane < HEADS, best, jnp.where(lane < 2 * HEADS, pltpu.roll(sums, HEADS, 1), 0.0))
        for head in range(HEADS):
            columns = slice(head * HEAD, (head + 1) * HEAD)
            first_head = jnp.broadcast_to(first_factor[:, head : head + 1], (chunk, HEAD))
            second_head = jnp.broadcast_to(second_factor[:, head : head + 1], (chunk, HEAD))
            partial = (
                pair_ref[0, dest, 0, :, columns].astype(jnp.float32) * first_head
                + pair_ref[1, dest, 0, :, columns].astype(jnp.float32) * second_head
            )
            merged_ref[dest, 0, :, columns] = partial.astype(merged_ref.dtype)
        merged_ref[dest, 0, :, width:] = pack_stats(stats, lane).astype(merged_ref.dtype)
        return carry

    lax.fori_loop(0, dests, step, 0, unroll=4)


def merge_pairs(pair):
    sources, dests, req_local, chunk, padded = pair.shape
    return pl.pallas_call(
        merge_kernel,
        grid=(req_local,),
        in_specs=[pl.BlockSpec((sources, dests, 1, chunk, padded), lambda r: (0, 0, r, 0, 0))],
        out_specs=pl.BlockSpec((dests, 1, chunk, padded), lambda r: (0, r, 0, 0)),
        out_shape=jax.ShapeDtypeStruct((dests, req_local, chunk, padded), jnp.bfloat16),
    )(pair)


def gather_by_shifts(rows, axis_name, count):
    seat = lax.axis_index(axis_name)
    shifted = [rows]
    for distance in range(1, count):
        pairs = [(source, (source + distance) % count) for source in range(count)]
        shifted.append(lax.ppermute(rows, axis_name, pairs))
    stacked = jnp.stack(shifted)
    order = (seat - jnp.arange(count, dtype=jnp.int32)) % count
    return jnp.take(stacked, order, axis=0).reshape(count * rows.shape[0], rows.shape[1])


def body(hidden_in, norm_gain, w_query, w_key, w_value, cache_keys, cache_values, cache_lengths):
    core_count = lax.axis_size("core")
    seq_count = lax.axis_size("sq") * core_count
    seq_seat = lax.axis_index("sq") * core_count + lax.axis_index("core")
    req_local, slice_len, model_width = hidden_in.shape
    cache_len_dev = cache_keys.shape[1]
    span_len = slice_len * seq_count
    inputs = hidden_in.astype(jnp.float32)
    normed = (
        inputs * lax.rsqrt(jnp.mean(inputs * inputs, axis=-1, keepdims=True) + EPSILON) * norm_gain
    ).astype(jnp.bfloat16)
    flat_rows = normed.reshape(req_local * slice_len, model_width)
    req_count = lax.axis_size("req")
    row_local = w_query.shape[0]
    query_cols = w_query.shape[1]
    key_cols = w_key.shape[1]
    joined = jnp.concatenate([w_query, w_key, w_value], axis=1)
    joined = gather_by_shifts(joined, "req", req_count)
    joined = lax.all_gather(joined, SEQ, axis=0, tiled=True)
    permuted_rows = (
        flat_rows.reshape(-1, req_count, seq_count, row_local)
        .transpose(0, 2, 1, 3)
        .reshape(-1, model_width)
    )
    projected = jnp.dot(permuted_rows, joined, preferred_element_type=jnp.float32)
    query_raw = projected[:, :query_cols]
    key_raw = projected[:, query_cols : query_cols + key_cols]
    value_raw = projected[:, query_cols + key_cols :]
    local_index = jnp.arange(slice_len, dtype=jnp.int32)
    positions = cache_lengths[:, None] + seq_seat * slice_len + local_index[None, :]
    cosine, sine_part = tables(positions, HEAD)
    queries = (
        rotate(query_raw.reshape(req_local, slice_len, HEADS, HEAD), cosine, sine_part)
        .reshape(req_local, slice_len, HEADS * HEAD)
        .astype(jnp.bfloat16)
    )
    new_keys = (
        rotate(key_raw.reshape(req_local, slice_len, KV_HEADS, HEAD), cosine, sine_part)
        .reshape(req_local, slice_len, KV_HEADS * HEAD)
        .astype(jnp.bfloat16)
    )
    new_values = value_raw.reshape(req_local, slice_len, KV_HEADS * HEAD).astype(jnp.bfloat16)
    token_major = queries.transpose(1, 0, 2).reshape(slice_len, req_local * HEADS * HEAD)
    all_queries = lax.all_gather(token_major, SEQ, axis=0, tiled=True)
    pad_rows = (-(cache_len_dev + slice_len)) % 128
    key_block = jnp.concatenate(
        [cache_keys, new_keys, jnp.zeros((req_local, pad_rows, KV_HEADS * HEAD), jnp.bfloat16)], axis=1
    )
    value_block = jnp.concatenate(
        [cache_values, new_values, jnp.zeros((req_local, pad_rows, KV_HEADS * HEAD), jnp.bfloat16)],
        axis=1,
    )
    scalars = jnp.concatenate([cache_lengths.astype(jnp.int32), seq_seat.astype(jnp.int32)[None]])
    out_all = block_attention(
        all_queries, key_block, value_block, scalars, cache_len_dev, slice_len, seq_count, core_count
    )
    pair = lax.all_to_all(out_all, "core", split_axis=0, concat_axis=0, tiled=True)
    merged = merge_pairs(pair)
    got_out = lax.all_to_all(merged, "sq", split_axis=0, concat_axis=0, tiled=True)
    attended = combine(got_out)
    return (attended, new_keys, new_values)


def solution(mesh):
    core_count = 2
    req_count, seq_count = mesh.devices.shape
    split_mesh = Mesh(
        mesh.devices.reshape(req_count, seq_count // core_count, core_count), ("req", "sq", "core")
    )
    in_specs = (
        P("req", SEQ, None),
        P(),
        P(("req",) + SEQ, None),
        P(("req",) + SEQ, None),
        P(("req",) + SEQ, None),
        P("req", SEQ, None),
        P("req", SEQ, None),
        P("req"),
    )
    out_specs = (P("req", SEQ, None), P("req", SEQ, None), P("req", SEQ, None))
    return jax.shard_map(body, mesh=split_mesh, in_specs=in_specs, out_specs=out_specs, check_vma=False)
```

```python
import functools

import jax
import jax.numpy as jnp
from jax import lax
from jax.experimental import pallas as pl
from jax.experimental.pallas import tpu as pltpu
from jax.sharding import Mesh
from jax.sharding import PartitionSpec as P

HEADS = 4
KV_HEADS = 2
HEAD = 256


EPSILON = 1e-06
THETA = 1000042.0
MASKED = -1e30
SEQ = ("sq", "core")


def tables(positions, head_size):
    half_size = head_size // 2
    frequency = THETA ** (-(jnp.arange(half_size, dtype=jnp.float32) * 2.0 / head_size))
    angles = positions.astype(jnp.float32)[..., None] * frequency
    return (jnp.cos(angles)[..., None, :], jnp.sin(angles)[..., None, :])


def rotate(values, cosine, sine_part):
    half_size = values.shape[-1] // 2
    first_half = values[..., :half_size]
    second_half = values[..., half_size:]
    return jnp.concatenate(
        [
            first_half * cosine - second_half * sine_part,
            second_half * cosine + first_half * sine_part,
        ],
        axis=-1,
    )


def pack_stats(stats, lane):
    width = 2 * HEADS
    first = stats.astype(jnp.bfloat16).astype(jnp.float32)
    rest = stats - first
    second = rest.astype(jnp.bfloat16).astype(jnp.float32)
    third = (rest - second).astype(jnp.bfloat16).astype(jnp.float32)
    return jnp.where(
        lane < width,
        first,
        jnp.where(
            lane < 2 * width,
            pltpu.roll(second, width, 1),
            jnp.where(lane < 3 * width, pltpu.roll(third, 2 * width, 1), 0.0),
        ),
    )


def unpack_stats(packed):
    width = 2 * HEADS
    return (packed + pltpu.roll(packed, 128 - width, 1)) + pltpu.roll(packed, 128 - 2 * width, 1)


def attention_kernel(scalar_ref, query_ref, key_ref, value_ref, out_ref, *, cache_len_dev, slice_len):
    request = pl.program_id(0)
    length = scalar_ref[request]
    seat = scalar_ref[scalar_ref.shape[0] - 1]
    span_len = query_ref.shape[0]
    key_rows = key_ref.shape[1]
    cores = out_ref.shape[0]
    blocks = cores * out_ref.shape[1]
    own_core = seat % cores
    key_index = lax.broadcasted_iota(jnp.int32, (span_len, key_rows), 1)
    query_index = lax.broadcasted_iota(jnp.int32, (span_len, key_rows), 0)
    cache_live = seat * cache_len_dev + key_index < length
    new_live = seat * slice_len + (key_index - cache_len_dev) <= query_index
    in_cache = key_index < cache_len_dev
    in_new = jnp.logical_not(in_cache) & (key_index < cache_len_dev + slice_len)
    live = (in_cache & cache_live) | (in_new & new_live)
    lane = lax.broadcasted_iota(jnp.int32, (span_len, 128), 1)
    stats = jnp.zeros((span_len, 128), jnp.float32)
    group_size = HEADS // KV_HEADS
    for head in range(HEADS):
        group = head // group_size
        query_rows = query_ref[:, head * HEAD : (head + 1) * HEAD]
        key_rows_h = key_ref[0, :, group * HEAD : (group + 1) * HEAD]
        value_rows_h = value_ref[0, :, group * HEAD : (group + 1) * HEAD]
        scores = lax.dot_general(
            query_rows, key_rows_h, (((1,), (1,)), ((), ())), preferred_element_type=jnp.float32
        ) * HEAD ** (-0.5)
        scores = jnp.where(live, scores, MASKED)
        block_max = jnp.max(scores, axis=1, keepdims=True)
        weights = jnp.where(live, jnp.exp(scores - block_max), 0.0)
        block_sum = jnp.sum(weights, axis=1, keepdims=True)
        block_out = jnp.dot(
            weights.astype(jnp.bfloat16), value_rows_h, preferred_element_type=jnp.float32
        )
        by_dest = block_out.astype(jnp.bfloat16).reshape(blocks // cores, cores, span_len // blocks, HEAD)
        for core in range(cores):
            out_ref[(core + own_core) % cores, :, 0, :, head * HEAD : (head + 1) * HEAD] = by_dest[:, core]
        stats = jnp.where(lane == head, block_max, stats)
        stats = jnp.where(lane == HEADS + head, block_sum, stats)
    packed = pack_stats(stats, lane)
    by_dest = packed.astype(jnp.bfloat16).reshape(blocks // cores, cores, span_len // blocks, 128)
    for core in range(cores):
        out_ref[(core + own_core) % cores, :, 0, :, HEADS * HEAD :] = by_dest[:, core]


def block_attention(all_queries, key_block, value_block, scalars, cache_len_dev, slice_len, blocks, cores):
    req_local = key_block.shape[0]
    span_len = all_queries.shape[0]
    query_width = all_queries.shape[1] // req_local
    key_rows = key_block.shape[1]
    kv_width = key_block.shape[2]
    chunk = span_len // blocks
    grid_spec = pltpu.PrefetchScalarGridSpec(
        num_scalar_prefetch=1,
        grid=(req_local,),
        in_specs=[
            pl.BlockSpec((span_len, query_width), lambda r, s: (0, r)),
            pl.BlockSpec((1, key_rows, kv_width), lambda r, s: (r, 0, 0)),
            pl.BlockSpec((1, key_rows, kv_width), lambda r, s: (r, 0, 0)),
        ],
        out_specs=pl.BlockSpec(
            (cores, blocks // cores, 1, chunk, query_width + 128), lambda r, s: (0, 0, r, 0, 0)
        ),
    )
    return pl.pallas_call(
        functools.partial(attention_kernel, cache_len_dev=cache_len_dev, slice_len=slice_len),
        grid_spec=grid_spec,
        out_shape=jax.ShapeDtypeStruct(
            (cores, blocks // cores, req_local, chunk, query_width + 128), jnp.bfloat16
        ),
    )(scalars, all_queries, key_block, value_block)


def combine_kernel(out_ref, result_ref):
    blocks, _, chunk, padded = out_ref.shape
    width = HEADS * HEAD
    stat_width = 2 * HEADS
    lane = lax.broadcasted_iota(jnp.int32, (chunk, 128), 1)

    def block_stats(block):
        return unpack_stats(out_ref[block, 0, :, width:].astype(jnp.float32))

    top = block_stats(0)
    for block in range(1, blocks):
        top = jnp.maximum(top, block_stats(block))
    top = jnp.where(lane < HEADS, top, 0.0)

    def step(block, carry):
        summed, total = carry
        row_stats = block_stats(block)
        factor = jnp.exp(jnp.where(lane < HEADS, row_stats, 0.0) - top)
        pieces = []
        new_total = []
        total = total + factor * pltpu.roll(row_stats, 128 - HEADS, 1)
        for head in range(HEADS):
            head_factor = jnp.broadcast_to(factor[:, head : head + 1], (chunk, HEAD))
            rows = out_ref[block, 0, :, head * HEAD : (head + 1) * HEAD].astype(jnp.float32)
            pieces.append(summed[head] + rows * head_factor)
        return (tuple(pieces), total)

    start = (
        tuple(jnp.zeros((chunk, HEAD), jnp.float32) for _ in range(HEADS)),
        jnp.zeros((chunk, 128), jnp.float32),
    )
    summed, total = lax.fori_loop(0, blocks, step, start, unroll=4)
    for head in range(HEADS):
        head_total = jnp.broadcast_to(total[:, head : head + 1], (chunk, HEAD))
        result_ref[0, :, head * HEAD : (head + 1) * HEAD] = (summed[head] / head_total).astype(
            result_ref.dtype
        )


def combine(got_out):
    blocks, req_local, chunk, padded = got_out.shape
    width = HEADS * HEAD
    return pl.pallas_call(
        combine_kernel,
        grid=(req_local,),
        in_specs=[pl.BlockSpec((blocks, 1, chunk, padded), lambda r: (0, r, 0, 0))],
        out_specs=pl.BlockSpec((1, chunk, width), lambda r: (r, 0, 0)),
        out_shape=jax.ShapeDtypeStruct((req_local, chunk, width), jnp.bfloat16),
    )(got_out)


def merge_kernel(keep_ref, received_ref, merged_ref):
    _, dests, _, chunk, padded = keep_ref.shape
    width = HEADS * HEAD
    lane = lax.broadcasted_iota(jnp.int32, (chunk, 128), 1)

    def step(dest, carry):
        first = unpack_stats(keep_ref[0, dest, 0, :, width:].astype(jnp.float32))
        second = unpack_stats(received_ref[dest, 0, :, width:].astype(jnp.float32))
        first_max = jnp.where(lane < HEADS, first, 0.0)
        second_max = jnp.where(lane < HEADS, second, 0.0)
        best = jnp.maximum(first_max, second_max)
        first_factor = jnp.exp(first_max - best)
        second_factor = jnp.exp(second_max - best)
        first_sums = pltpu.roll(first, 128 - HEADS, 1)
        second_sums = pltpu.roll(second, 128 - HEADS, 1)
        sums = first_factor * first_sums + second_factor * second_sums
        stats = jnp.where(lane < HEADS, best, jnp.where(lane < 2 * HEADS, pltpu.roll(sums, HEADS, 1), 0.0))
        for head in range(HEADS):
            columns = slice(head * HEAD, (head + 1) * HEAD)
            first_head = jnp.broadcast_to(first_factor[:, head : head + 1], (chunk, HEAD))
            second_head = jnp.broadcast_to(second_factor[:, head : head + 1], (chunk, HEAD))
            partial = (
                keep_ref[0, dest, 0, :, columns].astype(jnp.float32) * first_head
                + received_ref[dest, 0, :, columns].astype(jnp.float32) * second_head
            )
            merged_ref[dest, 0, :, columns] = partial.astype(merged_ref.dtype)
        merged_ref[dest, 0, :, width:] = pack_stats(stats, lane).astype(merged_ref.dtype)
        return carry

    lax.fori_loop(0, dests, step, 0, unroll=4)


def merge_pairs(out_all, received):
    sources, dests, req_local, chunk, padded = out_all.shape
    return pl.pallas_call(
        merge_kernel,
        grid=(req_local,),
        in_specs=[
            pl.BlockSpec((1, dests, 1, chunk, padded), lambda r: (0, 0, r, 0, 0)),
            pl.BlockSpec((dests, 1, chunk, padded), lambda r: (0, r, 0, 0)),
        ],
        out_specs=pl.BlockSpec((dests, 1, chunk, padded), lambda r: (0, r, 0, 0)),
        out_shape=jax.ShapeDtypeStruct((dests, req_local, chunk, padded), jnp.bfloat16),
    )(out_all, received)


def gather_by_shifts(rows, axis_name, count):
    seat = lax.axis_index(axis_name)
    shifted = [rows]
    for distance in range(1, count):
        pairs = [(source, (source + distance) % count) for source in range(count)]
        shifted.append(lax.ppermute(rows, axis_name, pairs))
    stacked = jnp.stack(shifted)
    order = (seat - jnp.arange(count, dtype=jnp.int32)) % count
    return jnp.take(stacked, order, axis=0).reshape(count * rows.shape[0], rows.shape[1])


def body(hidden_in, norm_gain, w_query, w_key, w_value, cache_keys, cache_values, cache_lengths):
    core_count = lax.axis_size("core")
    seq_count = lax.axis_size("sq") * core_count
    seq_seat = lax.axis_index("sq") * core_count + lax.axis_index("core")
    req_local, slice_len, model_width = hidden_in.shape
    cache_len_dev = cache_keys.shape[1]
    span_len = slice_len * seq_count
    inputs = hidden_in.astype(jnp.float32)
    normed = (
        inputs * lax.rsqrt(jnp.mean(inputs * inputs, axis=-1, keepdims=True) + EPSILON) * norm_gain
    ).astype(jnp.bfloat16)
    flat_rows = normed.reshape(req_local * slice_len, model_width)
    req_count = lax.axis_size("req")
    row_local = w_query.shape[0]
    query_cols = w_query.shape[1]
    key_cols = w_key.shape[1]
    joined = jnp.concatenate([w_query, w_key, w_value], axis=1)
    joined = gather_by_shifts(joined, "req", req_count)
    joined = lax.all_gather(joined, SEQ, axis=0, tiled=True)
    permuted_rows = (
        flat_rows.reshape(-1, req_count, seq_count, row_local)
        .transpose(0, 2, 1, 3)
        .reshape(-1, model_width)
    )
    projected = jnp.dot(permuted_rows, joined, preferred_element_type=jnp.float32)
    query_raw = projected[:, :query_cols]
    key_raw = projected[:, query_cols : query_cols + key_cols]
    value_raw = projected[:, query_cols + key_cols :]
    local_index = jnp.arange(slice_len, dtype=jnp.int32)
    positions = cache_lengths[:, None] + seq_seat * slice_len + local_index[None, :]
    cosine, sine_part = tables(positions, HEAD)
    queries = (
        rotate(query_raw.reshape(req_local, slice_len, HEADS, HEAD), cosine, sine_part)
        .reshape(req_local, slice_len, HEADS * HEAD)
        .astype(jnp.bfloat16)
    )
    new_keys = (
        rotate(key_raw.reshape(req_local, slice_len, KV_HEADS, HEAD), cosine, sine_part)
        .reshape(req_local, slice_len, KV_HEADS * HEAD)
        .astype(jnp.bfloat16)
    )
    new_values = value_raw.reshape(req_local, slice_len, KV_HEADS * HEAD).astype(jnp.bfloat16)
    token_major = queries.transpose(1, 0, 2).reshape(slice_len, req_local * HEADS * HEAD)
    all_queries = lax.all_gather(token_major, SEQ, axis=0, tiled=True)
    pad_rows = (-(cache_len_dev + slice_len)) % 128
    key_block = jnp.concatenate(
        [cache_keys, new_keys, jnp.zeros((req_local, pad_rows, KV_HEADS * HEAD), jnp.bfloat16)], axis=1
    )
    value_block = jnp.concatenate(
        [cache_values, new_values, jnp.zeros((req_local, pad_rows, KV_HEADS * HEAD), jnp.bfloat16)],
        axis=1,
    )
    scalars = jnp.concatenate([cache_lengths.astype(jnp.int32), seq_seat.astype(jnp.int32)[None]])
    out_all = block_attention(
        all_queries, key_block, value_block, scalars, cache_len_dev, slice_len, seq_count, core_count
    )
    swap = [(core, (core + 1) % core_count) for core in range(core_count)]
    received = lax.ppermute(out_all[1], "core", swap)
    merged = merge_pairs(out_all, received)
    got_out = lax.all_to_all(merged, "sq", split_axis=0, concat_axis=0, tiled=True)
    attended = combine(got_out)
    return (attended, new_keys, new_values)


def solution(mesh):
    core_count = 2
    req_count, seq_count = mesh.devices.shape
    split_mesh = Mesh(
        mesh.devices.reshape(req_count, seq_count // core_count, core_count), ("req", "sq", "core")
    )
    in_specs = (
        P("req", SEQ, None),
        P(),
        P(("req",) + SEQ, None),
        P(("req",) + SEQ, None),
        P(("req",) + SEQ, None),
        P("req", SEQ, None),
        P("req", SEQ, None),
        P("req"),
    )
    out_specs = (P("req", SEQ, None), P("req", SEQ, None), P("req", SEQ, None))
    return jax.shard_map(body, mesh=split_mesh, in_specs=in_specs, out_specs=out_specs, check_vma=False)
```

```python
import functools

import jax
import jax.numpy as jnp
from jax import lax
from jax.experimental import pallas as pl
from jax.experimental.pallas import tpu as pltpu
from jax.sharding import Mesh
from jax.sharding import PartitionSpec as P

HEADS = 4
KV_HEADS = 2
HEAD = 256


EPSILON = 1e-06
THETA = 1000042.0
MASKED = -1e30
SEQ = ("sq", "core")


def tables(positions, head_size):
    half_size = head_size // 2
    frequency = THETA ** (-(jnp.arange(half_size, dtype=jnp.float32) * 2.0 / head_size))
    angles = positions.astype(jnp.float32)[..., None] * frequency
    return (jnp.cos(angles)[..., None, :], jnp.sin(angles)[..., None, :])


def rotate(values, cosine, sine_part):
    half_size = values.shape[-1] // 2
    first_half = values[..., :half_size]
    second_half = values[..., half_size:]
    return jnp.concatenate(
        [
            first_half * cosine - second_half * sine_part,
            second_half * cosine + first_half * sine_part,
        ],
        axis=-1,
    )


def pack_stats(stats, lane):
    width = 2 * HEADS
    first = stats.astype(jnp.bfloat16).astype(jnp.float32)
    rest = stats - first
    second = rest.astype(jnp.bfloat16).astype(jnp.float32)
    third = (rest - second).astype(jnp.bfloat16).astype(jnp.float32)
    return jnp.where(
        lane < width,
        first,
        jnp.where(
            lane < 2 * width,
            pltpu.roll(second, width, 1),
            jnp.where(lane < 3 * width, pltpu.roll(third, 2 * width, 1), 0.0),
        ),
    )


def unpack_stats(packed):
    width = 2 * HEADS
    return (packed + pltpu.roll(packed, 128 - width, 1)) + pltpu.roll(packed, 128 - 2 * width, 1)


def attention_kernel(scalar_ref, query_ref, key_ref, value_ref, out_ref, *, cache_len_dev, slice_len):
    request = pl.program_id(0)
    length = scalar_ref[request]
    seat = scalar_ref[scalar_ref.shape[0] - 1]
    span_len = query_ref.shape[0]
    key_rows = key_ref.shape[1]
    cores = out_ref.shape[0]
    blocks = cores * out_ref.shape[1]
    own_core = seat % cores
    key_index = lax.broadcasted_iota(jnp.int32, (span_len, key_rows), 1)
    query_index = lax.broadcasted_iota(jnp.int32, (span_len, key_rows), 0)
    cache_live = seat * cache_len_dev + key_index < length
    new_live = seat * slice_len + (key_index - cache_len_dev) <= query_index
    in_cache = key_index < cache_len_dev
    in_new = jnp.logical_not(in_cache) & (key_index < cache_len_dev + slice_len)
    live = (in_cache & cache_live) | (in_new & new_live)
    lane = lax.broadcasted_iota(jnp.int32, (span_len, 128), 1)
    stats = jnp.zeros((span_len, 128), jnp.float32)
    group_size = HEADS // KV_HEADS
    for head in range(HEADS):
        group = head // group_size
        query_rows = query_ref[:, head * HEAD : (head + 1) * HEAD]
        key_rows_h = key_ref[0, :, group * HEAD : (group + 1) * HEAD]
        value_rows_h = value_ref[0, :, group * HEAD : (group + 1) * HEAD]
        scores = lax.dot_general(
            query_rows, key_rows_h, (((1,), (1,)), ((), ())), preferred_element_type=jnp.float32
        ) * HEAD ** (-0.5)
        scores = jnp.where(live, scores, MASKED)
        block_max = jnp.max(scores, axis=1, keepdims=True)
        weights = jnp.where(live, jnp.exp(scores - block_max), 0.0)
        block_sum = jnp.sum(weights, axis=1, keepdims=True)
        block_out = jnp.dot(
            weights.astype(jnp.bfloat16), value_rows_h, preferred_element_type=jnp.float32
        )
        by_dest = block_out.astype(jnp.bfloat16).reshape(blocks // cores, cores, span_len // blocks, HEAD)
        for core in range(cores):
            out_ref[(core + own_core) % cores, :, 0, :, head * HEAD : (head + 1) * HEAD] = by_dest[:, core]
        stats = jnp.where(lane == head, block_max, stats)
        stats = jnp.where(lane == HEADS + head, block_sum, stats)
    packed = pack_stats(stats, lane)
    by_dest = packed.astype(jnp.bfloat16).reshape(blocks // cores, cores, span_len // blocks, 128)
    for core in range(cores):
        out_ref[(core + own_core) % cores, :, 0, :, HEADS * HEAD :] = by_dest[:, core]


def block_attention(all_queries, key_block, value_block, scalars, cache_len_dev, slice_len, blocks, cores):
    req_local = key_block.shape[0]
    span_len = all_queries.shape[0]
    query_width = all_queries.shape[1] // req_local
    key_rows = key_block.shape[1]
    kv_width = key_block.shape[2]
    chunk = span_len // blocks
    grid_spec = pltpu.PrefetchScalarGridSpec(
        num_scalar_prefetch=1,
        grid=(req_local,),
        in_specs=[
            pl.BlockSpec((span_len, query_width), lambda r, s: (0, r)),
            pl.BlockSpec((1, key_rows, kv_width), lambda r, s: (r, 0, 0)),
            pl.BlockSpec((1, key_rows, kv_width), lambda r, s: (r, 0, 0)),
        ],
        out_specs=pl.BlockSpec(
            (cores, blocks // cores, 1, chunk, query_width + 128), lambda r, s: (0, 0, r, 0, 0)
        ),
    )
    return pl.pallas_call(
        functools.partial(attention_kernel, cache_len_dev=cache_len_dev, slice_len=slice_len),
        grid_spec=grid_spec,
        out_shape=jax.ShapeDtypeStruct(
            (cores, blocks // cores, req_local, chunk, query_width + 128), jnp.bfloat16
        ),
    )(scalars, all_queries, key_block, value_block)


def combine_kernel(out_ref, result_ref):
    blocks, _, chunk, padded = out_ref.shape
    width = HEADS * HEAD
    stat_width = 2 * HEADS
    lane = lax.broadcasted_iota(jnp.int32, (chunk, 128), 1)

    def block_stats(block):
        return unpack_stats(out_ref[block, 0, :, width:].astype(jnp.float32))

    top = block_stats(0)
    for block in range(1, blocks):
        top = jnp.maximum(top, block_stats(block))
    top = jnp.where(lane < HEADS, top, 0.0)

    def step(block, carry):
        summed, total = carry
        row_stats = block_stats(block)
        factor = jnp.exp(jnp.where(lane < HEADS, row_stats, 0.0) - top)
        pieces = []
        new_total = []
        total = total + factor * pltpu.roll(row_stats, 128 - HEADS, 1)
        for head in range(HEADS):
            head_factor = jnp.broadcast_to(factor[:, head : head + 1], (chunk, HEAD))
            rows = out_ref[block, 0, :, head * HEAD : (head + 1) * HEAD].astype(jnp.float32)
            pieces.append(summed[head] + rows * head_factor)
        return (tuple(pieces), total)

    start = (
        tuple(jnp.zeros((chunk, HEAD), jnp.float32) for _ in range(HEADS)),
        jnp.zeros((chunk, 128), jnp.float32),
    )
    summed, total = lax.fori_loop(0, blocks, step, start, unroll=4)
    for head in range(HEADS):
        head_total = jnp.broadcast_to(total[:, head : head + 1], (chunk, HEAD))
        result_ref[0, :, head * HEAD : (head + 1) * HEAD] = (summed[head] / head_total).astype(
            result_ref.dtype
        )


def combine(got_out):
    blocks, req_local, chunk, padded = got_out.shape
    width = HEADS * HEAD
    return pl.pallas_call(
        combine_kernel,
        grid=(req_local,),
        in_specs=[pl.BlockSpec((blocks, 1, chunk, padded), lambda r: (0, r, 0, 0))],
        out_specs=pl.BlockSpec((1, chunk, width), lambda r: (r, 0, 0)),
        out_shape=jax.ShapeDtypeStruct((req_local, chunk, width), jnp.bfloat16),
    )(got_out)


def merge_kernel(keep_ref, received_ref, merged_ref):
    _, dests, _, chunk, padded = keep_ref.shape
    width = HEADS * HEAD
    lane = lax.broadcasted_iota(jnp.int32, (chunk, 128), 1)

    def step(dest, carry):
        first = unpack_stats(keep_ref[0, dest, 0, :, width:].astype(jnp.float32))
        second = unpack_stats(received_ref[dest, 0, :, width:].astype(jnp.float32))
        first_max = jnp.where(lane < HEADS, first, 0.0)
        second_max = jnp.where(lane < HEADS, second, 0.0)
        best = jnp.maximum(first_max, second_max)
        first_factor = jnp.exp(first_max - best)
        second_factor = jnp.exp(second_max - best)
        first_sums = pltpu.roll(first, 128 - HEADS, 1)
        second_sums = pltpu.roll(second, 128 - HEADS, 1)
        sums = first_factor * first_sums + second_factor * second_sums
        stats = jnp.where(lane < HEADS, best, jnp.where(lane < 2 * HEADS, pltpu.roll(sums, HEADS, 1), 0.0))
        for head in range(HEADS):
            columns = slice(head * HEAD, (head + 1) * HEAD)
            first_head = jnp.broadcast_to(first_factor[:, head : head + 1], (chunk, HEAD))
            second_head = jnp.broadcast_to(second_factor[:, head : head + 1], (chunk, HEAD))
            partial = (
                keep_ref[0, dest, 0, :, columns].astype(jnp.float32) * first_head
                + received_ref[dest, 0, :, columns].astype(jnp.float32) * second_head
            )
            merged_ref[dest, 0, :, columns] = partial.astype(merged_ref.dtype)
        merged_ref[dest, 0, :, width:] = pack_stats(stats, lane).astype(merged_ref.dtype)
        return carry

    lax.fori_loop(0, dests, step, 0, unroll=4)


def merge_pairs(out_all, received):
    sources, dests, req_local, chunk, padded = out_all.shape
    return pl.pallas_call(
        merge_kernel,
        grid=(req_local,),
        in_specs=[
            pl.BlockSpec((1, dests, 1, chunk, padded), lambda r: (0, 0, r, 0, 0)),
            pl.BlockSpec((dests, 1, chunk, padded), lambda r: (0, r, 0, 0)),
        ],
        out_specs=pl.BlockSpec((dests, 1, chunk, padded), lambda r: (0, r, 0, 0)),
        out_shape=jax.ShapeDtypeStruct((dests, req_local, chunk, padded), jnp.bfloat16),
    )(out_all, received)


def gather_by_exchange(rows, axis_name, count):
    tiles = jnp.broadcast_to(rows[None], (count,) + rows.shape)
    gathered = lax.all_to_all(tiles, axis_name, split_axis=0, concat_axis=0, tiled=True)
    return gathered.reshape(count * rows.shape[0], rows.shape[1])


def body(hidden_in, norm_gain, w_query, w_key, w_value, cache_keys, cache_values, cache_lengths):
    core_count = lax.axis_size("core")
    seq_count = lax.axis_size("sq") * core_count
    seq_seat = lax.axis_index("sq") * core_count + lax.axis_index("core")
    req_local, slice_len, model_width = hidden_in.shape
    cache_len_dev = cache_keys.shape[1]
    span_len = slice_len * seq_count
    inputs = hidden_in.astype(jnp.float32)
    normed = (
        inputs * lax.rsqrt(jnp.mean(inputs * inputs, axis=-1, keepdims=True) + EPSILON) * norm_gain
    ).astype(jnp.bfloat16)
    flat_rows = normed.reshape(req_local * slice_len, model_width)
    req_count = lax.axis_size("req")
    row_local = w_query.shape[0]
    query_cols = w_query.shape[1]
    key_cols = w_key.shape[1]
    joined = jnp.concatenate([w_query, w_key, w_value], axis=1)
    joined = gather_by_exchange(joined, "req", req_count)
    joined = lax.all_gather(joined, SEQ, axis=0, tiled=True)
    permuted_rows = (
        flat_rows.reshape(-1, req_count, seq_count, row_local)
        .transpose(0, 2, 1, 3)
        .reshape(-1, model_width)
    )
    projected = jnp.dot(permuted_rows, joined, preferred_element_type=jnp.float32)
    query_raw = projected[:, :query_cols]
    key_raw = projected[:, query_cols : query_cols + key_cols]
    value_raw = projected[:, query_cols + key_cols :]
    local_index = jnp.arange(slice_len, dtype=jnp.int32)
    positions = cache_lengths[:, None] + seq_seat * slice_len + local_index[None, :]
    cosine, sine_part = tables(positions, HEAD)
    queries = (
        rotate(query_raw.reshape(req_local, slice_len, HEADS, HEAD), cosine, sine_part)
        .reshape(req_local, slice_len, HEADS * HEAD)
        .astype(jnp.bfloat16)
    )
    new_keys = (
        rotate(key_raw.reshape(req_local, slice_len, KV_HEADS, HEAD), cosine, sine_part)
        .reshape(req_local, slice_len, KV_HEADS * HEAD)
        .astype(jnp.bfloat16)
    )
    new_values = value_raw.reshape(req_local, slice_len, KV_HEADS * HEAD).astype(jnp.bfloat16)
    token_major = queries.transpose(1, 0, 2).reshape(slice_len, req_local * HEADS * HEAD)
    all_queries = lax.all_gather(token_major, SEQ, axis=0, tiled=True)
    pad_rows = (-(cache_len_dev + slice_len)) % 128
    key_block = jnp.concatenate(
        [cache_keys, new_keys, jnp.zeros((req_local, pad_rows, KV_HEADS * HEAD), jnp.bfloat16)], axis=1
    )
    value_block = jnp.concatenate(
        [cache_values, new_values, jnp.zeros((req_local, pad_rows, KV_HEADS * HEAD), jnp.bfloat16)],
        axis=1,
    )
    scalars = jnp.concatenate([cache_lengths.astype(jnp.int32), seq_seat.astype(jnp.int32)[None]])
    out_all = block_attention(
        all_queries, key_block, value_block, scalars, cache_len_dev, slice_len, seq_count, core_count
    )
    swap = [(core, (core + 1) % core_count) for core in range(core_count)]
    received = lax.ppermute(out_all[1], "core", swap)
    merged = merge_pairs(out_all, received)
    got_out = lax.all_to_all(merged, "sq", split_axis=0, concat_axis=0, tiled=True)
    attended = combine(got_out)
    return (attended, new_keys, new_values)


def solution(mesh):
    core_count = 2
    req_count, seq_count = mesh.devices.shape
    split_mesh = Mesh(
        mesh.devices.reshape(req_count, seq_count // core_count, core_count), ("req", "sq", "core")
    )
    in_specs = (
        P("req", SEQ, None),
        P(),
        P(("req",) + SEQ, None),
        P(("req",) + SEQ, None),
        P(("req",) + SEQ, None),
        P("req", SEQ, None),
        P("req", SEQ, None),
        P("req"),
    )
    out_specs = (P("req", SEQ, None), P("req", SEQ, None), P("req", SEQ, None))
    return jax.shard_map(body, mesh=split_mesh, in_specs=in_specs, out_specs=out_specs, check_vma=False)
```

```python
import functools

import jax
import jax.numpy as jnp
from jax import lax
from jax.experimental import pallas as pl
from jax.experimental.pallas import tpu as pltpu
from jax.sharding import Mesh
from jax.sharding import PartitionSpec as P

HEADS = 4
KV_HEADS = 2
HEAD = 256


EPSILON = 1e-06
THETA = 1000042.0
MASKED = -1e30
SEQ = ("sq", "core")


def tables(positions, head_size):
    half_size = head_size // 2
    frequency = THETA ** (-(jnp.arange(half_size, dtype=jnp.float32) * 2.0 / head_size))
    angles = positions.astype(jnp.float32)[..., None] * frequency
    return (jnp.cos(angles)[..., None, :], jnp.sin(angles)[..., None, :])


def rotate(values, cosine, sine_part):
    half_size = values.shape[-1] // 2
    first_half = values[..., :half_size]
    second_half = values[..., half_size:]
    return jnp.concatenate(
        [
            first_half * cosine - second_half * sine_part,
            second_half * cosine + first_half * sine_part,
        ],
        axis=-1,
    )


def pack_stats(stats, lane):
    width = 2 * HEADS
    first = stats.astype(jnp.bfloat16).astype(jnp.float32)
    rest = stats - first
    second = rest.astype(jnp.bfloat16).astype(jnp.float32)
    third = (rest - second).astype(jnp.bfloat16).astype(jnp.float32)
    return jnp.where(
        lane < width,
        first,
        jnp.where(
            lane < 2 * width,
            pltpu.roll(second, width, 1),
            jnp.where(lane < 3 * width, pltpu.roll(third, 2 * width, 1), 0.0),
        ),
    )


def unpack_stats(packed):
    width = 2 * HEADS
    return (packed + pltpu.roll(packed, 128 - width, 1)) + pltpu.roll(packed, 128 - 2 * width, 1)


def attention_kernel(scalar_ref, query_ref, key_ref, value_ref, out_ref, *, cache_len_dev, slice_len, request):
    length = scalar_ref[request]
    seat = scalar_ref[scalar_ref.shape[0] - 1]
    span_len = query_ref.shape[0]
    key_rows = key_ref.shape[1]
    cores = out_ref.shape[0]
    blocks = cores * out_ref.shape[1]
    own_core = seat % cores
    key_index = lax.broadcasted_iota(jnp.int32, (span_len, key_rows), 1)
    query_index = lax.broadcasted_iota(jnp.int32, (span_len, key_rows), 0)
    cache_live = seat * cache_len_dev + key_index < length
    new_live = seat * slice_len + (key_index - cache_len_dev) <= query_index
    in_cache = key_index < cache_len_dev
    in_new = jnp.logical_not(in_cache) & (key_index < cache_len_dev + slice_len)
    live = (in_cache & cache_live) | (in_new & new_live)
    lane = lax.broadcasted_iota(jnp.int32, (span_len, 128), 1)
    stats = jnp.zeros((span_len, 128), jnp.float32)
    group_size = HEADS // KV_HEADS
    for head in range(HEADS):
        group = head // group_size
        query_rows = query_ref[:, head * HEAD : (head + 1) * HEAD]
        key_rows_h = key_ref[0, :, group * HEAD : (group + 1) * HEAD]
        value_rows_h = value_ref[0, :, group * HEAD : (group + 1) * HEAD]
        scores = lax.dot_general(
            query_rows, key_rows_h, (((1,), (1,)), ((), ())), preferred_element_type=jnp.float32
        ) * HEAD ** (-0.5)
        scores = jnp.where(live, scores, MASKED)
        block_max = jnp.max(scores, axis=1, keepdims=True)
        weights = jnp.exp(scores - block_max)
        block_sum = jnp.sum(weights, axis=1, keepdims=True)
        block_out = jnp.dot(
            weights.astype(jnp.bfloat16), value_rows_h, preferred_element_type=jnp.float32
        )
        by_dest = block_out.astype(jnp.bfloat16).reshape(blocks // cores, cores, span_len // blocks, HEAD)
        for core in range(cores):
            out_ref[(core + own_core) % cores, :, 0, :, head * HEAD : (head + 1) * HEAD] = by_dest[:, core]
        stats = jnp.where(lane == head, block_max, stats)
        stats = jnp.where(lane == HEADS + head, block_sum, stats)
    packed = pack_stats(stats, lane)
    by_dest = packed.astype(jnp.bfloat16).reshape(blocks // cores, cores, span_len // blocks, 128)
    for core in range(cores):
        out_ref[(core + own_core) % cores, :, 0, :, HEADS * HEAD :] = by_dest[:, core]


def block_attention(all_queries, key_block, value_block, scalars, cache_len_dev, slice_len, blocks, cores, request):
    req_local = key_block.shape[0]
    span_len = all_queries.shape[0]
    query_width = all_queries.shape[1] // req_local
    key_rows = key_block.shape[1]
    kv_width = key_block.shape[2]
    chunk = span_len // blocks
    grid_spec = pltpu.PrefetchScalarGridSpec(
        num_scalar_prefetch=1,
        grid=(1,),
        in_specs=[
            pl.BlockSpec((span_len, query_width), lambda i, s: (0, request)),
            pl.BlockSpec((1, key_rows, kv_width), lambda i, s: (request, 0, 0)),
            pl.BlockSpec((1, key_rows, kv_width), lambda i, s: (request, 0, 0)),
        ],
        out_specs=pl.BlockSpec(
            (cores, blocks // cores, 1, chunk, query_width + 128), lambda i, s: (0, 0, 0, 0, 0)
        ),
    )
    return pl.pallas_call(
        functools.partial(
            attention_kernel, cache_len_dev=cache_len_dev, slice_len=slice_len, request=request
        ),
        grid_spec=grid_spec,
        out_shape=jax.ShapeDtypeStruct(
            (cores, blocks // cores, 1, chunk, query_width + 128), jnp.bfloat16
        ),
    )(scalars, all_queries, key_block, value_block)


def combine_kernel(out_ref, result_ref):
    blocks, _, chunk, _ = out_ref.shape
    width = HEADS * HEAD
    lane = lax.broadcasted_iota(jnp.int32, (chunk, 128), 1)

    def block_stats(block):
        return unpack_stats(out_ref[block, 0, :, width:].astype(jnp.float32))

    top = block_stats(0)
    for block in range(1, blocks):
        top = jnp.maximum(top, block_stats(block))
    top = jnp.where(lane < HEADS, top, 0.0)

    def step(block, carry):
        summed, total = carry
        row_stats = block_stats(block)
        factor = jnp.exp(jnp.where(lane < HEADS, row_stats, 0.0) - top)
        pieces = []
        total = total + factor * pltpu.roll(row_stats, 128 - HEADS, 1)
        for head in range(HEADS):
            head_factor = jnp.broadcast_to(factor[:, head : head + 1], (chunk, HEAD))
            rows = out_ref[block, 0, :, head * HEAD : (head + 1) * HEAD].astype(jnp.float32)
            pieces.append(summed[head] + rows * head_factor)
        return (tuple(pieces), total)

    start = (
        tuple(jnp.zeros((chunk, HEAD), jnp.float32) for _ in range(HEADS)),
        jnp.zeros((chunk, 128), jnp.float32),
    )
    summed, total = lax.fori_loop(0, blocks, step, start, unroll=4)
    for head in range(HEADS):
        head_total = jnp.broadcast_to(total[:, head : head + 1], (chunk, HEAD))
        result_ref[0, :, head * HEAD : (head + 1) * HEAD] = (summed[head] / head_total).astype(
            result_ref.dtype
        )


def combine(got_out):
    blocks, req_local, chunk, padded = got_out.shape
    width = HEADS * HEAD
    return pl.pallas_call(
        combine_kernel,
        grid=(req_local,),
        in_specs=[pl.BlockSpec((blocks, 1, chunk, padded), lambda r: (0, r, 0, 0))],
        out_specs=pl.BlockSpec((1, chunk, width), lambda r: (r, 0, 0)),
        out_shape=jax.ShapeDtypeStruct((req_local, chunk, width), jnp.bfloat16),
    )(got_out)


def merge_kernel(*refs):
    pieces = len(refs) // 2
    merged_ref = refs[-1]
    _, dests, _, chunk, _ = refs[0].shape
    width = HEADS * HEAD
    lane = lax.broadcasted_iota(jnp.int32, (chunk, 128), 1)

    def step(dest, carry, keep_ref, received_ref, request):
        first = unpack_stats(keep_ref[0, dest, 0, :, width:].astype(jnp.float32))
        second = unpack_stats(received_ref[dest, 0, :, width:].astype(jnp.float32))
        first_max = jnp.where(lane < HEADS, first, 0.0)
        second_max = jnp.where(lane < HEADS, second, 0.0)
        best = jnp.maximum(first_max, second_max)
        first_factor = jnp.exp(first_max - best)
        second_factor = jnp.exp(second_max - best)
        first_sums = pltpu.roll(first, 128 - HEADS, 1)
        second_sums = pltpu.roll(second, 128 - HEADS, 1)
        sums = first_factor * first_sums + second_factor * second_sums
        stats = jnp.where(lane < HEADS, best, jnp.where(lane < 2 * HEADS, pltpu.roll(sums, HEADS, 1), 0.0))
        for head in range(HEADS):
            columns = slice(head * HEAD, (head + 1) * HEAD)
            first_head = jnp.broadcast_to(first_factor[:, head : head + 1], (chunk, HEAD))
            second_head = jnp.broadcast_to(second_factor[:, head : head + 1], (chunk, HEAD))
            partial = (
                keep_ref[0, dest, 0, :, columns].astype(jnp.float32) * first_head
                + received_ref[dest, 0, :, columns].astype(jnp.float32) * second_head
            )
            merged_ref[dest, request, :, columns] = partial.astype(merged_ref.dtype)
        merged_ref[dest, request, :, width:] = pack_stats(stats, lane).astype(merged_ref.dtype)
        return carry

    for request in range(pieces):
        lax.fori_loop(
            0,
            dests,
            functools.partial(
                step, keep_ref=refs[request], received_ref=refs[pieces + request], request=request
            ),
            0,
            unroll=4,
        )


def merge_pairs(kept, received):
    _, dests, _, chunk, padded = kept[0].shape
    return pl.pallas_call(
        merge_kernel,
        out_shape=jax.ShapeDtypeStruct((dests, len(kept), chunk, padded), jnp.bfloat16),
    )(*kept, *received)


def gather_by_exchange(rows, axis_name, count):
    tiles = jnp.broadcast_to(rows[None], (count,) + rows.shape)
    gathered = lax.all_to_all(tiles, axis_name, split_axis=0, concat_axis=0, tiled=True)
    return gathered.reshape(count * rows.shape[0], rows.shape[1])


def body(hidden_in, norm_gain, w_query, w_key, w_value, cache_keys, cache_values, cache_lengths):
    core_count = lax.axis_size("core")
    seq_count = lax.axis_size("sq") * core_count
    seq_seat = lax.axis_index("sq") * core_count + lax.axis_index("core")
    req_local, slice_len, model_width = hidden_in.shape
    cache_len_dev = cache_keys.shape[1]
    inputs = hidden_in.astype(jnp.float32)
    normed = (
        inputs * lax.rsqrt(jnp.mean(inputs * inputs, axis=-1, keepdims=True) + EPSILON) * norm_gain
    ).astype(jnp.bfloat16)
    flat_rows = normed.reshape(req_local * slice_len, model_width)
    req_count = lax.axis_size("req")
    row_local = w_query.shape[0]
    query_cols = w_query.shape[1]
    key_cols = w_key.shape[1]
    joined = jnp.concatenate([w_query, w_key, w_value], axis=1)
    joined = gather_by_exchange(joined, "req", req_count)
    joined = lax.all_gather(joined, SEQ, axis=0, tiled=True)
    permuted_rows = (
        flat_rows.reshape(-1, req_count, seq_count, row_local)
        .transpose(0, 2, 1, 3)
        .reshape(-1, model_width)
    )
    projected = jnp.dot(permuted_rows, joined, preferred_element_type=jnp.float32)
    query_raw = projected[:, :query_cols]
    key_raw = projected[:, query_cols : query_cols + key_cols]
    value_raw = projected[:, query_cols + key_cols :]
    local_index = jnp.arange(slice_len, dtype=jnp.int32)
    positions = cache_lengths[:, None] + seq_seat * slice_len + local_index[None, :]
    cosine, sine_part = tables(positions, HEAD)
    queries = (
        rotate(query_raw.reshape(req_local, slice_len, HEADS, HEAD), cosine, sine_part)
        .reshape(req_local, slice_len, HEADS * HEAD)
        .astype(jnp.bfloat16)
    )
    new_keys = (
        rotate(key_raw.reshape(req_local, slice_len, KV_HEADS, HEAD), cosine, sine_part)
        .reshape(req_local, slice_len, KV_HEADS * HEAD)
        .astype(jnp.bfloat16)
    )
    new_values = value_raw.reshape(req_local, slice_len, KV_HEADS * HEAD).astype(jnp.bfloat16)
    token_major = queries.transpose(1, 0, 2).reshape(slice_len, req_local * HEADS * HEAD)
    all_queries = lax.all_gather(token_major, SEQ, axis=0, tiled=True)
    pad_rows = (-(cache_len_dev + slice_len)) % 128
    key_block = jnp.concatenate(
        [cache_keys, new_keys, jnp.zeros((req_local, pad_rows, KV_HEADS * HEAD), jnp.bfloat16)], axis=1
    )
    value_block = jnp.concatenate(
        [cache_values, new_values, jnp.zeros((req_local, pad_rows, KV_HEADS * HEAD), jnp.bfloat16)],
        axis=1,
    )
    scalars = jnp.concatenate([cache_lengths.astype(jnp.int32), seq_seat.astype(jnp.int32)[None]])
    swap = [(core, (core + 1) % core_count) for core in range(core_count)]
    kept = []
    received = []
    for request in range(req_local):
        out_one = block_attention(
            all_queries, key_block, value_block, scalars, cache_len_dev, slice_len, seq_count,
            core_count, request,
        )
        kept.append(out_one)
        received.append(lax.ppermute(out_one[1], "core", swap))
    merged = merge_pairs(kept, received)
    got_out = lax.all_to_all(merged, "sq", split_axis=0, concat_axis=0, tiled=True)
    attended = combine(got_out)
    return (attended, new_keys, new_values)


def solution(mesh):
    core_count = 2
    req_count, seq_count = mesh.devices.shape
    split_mesh = Mesh(
        mesh.devices.reshape(req_count, seq_count // core_count, core_count), ("req", "sq", "core")
    )
    in_specs = (
        P("req", SEQ, None),
        P(),
        P(("req",) + SEQ, None),
        P(("req",) + SEQ, None),
        P(("req",) + SEQ, None),
        P("req", SEQ, None),
        P("req", SEQ, None),
        P("req"),
    )
    out_specs = (P("req", SEQ, None), P("req", SEQ, None), P("req", SEQ, None))

    return jax.shard_map(body, mesh=split_mesh, in_specs=in_specs, out_specs=out_specs, check_vma=False)
```

```python
import functools

import jax
import jax.numpy as jnp
from jax import lax
from jax.experimental import pallas as pl
from jax.experimental.pallas import tpu as pltpu
from jax.sharding import Mesh
from jax.sharding import PartitionSpec as P

HEADS = 4
KV_HEADS = 2
HEAD = 256


EPSILON = 1e-06
THETA = 1000042.0
MASKED = -1e30
SEQ = ("sq", "core")


def tables(positions, head_size):
    half_size = head_size // 2
    frequency = THETA ** (-(jnp.arange(half_size, dtype=jnp.float32) * 2.0 / head_size))
    angles = positions.astype(jnp.float32)[..., None] * frequency
    return (jnp.cos(angles)[..., None, :], jnp.sin(angles)[..., None, :])


def rotate(values, cosine, sine_part):
    half_size = values.shape[-1] // 2
    first_half = values[..., :half_size]
    second_half = values[..., half_size:]
    return jnp.concatenate(
        [
            first_half * cosine - second_half * sine_part,
            second_half * cosine + first_half * sine_part,
        ],
        axis=-1,
    )


def pack_stats(stats, lane):
    width = 2 * HEADS
    first = stats.astype(jnp.bfloat16).astype(jnp.float32)
    rest = stats - first
    second = rest.astype(jnp.bfloat16).astype(jnp.float32)
    third = (rest - second).astype(jnp.bfloat16).astype(jnp.float32)
    return jnp.where(
        lane < width,
        first,
        jnp.where(
            lane < 2 * width,
            pltpu.roll(second, width, 1),
            jnp.where(lane < 3 * width, pltpu.roll(third, 2 * width, 1), 0.0),
        ),
    )


def unpack_stats(packed):
    width = 2 * HEADS
    return (packed + pltpu.roll(packed, 128 - width, 1)) + pltpu.roll(packed, 128 - 2 * width, 1)


def attention_kernel(scalar_ref, query_ref, key_ref, value_ref, out_ref, *, cache_len_dev, slice_len):
    request = pl.program_id(0)
    length = scalar_ref[request]
    seat = scalar_ref[scalar_ref.shape[0] - 1]
    span_len = query_ref.shape[0]
    key_rows = key_ref.shape[1]
    cores = out_ref.shape[0]
    blocks = cores * out_ref.shape[1]
    own_core = seat % cores
    key_index = lax.broadcasted_iota(jnp.int32, (span_len, key_rows), 1)
    query_index = lax.broadcasted_iota(jnp.int32, (span_len, key_rows), 0)
    cache_live = seat * cache_len_dev + key_index < length
    new_live = seat * slice_len + (key_index - cache_len_dev) <= query_index
    in_cache = key_index < cache_len_dev
    in_new = jnp.logical_not(in_cache) & (key_index < cache_len_dev + slice_len)
    live = (in_cache & cache_live) | (in_new & new_live)
    lane = lax.broadcasted_iota(jnp.int32, (span_len, 128), 1)
    stats = jnp.zeros((span_len, 128), jnp.float32)
    group_size = HEADS // KV_HEADS
    for head in range(HEADS):
        group = head // group_size
        query_rows = query_ref[:, head * HEAD : (head + 1) * HEAD]
        key_rows_h = key_ref[0, :, group * HEAD : (group + 1) * HEAD]
        value_rows_h = value_ref[0, :, group * HEAD : (group + 1) * HEAD]
        scores = lax.dot_general(
            query_rows, key_rows_h, (((1,), (1,)), ((), ())), preferred_element_type=jnp.float32
        ) * HEAD ** (-0.5)
        scores = jnp.where(live, scores, MASKED)
        block_max = jnp.max(scores, axis=1, keepdims=True)
        weights = jnp.exp(scores - block_max)
        block_sum = jnp.sum(weights, axis=1, keepdims=True)
        block_out = jnp.dot(
            weights.astype(jnp.bfloat16), value_rows_h, preferred_element_type=jnp.float32
        )
        by_dest = block_out.astype(jnp.bfloat16).reshape(blocks // cores, cores, span_len // blocks, HEAD)
        for core in range(cores):
            out_ref[(core + own_core) % cores, :, 0, :, head * HEAD : (head + 1) * HEAD] = by_dest[:, core]
        stats = jnp.where(lane == head, block_max, stats)
        stats = jnp.where(lane == HEADS + head, block_sum, stats)
    packed = pack_stats(stats, lane)
    by_dest = packed.astype(jnp.bfloat16).reshape(blocks // cores, cores, span_len // blocks, 128)
    for core in range(cores):
        out_ref[(core + own_core) % cores, :, 0, :, HEADS * HEAD :] = by_dest[:, core]


def block_attention(all_queries, key_block, value_block, scalars, cache_len_dev, slice_len, blocks, cores):
    req_local = key_block.shape[0]
    span_len = all_queries.shape[0]
    query_width = all_queries.shape[1] // req_local
    key_rows = key_block.shape[1]
    kv_width = key_block.shape[2]
    chunk = span_len // blocks
    grid_spec = pltpu.PrefetchScalarGridSpec(
        num_scalar_prefetch=1,
        grid=(req_local,),
        in_specs=[
            pl.BlockSpec((span_len, query_width), lambda r, s: (0, r)),
            pl.BlockSpec((1, key_rows, kv_width), lambda r, s: (r, 0, 0)),
            pl.BlockSpec((1, key_rows, kv_width), lambda r, s: (r, 0, 0)),
        ],
        out_specs=pl.BlockSpec(
            (cores, blocks // cores, 1, chunk, query_width + 128), lambda r, s: (0, 0, r, 0, 0)
        ),
    )
    return pl.pallas_call(
        functools.partial(attention_kernel, cache_len_dev=cache_len_dev, slice_len=slice_len),
        grid_spec=grid_spec,
        out_shape=jax.ShapeDtypeStruct(
            (cores, blocks // cores, req_local, chunk, query_width + 128), jnp.bfloat16
        ),
    )(scalars, all_queries, key_block, value_block)


def combine_kernel(out_ref, result_ref):
    blocks, _, chunk, padded = out_ref.shape
    width = HEADS * HEAD
    stat_width = 2 * HEADS
    lane = lax.broadcasted_iota(jnp.int32, (chunk, 128), 1)

    def block_stats(block):
        return unpack_stats(out_ref[block, 0, :, width:].astype(jnp.float32))

    top = block_stats(0)
    for block in range(1, blocks):
        top = jnp.maximum(top, block_stats(block))
    top = jnp.where(lane < HEADS, top, 0.0)

    def step(block, carry):
        summed, total = carry
        row_stats = block_stats(block)
        factor = jnp.exp(jnp.where(lane < HEADS, row_stats, 0.0) - top)
        pieces = []
        new_total = []
        total = total + factor * pltpu.roll(row_stats, 128 - HEADS, 1)
        for head in range(HEADS):
            head_factor = jnp.broadcast_to(factor[:, head : head + 1], (chunk, HEAD))
            rows = out_ref[block, 0, :, head * HEAD : (head + 1) * HEAD].astype(jnp.float32)
            pieces.append(summed[head] + rows * head_factor)
        return (tuple(pieces), total)

    start = (
        tuple(jnp.zeros((chunk, HEAD), jnp.float32) for _ in range(HEADS)),
        jnp.zeros((chunk, 128), jnp.float32),
    )
    summed, total = lax.fori_loop(0, blocks, step, start, unroll=4)
    for head in range(HEADS):
        head_total = jnp.broadcast_to(total[:, head : head + 1], (chunk, HEAD))
        result_ref[0, :, head * HEAD : (head + 1) * HEAD] = (summed[head] / head_total).astype(
            result_ref.dtype
        )


def combine(got_out):
    blocks, req_local, chunk, padded = got_out.shape
    width = HEADS * HEAD
    return pl.pallas_call(
        combine_kernel,
        grid=(req_local,),
        in_specs=[pl.BlockSpec((blocks, 1, chunk, padded), lambda r: (0, r, 0, 0))],
        out_specs=pl.BlockSpec((1, chunk, width), lambda r: (r, 0, 0)),
        out_shape=jax.ShapeDtypeStruct((req_local, chunk, width), jnp.bfloat16),
    )(got_out)


def merge_kernel(keep_ref, received_ref, merged_ref):
    _, dests, _, chunk, padded = keep_ref.shape
    width = HEADS * HEAD
    lane = lax.broadcasted_iota(jnp.int32, (chunk, 128), 1)

    def step(dest, carry):
        first = unpack_stats(keep_ref[0, dest, 0, :, width:].astype(jnp.float32))
        second = unpack_stats(received_ref[dest, 0, :, width:].astype(jnp.float32))
        first_max = jnp.where(lane < HEADS, first, 0.0)
        second_max = jnp.where(lane < HEADS, second, 0.0)
        best = jnp.maximum(first_max, second_max)
        first_factor = jnp.exp(first_max - best)
        second_factor = jnp.exp(second_max - best)
        first_sums = pltpu.roll(first, 128 - HEADS, 1)
        second_sums = pltpu.roll(second, 128 - HEADS, 1)
        sums = first_factor * first_sums + second_factor * second_sums
        stats = jnp.where(lane < HEADS, best, jnp.where(lane < 2 * HEADS, pltpu.roll(sums, HEADS, 1), 0.0))
        for head in range(HEADS):
            columns = slice(head * HEAD, (head + 1) * HEAD)
            first_head = jnp.broadcast_to(first_factor[:, head : head + 1], (chunk, HEAD))
            second_head = jnp.broadcast_to(second_factor[:, head : head + 1], (chunk, HEAD))
            partial = (
                keep_ref[0, dest, 0, :, columns].astype(jnp.float32) * first_head
                + received_ref[dest, 0, :, columns].astype(jnp.float32) * second_head
            )
            merged_ref[dest, 0, :, columns] = partial.astype(merged_ref.dtype)
        merged_ref[dest, 0, :, width:] = pack_stats(stats, lane).astype(merged_ref.dtype)
        return carry

    lax.fori_loop(0, dests, step, 0, unroll=4)


def merge_pairs(out_all, received):
    sources, dests, req_local, chunk, padded = out_all.shape
    return pl.pallas_call(
        merge_kernel,
        grid=(req_local,),
        in_specs=[
            pl.BlockSpec((1, dests, 1, chunk, padded), lambda r: (0, 0, r, 0, 0)),
            pl.BlockSpec((dests, 1, chunk, padded), lambda r: (0, r, 0, 0)),
        ],
        out_specs=pl.BlockSpec((dests, 1, chunk, padded), lambda r: (0, r, 0, 0)),
        out_shape=jax.ShapeDtypeStruct((dests, req_local, chunk, padded), jnp.bfloat16),
    )(out_all, received)


def gather_by_exchange(rows, axis_name, count):
    tiles = jnp.broadcast_to(rows[None], (count,) + rows.shape)
    gathered = lax.all_to_all(tiles, axis_name, split_axis=0, concat_axis=0, tiled=True)
    return gathered.reshape(count * rows.shape[0], rows.shape[1])


def body(hidden_in, norm_gain, w_query, w_key, w_value, cache_keys, cache_values, cache_lengths):
    core_count = lax.axis_size("core")
    seq_count = lax.axis_size("sq") * core_count
    seq_seat = lax.axis_index("sq") * core_count + lax.axis_index("core")
    req_local, slice_len, model_width = hidden_in.shape
    cache_len_dev = cache_keys.shape[1]
    span_len = slice_len * seq_count
    inputs = hidden_in.astype(jnp.float32)
    normed = (
        inputs * lax.rsqrt(jnp.mean(inputs * inputs, axis=-1, keepdims=True) + EPSILON) * norm_gain
    ).astype(jnp.bfloat16)
    flat_rows = normed.reshape(req_local * slice_len, model_width)
    req_count = lax.axis_size("req")
    row_local = w_query.shape[0]
    query_cols = w_query.shape[1]
    key_cols = w_key.shape[1]
    joined = jnp.concatenate([w_query, w_key, w_value], axis=1)
    joined = gather_by_exchange(joined, "req", req_count)
    joined = lax.all_gather(joined, SEQ, axis=0, tiled=True)
    permuted_rows = (
        flat_rows.reshape(-1, req_count, seq_count, row_local)
        .transpose(0, 2, 1, 3)
        .reshape(-1, model_width)
    )
    projected = jnp.dot(permuted_rows, joined, preferred_element_type=jnp.float32)
    query_raw = projected[:, :query_cols]
    key_raw = projected[:, query_cols : query_cols + key_cols]
    value_raw = projected[:, query_cols + key_cols :]
    local_index = jnp.arange(slice_len, dtype=jnp.int32)
    positions = cache_lengths[:, None] + seq_seat * slice_len + local_index[None, :]
    cosine, sine_part = tables(positions, HEAD)
    queries = (
        rotate(query_raw.reshape(req_local, slice_len, HEADS, HEAD), cosine, sine_part)
        .reshape(req_local, slice_len, HEADS * HEAD)
        .astype(jnp.bfloat16)
    )
    new_keys = (
        rotate(key_raw.reshape(req_local, slice_len, KV_HEADS, HEAD), cosine, sine_part)
        .reshape(req_local, slice_len, KV_HEADS * HEAD)
        .astype(jnp.bfloat16)
    )
    new_values = value_raw.reshape(req_local, slice_len, KV_HEADS * HEAD).astype(jnp.bfloat16)
    token_major = queries.transpose(1, 0, 2).reshape(slice_len, req_local * HEADS * HEAD)
    all_queries = lax.all_gather(token_major, SEQ, axis=0, tiled=True)
    pad_rows = (-(cache_len_dev + slice_len)) % 128
    key_block = jnp.concatenate(
        [cache_keys, new_keys, jnp.zeros((req_local, pad_rows, KV_HEADS * HEAD), jnp.bfloat16)], axis=1
    )
    value_block = jnp.concatenate(
        [cache_values, new_values, jnp.zeros((req_local, pad_rows, KV_HEADS * HEAD), jnp.bfloat16)],
        axis=1,
    )
    scalars = jnp.concatenate([cache_lengths.astype(jnp.int32), seq_seat.astype(jnp.int32)[None]])
    out_all = block_attention(
        all_queries, key_block, value_block, scalars, cache_len_dev, slice_len, seq_count, core_count
    )
    swap = [(core, (core + 1) % core_count) for core in range(core_count)]
    received = lax.ppermute(out_all[1], "core", swap)
    merged = merge_pairs(out_all, received)
    got_out = lax.all_to_all(merged, "sq", split_axis=0, concat_axis=0, tiled=True)
    attended = combine(got_out)
    return (attended, new_keys, new_values)


def solution(mesh):
    core_count = 2
    req_count, seq_count = mesh.devices.shape
    split_mesh = Mesh(
        mesh.devices.reshape(req_count, seq_count // core_count, core_count), ("req", "sq", "core")
    )
    in_specs = (
        P("req", SEQ, None),
        P(),
        P(("req",) + SEQ, None),
        P(("req",) + SEQ, None),
        P(("req",) + SEQ, None),
        P("req", SEQ, None),
        P("req", SEQ, None),
        P("req"),
    )
    out_specs = (P("req", SEQ, None), P("req", SEQ, None), P("req", SEQ, None))
    return jax.shard_map(body, mesh=split_mesh, in_specs=in_specs, out_specs=out_specs, check_vma=False)
```

```python
import functools

import jax
import jax.numpy as jnp
from jax import lax
from jax.experimental import pallas as pl
from jax.experimental.pallas import tpu as pltpu
from jax.sharding import Mesh
from jax.sharding import PartitionSpec as P

HEADS = 4
KV_HEADS = 2
HEAD = 256


EPSILON = 1e-06
THETA = 1000042.0
MASKED = -1e30
SEQ = ("sq", "core")


def tables(positions, head_size):
    half_size = head_size // 2
    frequency = THETA ** (-(jnp.arange(half_size, dtype=jnp.float32) * 2.0 / head_size))
    angles = positions.astype(jnp.float32)[..., None] * frequency
    return (jnp.cos(angles)[..., None, :], jnp.sin(angles)[..., None, :])


def rotate(values, cosine, sine_part):
    half_size = values.shape[-1] // 2
    first_half = values[..., :half_size]
    second_half = values[..., half_size:]
    return jnp.concatenate(
        [
            first_half * cosine - second_half * sine_part,
            second_half * cosine + first_half * sine_part,
        ],
        axis=-1,
    )


def pack_stats(stats, lane):
    width = 2 * HEADS
    first = stats.astype(jnp.bfloat16).astype(jnp.float32)
    rest = stats - first
    second = rest.astype(jnp.bfloat16).astype(jnp.float32)
    third = (rest - second).astype(jnp.bfloat16).astype(jnp.float32)
    return jnp.where(
        lane < width,
        first,
        jnp.where(
            lane < 2 * width,
            pltpu.roll(second, width, 1),
            jnp.where(lane < 3 * width, pltpu.roll(third, 2 * width, 1), 0.0),
        ),
    )


def unpack_stats(packed):
    width = 2 * HEADS
    return (packed + pltpu.roll(packed, 128 - width, 1)) + pltpu.roll(packed, 128 - 2 * width, 1)


def attention_kernel(scalar_ref, query_ref, key_ref, value_ref, out_ref, *, cache_len_dev, slice_len):
    request = pl.program_id(0)
    length = scalar_ref[request]
    seat = scalar_ref[scalar_ref.shape[0] - 1]
    span_len = query_ref.shape[0]
    key_rows = key_ref.shape[1]
    cores = out_ref.shape[0]
    blocks = cores * out_ref.shape[1]
    own_core = seat % cores
    key_index = lax.broadcasted_iota(jnp.int32, (span_len, key_rows), 1)
    query_index = lax.broadcasted_iota(jnp.int32, (span_len, key_rows), 0)
    cache_live = seat * cache_len_dev + key_index < length
    new_live = seat * slice_len + (key_index - cache_len_dev) <= query_index
    in_cache = key_index < cache_len_dev
    in_new = jnp.logical_not(in_cache) & (key_index < cache_len_dev + slice_len)
    live = (in_cache & cache_live) | (in_new & new_live)
    lane = lax.broadcasted_iota(jnp.int32, (span_len, 128), 1)
    stats = jnp.zeros((span_len, 128), jnp.float32)
    group_size = HEADS // KV_HEADS
    for head in range(HEADS):
        group = head // group_size
        query_rows = query_ref[:, head * HEAD : (head + 1) * HEAD]
        key_rows_h = key_ref[0, :, group * HEAD : (group + 1) * HEAD]
        value_rows_h = value_ref[0, :, group * HEAD : (group + 1) * HEAD]
        scores = lax.dot_general(
            query_rows, key_rows_h, (((1,), (1,)), ((), ())), preferred_element_type=jnp.float32
        ) * HEAD ** (-0.5)
        scores = jnp.where(live, scores, MASKED)
        block_max = jnp.max(scores, axis=1, keepdims=True)
        weights = jnp.where(live, jnp.exp(scores - block_max), 0.0)
        block_sum = jnp.sum(weights, axis=1, keepdims=True)
        block_out = jnp.dot(
            weights.astype(jnp.bfloat16), value_rows_h, preferred_element_type=jnp.float32
        )
        by_dest = block_out.astype(jnp.bfloat16).reshape(blocks // cores, cores, span_len // blocks, HEAD)
        for core in range(cores):
            out_ref[(core + own_core) % cores, :, 0, :, head * HEAD : (head + 1) * HEAD] = by_dest[:, core]
        stats = jnp.where(lane == head, block_max, stats)
        stats = jnp.where(lane == HEADS + head, block_sum, stats)
    packed = pack_stats(stats, lane)
    by_dest = packed.astype(jnp.bfloat16).reshape(blocks // cores, cores, span_len // blocks, 128)
    for core in range(cores):
        out_ref[(core + own_core) % cores, :, 0, :, HEADS * HEAD :] = by_dest[:, core]


def block_attention(all_queries, key_block, value_block, scalars, cache_len_dev, slice_len, blocks, cores):
    req_local = key_block.shape[0]
    span_len = all_queries.shape[0]
    query_width = all_queries.shape[1] // req_local
    key_rows = key_block.shape[1]
    kv_width = key_block.shape[2]
    chunk = span_len // blocks
    grid_spec = pltpu.PrefetchScalarGridSpec(
        num_scalar_prefetch=1,
        grid=(req_local,),
        in_specs=[
            pl.BlockSpec((span_len, query_width), lambda r, s: (0, r)),
            pl.BlockSpec((1, key_rows, kv_width), lambda r, s: (r, 0, 0)),
            pl.BlockSpec((1, key_rows, kv_width), lambda r, s: (r, 0, 0)),
        ],
        out_specs=pl.BlockSpec(
            (cores, blocks // cores, 1, chunk, query_width + 128), lambda r, s: (0, 0, r, 0, 0)
        ),
    )
    return pl.pallas_call(
        functools.partial(attention_kernel, cache_len_dev=cache_len_dev, slice_len=slice_len),
        grid_spec=grid_spec,
        out_shape=jax.ShapeDtypeStruct(
            (cores, blocks // cores, req_local, chunk, query_width + 128), jnp.bfloat16
        ),
    )(scalars, all_queries, key_block, value_block)


def combine_kernel(out_ref, result_ref):
    blocks, _, chunk, padded = out_ref.shape
    width = HEADS * HEAD
    stat_width = 2 * HEADS
    lane = lax.broadcasted_iota(jnp.int32, (chunk, 128), 1)

    def block_stats(block):
        return unpack_stats(out_ref[block, 0, :, width:].astype(jnp.float32))

    top = block_stats(0)
    for block in range(1, blocks):
        top = jnp.maximum(top, block_stats(block))
    top = jnp.where(lane < HEADS, top, 0.0)

    def step(block, carry):
        summed, total = carry
        row_stats = block_stats(block)
        factor = jnp.exp(jnp.where(lane < HEADS, row_stats, 0.0) - top)
        pieces = []
        new_total = []
        total = total + factor * pltpu.roll(row_stats, 128 - HEADS, 1)
        for head in range(HEADS):
            head_factor = jnp.broadcast_to(factor[:, head : head + 1], (chunk, HEAD))
            rows = out_ref[block, 0, :, head * HEAD : (head + 1) * HEAD].astype(jnp.float32)
            pieces.append(summed[head] + rows * head_factor)
        return (tuple(pieces), total)

    start = (
        tuple(jnp.zeros((chunk, HEAD), jnp.float32) for _ in range(HEADS)),
        jnp.zeros((chunk, 128), jnp.float32),
    )
    summed, total = lax.fori_loop(0, blocks, step, start, unroll=8)
    for head in range(HEADS):
        head_total = jnp.broadcast_to(total[:, head : head + 1], (chunk, HEAD))
        result_ref[0, :, head * HEAD : (head + 1) * HEAD] = (summed[head] / head_total).astype(
            result_ref.dtype
        )


def combine(got_out):
    blocks, req_local, chunk, padded = got_out.shape
    width = HEADS * HEAD
    return pl.pallas_call(
        combine_kernel,
        grid=(req_local,),
        in_specs=[pl.BlockSpec((blocks, 1, chunk, padded), lambda r: (0, r, 0, 0))],
        out_specs=pl.BlockSpec((1, chunk, width), lambda r: (r, 0, 0)),
        out_shape=jax.ShapeDtypeStruct((req_local, chunk, width), jnp.bfloat16),
    )(got_out)


def merge_kernel(keep_ref, received_ref, merged_ref):
    _, dests, _, chunk, padded = keep_ref.shape
    width = HEADS * HEAD
    lane = lax.broadcasted_iota(jnp.int32, (chunk, 128), 1)

    def step(dest, carry):
        first = unpack_stats(keep_ref[0, dest, 0, :, width:].astype(jnp.float32))
        second = unpack_stats(received_ref[dest, 0, :, width:].astype(jnp.float32))
        first_max = jnp.where(lane < HEADS, first, 0.0)
        second_max = jnp.where(lane < HEADS, second, 0.0)
        best = jnp.maximum(first_max, second_max)
        first_factor = jnp.exp(first_max - best)
        second_factor = jnp.exp(second_max - best)
        first_sums = pltpu.roll(first, 128 - HEADS, 1)
        second_sums = pltpu.roll(second, 128 - HEADS, 1)
        sums = first_factor * first_sums + second_factor * second_sums
        stats = jnp.where(lane < HEADS, best, jnp.where(lane < 2 * HEADS, pltpu.roll(sums, HEADS, 1), 0.0))
        for head in range(HEADS):
            columns = slice(head * HEAD, (head + 1) * HEAD)
            first_head = jnp.broadcast_to(first_factor[:, head : head + 1], (chunk, HEAD))
            second_head = jnp.broadcast_to(second_factor[:, head : head + 1], (chunk, HEAD))
            partial = (
                keep_ref[0, dest, 0, :, columns].astype(jnp.float32) * first_head
                + received_ref[dest, 0, :, columns].astype(jnp.float32) * second_head
            )
            merged_ref[dest, 0, :, columns] = partial.astype(merged_ref.dtype)
        merged_ref[dest, 0, :, width:] = pack_stats(stats, lane).astype(merged_ref.dtype)
        return carry

    lax.fori_loop(0, dests, step, 0, unroll=True)


def merge_pairs(out_all, received):
    sources, dests, req_local, chunk, padded = out_all.shape
    return pl.pallas_call(
        merge_kernel,
        grid=(req_local,),
        in_specs=[
            pl.BlockSpec((1, dests, 1, chunk, padded), lambda r: (0, 0, r, 0, 0)),
            pl.BlockSpec((dests, 1, chunk, padded), lambda r: (0, r, 0, 0)),
        ],
        out_specs=pl.BlockSpec((dests, 1, chunk, padded), lambda r: (0, r, 0, 0)),
        out_shape=jax.ShapeDtypeStruct((dests, req_local, chunk, padded), jnp.bfloat16),
    )(out_all, received)


def gather_by_exchange(rows, axis_name, count):
    tiles = jnp.broadcast_to(rows[None], (count,) + rows.shape)
    gathered = lax.all_to_all(tiles, axis_name, split_axis=0, concat_axis=0, tiled=True)
    return gathered.reshape(count * rows.shape[0], rows.shape[1])


def body(hidden_in, norm_gain, w_query, w_key, w_value, cache_keys, cache_values, cache_lengths):
    core_count = lax.axis_size("core")
    seq_count = lax.axis_size("sq") * core_count
    seq_seat = lax.axis_index("sq") * core_count + lax.axis_index("core")
    req_local, slice_len, model_width = hidden_in.shape
    cache_len_dev = cache_keys.shape[1]
    span_len = slice_len * seq_count
    inputs = hidden_in.astype(jnp.float32)
    normed = (
        inputs * lax.rsqrt(jnp.mean(inputs * inputs, axis=-1, keepdims=True) + EPSILON) * norm_gain
    ).astype(jnp.bfloat16)
    flat_rows = normed.reshape(req_local * slice_len, model_width)
    req_count = lax.axis_size("req")
    row_local = w_query.shape[0]
    query_cols = w_query.shape[1]
    key_cols = w_key.shape[1]
    joined = jnp.concatenate([w_query, w_key, w_value], axis=1)
    joined = gather_by_exchange(joined, "req", req_count)
    joined = lax.all_gather(joined, SEQ, axis=0, tiled=True)
    permuted_rows = (
        flat_rows.reshape(-1, req_count, seq_count, row_local)
        .transpose(0, 2, 1, 3)
        .reshape(-1, model_width)
    )
    projected = jnp.dot(permuted_rows, joined, preferred_element_type=jnp.float32)
    query_raw = projected[:, :query_cols]
    key_raw = projected[:, query_cols : query_cols + key_cols]
    value_raw = projected[:, query_cols + key_cols :]
    local_index = jnp.arange(slice_len, dtype=jnp.int32)
    positions = cache_lengths[:, None] + seq_seat * slice_len + local_index[None, :]
    cosine, sine_part = tables(positions, HEAD)
    queries = (
        rotate(query_raw.reshape(req_local, slice_len, HEADS, HEAD), cosine, sine_part)
        .reshape(req_local, slice_len, HEADS * HEAD)
        .astype(jnp.bfloat16)
    )
    new_keys = (
        rotate(key_raw.reshape(req_local, slice_len, KV_HEADS, HEAD), cosine, sine_part)
        .reshape(req_local, slice_len, KV_HEADS * HEAD)
        .astype(jnp.bfloat16)
    )
    new_values = value_raw.reshape(req_local, slice_len, KV_HEADS * HEAD).astype(jnp.bfloat16)
    token_major = queries.transpose(1, 0, 2).reshape(slice_len, req_local * HEADS * HEAD)
    all_queries = lax.all_gather(token_major, SEQ, axis=0, tiled=True)
    pad_rows = (-(cache_len_dev + slice_len)) % 128
    key_block = jnp.concatenate(
        [cache_keys, new_keys, jnp.zeros((req_local, pad_rows, KV_HEADS * HEAD), jnp.bfloat16)], axis=1
    )
    value_block = jnp.concatenate(
        [cache_values, new_values, jnp.zeros((req_local, pad_rows, KV_HEADS * HEAD), jnp.bfloat16)],
        axis=1,
    )
    scalars = jnp.concatenate([cache_lengths.astype(jnp.int32), seq_seat.astype(jnp.int32)[None]])
    out_all = block_attention(
        all_queries, key_block, value_block, scalars, cache_len_dev, slice_len, seq_count, core_count
    )
    swap = [(core, (core + 1) % core_count) for core in range(core_count)]
    received = lax.ppermute(out_all[1], "core", swap)
    merged = merge_pairs(out_all, received)
    got_out = lax.all_to_all(merged, "sq", split_axis=0, concat_axis=0, tiled=True)
    attended = combine(got_out)
    return (attended, new_keys, new_values)


def solution(mesh):
    core_count = 2
    req_count, seq_count = mesh.devices.shape
    split_mesh = Mesh(
        mesh.devices.reshape(req_count, seq_count // core_count, core_count), ("req", "sq", "core")
    )
    in_specs = (
        P("req", SEQ, None),
        P(),
        P(("req",) + SEQ, None),
        P(("req",) + SEQ, None),
        P(("req",) + SEQ, None),
        P("req", SEQ, None),
        P("req", SEQ, None),
        P("req"),
    )
    out_specs = (P("req", SEQ, None), P("req", SEQ, None), P("req", SEQ, None))
    return jax.shard_map(body, mesh=split_mesh, in_specs=in_specs, out_specs=out_specs, check_vma=False)
```

```python
import functools

import jax
import jax.numpy as jnp
from jax import lax
from jax.experimental import pallas as pl
from jax.experimental.pallas import tpu as pltpu
from jax.sharding import Mesh
from jax.sharding import PartitionSpec as P

HEADS = 4
KV_HEADS = 2
HEAD = 256


EPSILON = 1e-06
THETA = 1000042.0
MASKED = -1e30
SEQ = ("sq", "core")


def tables(positions, head_size):
    half_size = head_size // 2
    frequency = THETA ** (-(jnp.arange(half_size, dtype=jnp.float32) * 2.0 / head_size))
    angles = positions.astype(jnp.float32)[..., None] * frequency
    return (jnp.cos(angles)[..., None, :], jnp.sin(angles)[..., None, :])


def rotate(values, cosine, sine_part):
    half_size = values.shape[-1] // 2
    first_half = values[..., :half_size]
    second_half = values[..., half_size:]
    return jnp.concatenate(
        [
            first_half * cosine - second_half * sine_part,
            second_half * cosine + first_half * sine_part,
        ],
        axis=-1,
    )


def pack_stats(stats, lane):
    width = 2 * HEADS
    first = stats.astype(jnp.bfloat16).astype(jnp.float32)
    rest = stats - first
    second = rest.astype(jnp.bfloat16).astype(jnp.float32)
    third = (rest - second).astype(jnp.bfloat16).astype(jnp.float32)
    return jnp.where(
        lane < width,
        first,
        jnp.where(
            lane < 2 * width,
            pltpu.roll(second, width, 1),
            jnp.where(lane < 3 * width, pltpu.roll(third, 2 * width, 1), 0.0),
        ),
    )


def unpack_stats(packed):
    width = 2 * HEADS
    return (packed + pltpu.roll(packed, 128 - width, 1)) + pltpu.roll(packed, 128 - 2 * width, 1)


def attention_kernel(scalar_ref, query_ref, key_ref, value_ref, keep_ref, send_ref, *, cache_len_dev, slice_len):
    request = pl.program_id(0)
    length = scalar_ref[request]
    seat = scalar_ref[scalar_ref.shape[0] - 1]
    span_len = query_ref.shape[0]
    key_rows = key_ref.shape[1]
    cores = 2
    blocks = cores * keep_ref.shape[0]
    own_core = seat % cores

    def store(by_dest, columns):
        for core in range(cores):
            @pl.when(own_core == core)
            def _():
                keep_ref[:, 0, :, columns] = by_dest[:, core]

            @pl.when(own_core != core)
            def _():
                send_ref[:, 0, :, columns] = by_dest[:, core]
    key_index = lax.broadcasted_iota(jnp.int32, (span_len, key_rows), 1)
    query_index = lax.broadcasted_iota(jnp.int32, (span_len, key_rows), 0)
    cache_live = seat * cache_len_dev + key_index < length
    new_live = seat * slice_len + (key_index - cache_len_dev) <= query_index
    in_cache = key_index < cache_len_dev
    in_new = jnp.logical_not(in_cache) & (key_index < cache_len_dev + slice_len)
    live = (in_cache & cache_live) | (in_new & new_live)
    lane = lax.broadcasted_iota(jnp.int32, (span_len, 128), 1)
    stats = jnp.zeros((span_len, 128), jnp.float32)
    group_size = HEADS // KV_HEADS
    for head in range(HEADS):
        group = head // group_size
        query_rows = query_ref[:, head * HEAD : (head + 1) * HEAD]
        key_rows_h = key_ref[0, :, group * HEAD : (group + 1) * HEAD]
        value_rows_h = value_ref[0, :, group * HEAD : (group + 1) * HEAD]
        scores = lax.dot_general(
            query_rows, key_rows_h, (((1,), (1,)), ((), ())), preferred_element_type=jnp.float32
        ) * HEAD ** (-0.5)
        scores = jnp.where(live, scores, MASKED)
        block_max = jnp.max(scores, axis=1, keepdims=True)
        weights = jnp.where(live, jnp.exp(scores - block_max), 0.0)
        block_sum = jnp.sum(weights, axis=1, keepdims=True)
        block_out = jnp.dot(
            weights.astype(jnp.bfloat16), value_rows_h, preferred_element_type=jnp.float32
        )
        by_dest = block_out.astype(jnp.bfloat16).reshape(blocks // cores, cores, span_len // blocks, HEAD)
        store(by_dest, slice(head * HEAD, (head + 1) * HEAD))
        stats = jnp.where(lane == head, block_max, stats)
        stats = jnp.where(lane == HEADS + head, block_sum, stats)
    packed = pack_stats(stats, lane)
    by_dest = packed.astype(jnp.bfloat16).reshape(blocks // cores, cores, span_len // blocks, 128)
    store(by_dest, slice(HEADS * HEAD, None))


def block_attention(all_queries, key_block, value_block, scalars, cache_len_dev, slice_len, blocks, cores):
    req_local = key_block.shape[0]
    span_len = all_queries.shape[0]
    query_width = all_queries.shape[1] // req_local
    key_rows = key_block.shape[1]
    kv_width = key_block.shape[2]
    chunk = span_len // blocks
    grid_spec = pltpu.PrefetchScalarGridSpec(
        num_scalar_prefetch=1,
        grid=(req_local,),
        in_specs=[
            pl.BlockSpec((span_len, query_width), lambda r, s: (0, r)),
            pl.BlockSpec((1, key_rows, kv_width), lambda r, s: (r, 0, 0)),
            pl.BlockSpec((1, key_rows, kv_width), lambda r, s: (r, 0, 0)),
        ],
        out_specs=[
            pl.BlockSpec((blocks // cores, 1, chunk, query_width + 128), lambda r, s: (0, r, 0, 0)),
            pl.BlockSpec((blocks // cores, 1, chunk, query_width + 128), lambda r, s: (0, r, 0, 0)),
        ],
    )
    return pl.pallas_call(
        functools.partial(attention_kernel, cache_len_dev=cache_len_dev, slice_len=slice_len),
        grid_spec=grid_spec,
        out_shape=[
            jax.ShapeDtypeStruct((blocks // cores, req_local, chunk, query_width + 128), jnp.bfloat16),
            jax.ShapeDtypeStruct((blocks // cores, req_local, chunk, query_width + 128), jnp.bfloat16),
        ],
    )(scalars, all_queries, key_block, value_block)


def combine_kernel(out_ref, result_ref):
    blocks, _, chunk, padded = out_ref.shape
    width = HEADS * HEAD
    stat_width = 2 * HEADS
    lane = lax.broadcasted_iota(jnp.int32, (chunk, 128), 1)

    def block_stats(block):
        return unpack_stats(out_ref[block, 0, :, width:].astype(jnp.float32))

    top = block_stats(0)
    for block in range(1, blocks):
        top = jnp.maximum(top, block_stats(block))
    top = jnp.where(lane < HEADS, top, 0.0)

    def step(block, carry):
        summed, total = carry
        row_stats = block_stats(block)
        factor = jnp.exp(jnp.where(lane < HEADS, row_stats, 0.0) - top)
        pieces = []
        new_total = []
        total = total + factor * pltpu.roll(row_stats, 128 - HEADS, 1)
        for head in range(HEADS):
            head_factor = jnp.broadcast_to(factor[:, head : head + 1], (chunk, HEAD))
            rows = out_ref[block, 0, :, head * HEAD : (head + 1) * HEAD].astype(jnp.float32)
            pieces.append(summed[head] + rows * head_factor)
        return (tuple(pieces), total)

    start = (
        tuple(jnp.zeros((chunk, HEAD), jnp.float32) for _ in range(HEADS)),
        jnp.zeros((chunk, 128), jnp.float32),
    )
    summed, total = lax.fori_loop(0, blocks, step, start, unroll=4)
    for head in range(HEADS):
        head_total = jnp.broadcast_to(total[:, head : head + 1], (chunk, HEAD))
        result_ref[0, :, head * HEAD : (head + 1) * HEAD] = (summed[head] / head_total).astype(
            result_ref.dtype
        )


def combine(got_out):
    blocks, req_local, chunk, padded = got_out.shape
    width = HEADS * HEAD
    return pl.pallas_call(
        combine_kernel,
        grid=(req_local,),
        in_specs=[pl.BlockSpec((blocks, 1, chunk, padded), lambda r: (0, r, 0, 0))],
        out_specs=pl.BlockSpec((1, chunk, width), lambda r: (r, 0, 0)),
        out_shape=jax.ShapeDtypeStruct((req_local, chunk, width), jnp.bfloat16),
    )(got_out)


def merge_kernel(keep_ref, received_ref, merged_ref):
    dests, _, chunk, padded = keep_ref.shape
    width = HEADS * HEAD
    lane = lax.broadcasted_iota(jnp.int32, (chunk, 128), 1)

    def step(dest, carry):
        first = unpack_stats(keep_ref[dest, 0, :, width:].astype(jnp.float32))
        second = unpack_stats(received_ref[dest, 0, :, width:].astype(jnp.float32))
        first_max = jnp.where(lane < HEADS, first, 0.0)
        second_max = jnp.where(lane < HEADS, second, 0.0)
        best = jnp.maximum(first_max, second_max)
        first_factor = jnp.exp(first_max - best)
        second_factor = jnp.exp(second_max - best)
        first_sums = pltpu.roll(first, 128 - HEADS, 1)
        second_sums = pltpu.roll(second, 128 - HEADS, 1)
        sums = first_factor * first_sums + second_factor * second_sums
        stats = jnp.where(lane < HEADS, best, jnp.where(lane < 2 * HEADS, pltpu.roll(sums, HEADS, 1), 0.0))
        for head in range(HEADS):
            columns = slice(head * HEAD, (head + 1) * HEAD)
            first_head = jnp.broadcast_to(first_factor[:, head : head + 1], (chunk, HEAD))
            second_head = jnp.broadcast_to(second_factor[:, head : head + 1], (chunk, HEAD))
            partial = (
                keep_ref[dest, 0, :, columns].astype(jnp.float32) * first_head
                + received_ref[dest, 0, :, columns].astype(jnp.float32) * second_head
            )
            merged_ref[dest, 0, :, columns] = partial.astype(merged_ref.dtype)
        merged_ref[dest, 0, :, width:] = pack_stats(stats, lane).astype(merged_ref.dtype)
        return carry

    lax.fori_loop(0, dests, step, 0, unroll=4)


def merge_pairs(kept, received):
    dests, req_local, chunk, padded = kept.shape
    return pl.pallas_call(
        merge_kernel,
        grid=(req_local,),
        in_specs=[
            pl.BlockSpec((dests, 1, chunk, padded), lambda r: (0, r, 0, 0)),
            pl.BlockSpec((dests, 1, chunk, padded), lambda r: (0, r, 0, 0)),
        ],
        out_specs=pl.BlockSpec((dests, 1, chunk, padded), lambda r: (0, r, 0, 0)),
        out_shape=jax.ShapeDtypeStruct((dests, req_local, chunk, padded), jnp.bfloat16),
    )(kept, received)


def gather_by_exchange(rows, axis_name, count):
    tiles = jnp.broadcast_to(rows[None], (count,) + rows.shape)
    gathered = lax.all_to_all(tiles, axis_name, split_axis=0, concat_axis=0, tiled=True)
    return gathered.reshape(count * rows.shape[0], rows.shape[1])


def body(hidden_in, norm_gain, w_query, w_key, w_value, cache_keys, cache_values, cache_lengths):
    core_count = lax.axis_size("core")
    seq_count = lax.axis_size("sq") * core_count
    seq_seat = lax.axis_index("sq") * core_count + lax.axis_index("core")
    req_local, slice_len, model_width = hidden_in.shape
    cache_len_dev = cache_keys.shape[1]
    span_len = slice_len * seq_count
    inputs = hidden_in.astype(jnp.float32)
    normed = (
        inputs * lax.rsqrt(jnp.mean(inputs * inputs, axis=-1, keepdims=True) + EPSILON) * norm_gain
    ).astype(jnp.bfloat16)
    flat_rows = normed.reshape(req_local * slice_len, model_width)
    req_count = lax.axis_size("req")
    row_local = w_query.shape[0]
    query_cols = w_query.shape[1]
    key_cols = w_key.shape[1]
    joined = jnp.concatenate([w_query, w_key, w_value], axis=1)
    joined = gather_by_exchange(joined, "req", req_count)
    joined = lax.all_gather(joined, SEQ, axis=0, tiled=True)
    permuted_rows = (
        flat_rows.reshape(-1, req_count, seq_count, row_local)
        .transpose(0, 2, 1, 3)
        .reshape(-1, model_width)
    )
    projected = jnp.dot(permuted_rows, joined, preferred_element_type=jnp.float32)
    query_raw = projected[:, :query_cols]
    key_raw = projected[:, query_cols : query_cols + key_cols]
    value_raw = projected[:, query_cols + key_cols :]
    local_index = jnp.arange(slice_len, dtype=jnp.int32)
    positions = cache_lengths[:, None] + seq_seat * slice_len + local_index[None, :]
    cosine, sine_part = tables(positions, HEAD)
    queries = (
        rotate(query_raw.reshape(req_local, slice_len, HEADS, HEAD), cosine, sine_part)
        .reshape(req_local, slice_len, HEADS * HEAD)
        .astype(jnp.bfloat16)
    )
    new_keys = (
        rotate(key_raw.reshape(req_local, slice_len, KV_HEADS, HEAD), cosine, sine_part)
        .reshape(req_local, slice_len, KV_HEADS * HEAD)
        .astype(jnp.bfloat16)
    )
    new_values = value_raw.reshape(req_local, slice_len, KV_HEADS * HEAD).astype(jnp.bfloat16)
    token_major = queries.transpose(1, 0, 2).reshape(slice_len, req_local * HEADS * HEAD)
    all_queries = lax.all_gather(token_major, SEQ, axis=0, tiled=True)
    pad_rows = (-(cache_len_dev + slice_len)) % 128
    key_block = jnp.concatenate(
        [cache_keys, new_keys, jnp.zeros((req_local, pad_rows, KV_HEADS * HEAD), jnp.bfloat16)], axis=1
    )
    value_block = jnp.concatenate(
        [cache_values, new_values, jnp.zeros((req_local, pad_rows, KV_HEADS * HEAD), jnp.bfloat16)],
        axis=1,
    )
    scalars = jnp.concatenate([cache_lengths.astype(jnp.int32), seq_seat.astype(jnp.int32)[None]])
    kept, sent = block_attention(
        all_queries, key_block, value_block, scalars, cache_len_dev, slice_len, seq_count, core_count
    )
    swap = [(core, (core + 1) % core_count) for core in range(core_count)]
    received = lax.ppermute(sent, "core", swap)
    merged = merge_pairs(kept, received)
    got_out = lax.all_to_all(merged, "sq", split_axis=0, concat_axis=0, tiled=True)
    attended = combine(got_out)
    return (attended, new_keys, new_values)


def solution(mesh):
    core_count = 2
    req_count, seq_count = mesh.devices.shape
    split_mesh = Mesh(
        mesh.devices.reshape(req_count, seq_count // core_count, core_count), ("req", "sq", "core")
    )
    in_specs = (
        P("req", SEQ, None),
        P(),
        P(("req",) + SEQ, None),
        P(("req",) + SEQ, None),
        P(("req",) + SEQ, None),
        P("req", SEQ, None),
        P("req", SEQ, None),
        P("req"),
    )
    out_specs = (P("req", SEQ, None), P("req", SEQ, None), P("req", SEQ, None))
    return jax.shard_map(body, mesh=split_mesh, in_specs=in_specs, out_specs=out_specs, check_vma=False)
```

```python
import functools

import jax
import jax.numpy as jnp
from jax import lax
from jax.experimental import pallas as pl
from jax.experimental.pallas import tpu as pltpu
from jax.sharding import Mesh
from jax.sharding import PartitionSpec as P

HEADS = 4
KV_HEADS = 2
HEAD = 256


EPSILON = 1e-06
THETA = 1000042.0
MASKED = -1e30
SEQ = ("sq", "core")


def tables(positions, head_size):
    half_size = head_size // 2
    frequency = THETA ** (-(jnp.arange(half_size, dtype=jnp.float32) * 2.0 / head_size))
    angles = positions.astype(jnp.float32)[..., None] * frequency
    return (jnp.cos(angles)[..., None, :], jnp.sin(angles)[..., None, :])


def rotate(values, cosine, sine_part):
    half_size = values.shape[-1] // 2
    first_half = values[..., :half_size]
    second_half = values[..., half_size:]
    return jnp.concatenate(
        [
            first_half * cosine - second_half * sine_part,
            second_half * cosine + first_half * sine_part,
        ],
        axis=-1,
    )


def pack_stats(stats, lane):
    width = 2 * HEADS
    first = stats.astype(jnp.bfloat16).astype(jnp.float32)
    rest = stats - first
    second = rest.astype(jnp.bfloat16).astype(jnp.float32)
    third = (rest - second).astype(jnp.bfloat16).astype(jnp.float32)
    return jnp.where(
        lane < width,
        first,
        jnp.where(
            lane < 2 * width,
            pltpu.roll(second, width, 1),
            jnp.where(lane < 3 * width, pltpu.roll(third, 2 * width, 1), 0.0),
        ),
    )


def unpack_stats(packed):
    width = 2 * HEADS
    return (packed + pltpu.roll(packed, 128 - width, 1)) + pltpu.roll(packed, 128 - 2 * width, 1)


def attention_kernel(scalar_ref, query_ref, key_ref, value_ref, out_ref, *, cache_len_dev, slice_len):
    request = pl.program_id(0)
    length = scalar_ref[request]
    seat = scalar_ref[scalar_ref.shape[0] - 1]
    span_len = query_ref.shape[0]
    key_rows = key_ref.shape[1]
    cores = out_ref.shape[0]
    blocks = cores * out_ref.shape[1]
    own_core = seat % cores
    key_index = lax.broadcasted_iota(jnp.int32, (span_len, key_rows), 1)
    query_index = lax.broadcasted_iota(jnp.int32, (span_len, key_rows), 0)
    cache_live = seat * cache_len_dev + key_index < length
    new_live = seat * slice_len + (key_index - cache_len_dev) <= query_index
    in_cache = key_index < cache_len_dev
    in_new = jnp.logical_not(in_cache) & (key_index < cache_len_dev + slice_len)
    live = (in_cache & cache_live) | (in_new & new_live)
    lane = lax.broadcasted_iota(jnp.int32, (span_len, 128), 1)
    stats = jnp.zeros((span_len, 128), jnp.float32)
    group_size = HEADS // KV_HEADS
    for head in range(HEADS):
        group = head // group_size
        query_rows = query_ref[:, head * HEAD : (head + 1) * HEAD]
        key_rows_h = key_ref[0, :, group * HEAD : (group + 1) * HEAD]
        value_rows_h = value_ref[0, :, group * HEAD : (group + 1) * HEAD]
        scores = lax.dot_general(
            query_rows, key_rows_h, (((1,), (1,)), ((), ())), preferred_element_type=jnp.float32
        ) * HEAD ** (-0.5)
        scores = jnp.where(live, scores, MASKED)
        block_max = jnp.max(scores, axis=1, keepdims=True)
        weights = jnp.where(live, jnp.exp(scores - block_max), 0.0)
        block_sum = jnp.sum(weights, axis=1, keepdims=True)
        block_out = jnp.dot(
            weights.astype(jnp.bfloat16), value_rows_h, preferred_element_type=jnp.float32
        )
        by_dest = block_out.astype(jnp.bfloat16).reshape(blocks // cores, cores, span_len // blocks, HEAD)
        for core in range(cores):
            out_ref[(core + own_core) % cores, :, 0, :, head * HEAD : (head + 1) * HEAD] = by_dest[:, core]
        stats = jnp.where(lane == head, block_max, stats)
        stats = jnp.where(lane == HEADS + head, block_sum, stats)
    packed = pack_stats(stats, lane)
    by_dest = packed.astype(jnp.bfloat16).reshape(blocks // cores, cores, span_len // blocks, 128)
    for core in range(cores):
        out_ref[(core + own_core) % cores, :, 0, :, HEADS * HEAD :] = by_dest[:, core]


def block_attention(all_queries, key_block, value_block, scalars, cache_len_dev, slice_len, blocks, cores):
    req_local = key_block.shape[0]
    span_len = all_queries.shape[0]
    query_width = all_queries.shape[1] // req_local
    key_rows = key_block.shape[1]
    kv_width = key_block.shape[2]
    chunk = span_len // blocks
    grid_spec = pltpu.PrefetchScalarGridSpec(
        num_scalar_prefetch=1,
        grid=(req_local,),
        in_specs=[
            pl.BlockSpec((span_len, query_width), lambda r, s: (0, r)),
            pl.BlockSpec((1, key_rows, kv_width), lambda r, s: (r, 0, 0)),
            pl.BlockSpec((1, key_rows, kv_width), lambda r, s: (r, 0, 0)),
        ],
        out_specs=pl.BlockSpec(
            (cores, blocks // cores, 1, chunk, query_width + 128), lambda r, s: (0, 0, r, 0, 0)
        ),
    )
    return pl.pallas_call(
        functools.partial(attention_kernel, cache_len_dev=cache_len_dev, slice_len=slice_len),
        grid_spec=grid_spec,
        out_shape=jax.ShapeDtypeStruct(
            (cores, blocks // cores, req_local, chunk, query_width + 128), jnp.bfloat16
        ),
    )(scalars, all_queries, key_block, value_block)


def combine_kernel(out_ref, result_ref):
    blocks, _, chunk, padded = out_ref.shape
    width = HEADS * HEAD
    stat_width = 2 * HEADS
    lane = lax.broadcasted_iota(jnp.int32, (chunk, 128), 1)

    def block_stats(block):
        return unpack_stats(out_ref[block, 0, :, width:].astype(jnp.float32))

    top = block_stats(0)
    for block in range(1, blocks):
        top = jnp.maximum(top, block_stats(block))
    top = jnp.where(lane < HEADS, top, 0.0)

    def step(block, carry):
        summed, total = carry
        row_stats = block_stats(block)
        factor = jnp.exp(jnp.where(lane < HEADS, row_stats, 0.0) - top)
        pieces = []
        new_total = []
        total = total + factor * pltpu.roll(row_stats, 128 - HEADS, 1)
        for head in range(HEADS):
            head_factor = jnp.broadcast_to(factor[:, head : head + 1], (chunk, HEAD))
            rows = out_ref[block, 0, :, head * HEAD : (head + 1) * HEAD].astype(jnp.float32)
            pieces.append(summed[head] + rows * head_factor)
        return (tuple(pieces), total)

    start = (
        tuple(jnp.zeros((chunk, HEAD), jnp.float32) for _ in range(HEADS)),
        jnp.zeros((chunk, 128), jnp.float32),
    )
    summed, total = lax.fori_loop(0, blocks, step, start, unroll=4)
    for head in range(HEADS):
        head_total = jnp.broadcast_to(total[:, head : head + 1], (chunk, HEAD))
        result_ref[0, :, head * HEAD : (head + 1) * HEAD] = (summed[head] / head_total).astype(
            result_ref.dtype
        )


def combine(got_out):
    blocks, req_local, chunk, padded = got_out.shape
    width = HEADS * HEAD
    return pl.pallas_call(
        combine_kernel,
        grid=(req_local,),
        in_specs=[pl.BlockSpec((blocks, 1, chunk, padded), lambda r: (0, r, 0, 0))],
        out_specs=pl.BlockSpec((1, chunk, width), lambda r: (r, 0, 0)),
        out_shape=jax.ShapeDtypeStruct((req_local, chunk, width), jnp.bfloat16),
    )(got_out)


def merge_kernel(keep_ref, received_ref, merged_ref):
    _, dests, _, chunk, padded = keep_ref.shape
    width = HEADS * HEAD
    lane = lax.broadcasted_iota(jnp.int32, (chunk, 128), 1)

    def step(dest, carry):
        first = unpack_stats(keep_ref[0, dest, 0, :, width:].astype(jnp.float32))
        second = unpack_stats(received_ref[dest, 0, :, width:].astype(jnp.float32))
        first_max = jnp.where(lane < HEADS, first, 0.0)
        second_max = jnp.where(lane < HEADS, second, 0.0)
        best = jnp.maximum(first_max, second_max)
        first_factor = jnp.exp(first_max - best)
        second_factor = jnp.exp(second_max - best)
        first_sums = pltpu.roll(first, 128 - HEADS, 1)
        second_sums = pltpu.roll(second, 128 - HEADS, 1)
        sums = first_factor * first_sums + second_factor * second_sums
        stats = jnp.where(lane < HEADS, best, jnp.where(lane < 2 * HEADS, pltpu.roll(sums, HEADS, 1), 0.0))
        for head in range(HEADS):
            columns = slice(head * HEAD, (head + 1) * HEAD)
            first_head = jnp.broadcast_to(first_factor[:, head : head + 1], (chunk, HEAD))
            second_head = jnp.broadcast_to(second_factor[:, head : head + 1], (chunk, HEAD))
            partial = (
                keep_ref[0, dest, 0, :, columns].astype(jnp.float32) * first_head
                + received_ref[dest, 0, :, columns].astype(jnp.float32) * second_head
            )
            merged_ref[dest, 0, :, columns] = partial.astype(merged_ref.dtype)
        merged_ref[dest, 0, :, width:] = pack_stats(stats, lane).astype(merged_ref.dtype)
        return carry

    lax.fori_loop(0, dests, step, 0, unroll=2)


def merge_pairs(out_all, received):
    sources, dests, req_local, chunk, padded = out_all.shape
    return pl.pallas_call(
        merge_kernel,
        grid=(req_local,),
        in_specs=[
            pl.BlockSpec((1, dests, 1, chunk, padded), lambda r: (0, 0, r, 0, 0)),
            pl.BlockSpec((dests, 1, chunk, padded), lambda r: (0, r, 0, 0)),
        ],
        out_specs=pl.BlockSpec((dests, 1, chunk, padded), lambda r: (0, r, 0, 0)),
        out_shape=jax.ShapeDtypeStruct((dests, req_local, chunk, padded), jnp.bfloat16),
    )(out_all, received)


def gather_by_exchange(rows, axis_name, count):
    tiles = jnp.broadcast_to(rows[None], (count,) + rows.shape)
    gathered = lax.all_to_all(tiles, axis_name, split_axis=0, concat_axis=0, tiled=True)
    return gathered.reshape(count * rows.shape[0], rows.shape[1])


def body(hidden_in, norm_gain, w_query, w_key, w_value, cache_keys, cache_values, cache_lengths):
    core_count = lax.axis_size("core")
    seq_count = lax.axis_size("sq") * core_count
    seq_seat = lax.axis_index("sq") * core_count + lax.axis_index("core")
    req_local, slice_len, model_width = hidden_in.shape
    cache_len_dev = cache_keys.shape[1]
    span_len = slice_len * seq_count
    inputs = hidden_in.astype(jnp.float32)
    normed = (
        inputs * lax.rsqrt(jnp.mean(inputs * inputs, axis=-1, keepdims=True) + EPSILON) * norm_gain
    ).astype(jnp.bfloat16)
    flat_rows = normed.reshape(req_local * slice_len, model_width)
    req_count = lax.axis_size("req")
    row_local = w_query.shape[0]
    query_cols = w_query.shape[1]
    key_cols = w_key.shape[1]
    joined = jnp.concatenate([w_query, w_key, w_value], axis=1)
    joined = gather_by_exchange(joined, "req", req_count)
    joined = lax.all_gather(joined, SEQ, axis=0, tiled=True)
    permuted_rows = (
        flat_rows.reshape(-1, req_count, seq_count, row_local)
        .transpose(0, 2, 1, 3)
        .reshape(-1, model_width)
    )
    projected = jnp.dot(permuted_rows, joined, preferred_element_type=jnp.float32)
    query_raw = projected[:, :query_cols]
    key_raw = projected[:, query_cols : query_cols + key_cols]
    value_raw = projected[:, query_cols + key_cols :]
    local_index = jnp.arange(slice_len, dtype=jnp.int32)
    positions = cache_lengths[:, None] + seq_seat * slice_len + local_index[None, :]
    cosine, sine_part = tables(positions, HEAD)
    queries = (
        rotate(query_raw.reshape(req_local, slice_len, HEADS, HEAD), cosine, sine_part)
        .reshape(req_local, slice_len, HEADS * HEAD)
        .astype(jnp.bfloat16)
    )
    new_keys = (
        rotate(key_raw.reshape(req_local, slice_len, KV_HEADS, HEAD), cosine, sine_part)
        .reshape(req_local, slice_len, KV_HEADS * HEAD)
        .astype(jnp.bfloat16)
    )
    new_values = value_raw.reshape(req_local, slice_len, KV_HEADS * HEAD).astype(jnp.bfloat16)
    token_major = queries.transpose(1, 0, 2).reshape(slice_len, req_local * HEADS * HEAD)
    all_queries = lax.all_gather(token_major, SEQ, axis=0, tiled=True)
    pad_rows = (-(cache_len_dev + slice_len)) % 128
    key_block = jnp.concatenate(
        [cache_keys, new_keys, jnp.zeros((req_local, pad_rows, KV_HEADS * HEAD), jnp.bfloat16)], axis=1
    )
    value_block = jnp.concatenate(
        [cache_values, new_values, jnp.zeros((req_local, pad_rows, KV_HEADS * HEAD), jnp.bfloat16)],
        axis=1,
    )
    scalars = jnp.concatenate([cache_lengths.astype(jnp.int32), seq_seat.astype(jnp.int32)[None]])
    out_all = block_attention(
        all_queries, key_block, value_block, scalars, cache_len_dev, slice_len, seq_count, core_count
    )
    swap = [(core, (core + 1) % core_count) for core in range(core_count)]
    received = lax.ppermute(out_all[1], "core", swap)
    merged = merge_pairs(out_all, received)
    got_out = lax.all_to_all(merged, "sq", split_axis=0, concat_axis=0, tiled=True)
    attended = combine(got_out)
    return (attended, new_keys, new_values)


def solution(mesh):
    core_count = 2
    req_count, seq_count = mesh.devices.shape
    split_mesh = Mesh(
        mesh.devices.reshape(req_count, seq_count // core_count, core_count), ("req", "sq", "core")
    )
    in_specs = (
        P("req", SEQ, None),
        P(),
        P(("req",) + SEQ, None),
        P(("req",) + SEQ, None),
        P(("req",) + SEQ, None),
        P("req", SEQ, None),
        P("req", SEQ, None),
        P("req"),
    )
    out_specs = (P("req", SEQ, None), P("req", SEQ, None), P("req", SEQ, None))
    return jax.shard_map(body, mesh=split_mesh, in_specs=in_specs, out_specs=out_specs, check_vma=False)
```

```python
import functools

import jax
import jax.numpy as jnp
from jax import lax
from jax.experimental import pallas as pl
from jax.experimental.pallas import tpu as pltpu
from jax.sharding import Mesh
from jax.sharding import PartitionSpec as P

HEADS = 4
KV_HEADS = 2
HEAD = 256


EPSILON = 1e-06
THETA = 1000042.0
MASKED = -1e30
SEQ = ("sq", "core")


def tables(positions, head_size):
    half_size = head_size // 2
    frequency = THETA ** (-(jnp.arange(half_size, dtype=jnp.float32) * 2.0 / head_size))
    angles = positions.astype(jnp.float32)[..., None] * frequency
    return (jnp.cos(angles)[..., None, :], jnp.sin(angles)[..., None, :])


def rotate(values, cosine, sine_part):
    half_size = values.shape[-1] // 2
    first_half = values[..., :half_size]
    second_half = values[..., half_size:]
    return jnp.concatenate(
        [
            first_half * cosine - second_half * sine_part,
            second_half * cosine + first_half * sine_part,
        ],
        axis=-1,
    )


def pack_stats(stats, lane):
    width = 2 * HEADS
    first = stats.astype(jnp.bfloat16).astype(jnp.float32)
    rest = stats - first
    second = rest.astype(jnp.bfloat16).astype(jnp.float32)
    third = (rest - second).astype(jnp.bfloat16).astype(jnp.float32)
    return jnp.where(
        lane < width,
        first,
        jnp.where(
            lane < 2 * width,
            pltpu.roll(second, width, 1),
            jnp.where(lane < 3 * width, pltpu.roll(third, 2 * width, 1), 0.0),
        ),
    )


def unpack_stats(packed):
    width = 2 * HEADS
    return (packed + pltpu.roll(packed, 128 - width, 1)) + pltpu.roll(packed, 128 - 2 * width, 1)


def attention_kernel(scalar_ref, query_ref, key_ref, value_ref, out_ref, *, cache_len_dev, slice_len):
    request = pl.program_id(0)
    length = scalar_ref[request]
    seat = scalar_ref[scalar_ref.shape[0] - 1]
    span_len = query_ref.shape[0]
    key_rows = key_ref.shape[1]
    cores = out_ref.shape[0]
    blocks = cores * out_ref.shape[1]
    own_core = seat % cores
    key_index = lax.broadcasted_iota(jnp.int32, (span_len, key_rows), 1)
    query_index = lax.broadcasted_iota(jnp.int32, (span_len, key_rows), 0)
    cache_live = seat * cache_len_dev + key_index < length
    new_live = seat * slice_len + (key_index - cache_len_dev) <= query_index
    in_cache = key_index < cache_len_dev
    in_new = jnp.logical_not(in_cache) & (key_index < cache_len_dev + slice_len)
    live = (in_cache & cache_live) | (in_new & new_live)
    lane = lax.broadcasted_iota(jnp.int32, (span_len, 128), 1)
    stats = jnp.zeros((span_len, 128), jnp.float32)
    group_size = HEADS // KV_HEADS
    for head in range(HEADS):
        group = head // group_size
        query_rows = query_ref[:, head * HEAD : (head + 1) * HEAD]
        key_rows_h = key_ref[0, :, group * HEAD : (group + 1) * HEAD]
        value_rows_h = value_ref[0, :, group * HEAD : (group + 1) * HEAD]
        scores = lax.dot_general(
            query_rows, key_rows_h, (((1,), (1,)), ((), ())), preferred_element_type=jnp.float32
        ) * HEAD ** (-0.5)
        scores = jnp.where(live, scores, MASKED)
        block_max = jnp.max(scores, axis=1, keepdims=True)
        weights = jnp.where(live, jnp.exp(scores - block_max), 0.0)
        block_sum = jnp.sum(weights, axis=1, keepdims=True)
        block_out = jnp.dot(
            weights.astype(jnp.bfloat16), value_rows_h, preferred_element_type=jnp.float32
        )
        by_dest = block_out.astype(jnp.bfloat16).reshape(blocks // cores, cores, span_len // blocks, HEAD)
        for core in range(cores):
            out_ref[(core + own_core) % cores, :, 0, :, head * HEAD : (head + 1) * HEAD] = by_dest[:, core]
        stats = jnp.where(lane == head, block_max, stats)
        stats = jnp.where(lane == HEADS + head, block_sum, stats)
    packed = pack_stats(stats, lane)
    by_dest = packed.astype(jnp.bfloat16).reshape(blocks // cores, cores, span_len // blocks, 128)
    for core in range(cores):
        out_ref[(core + own_core) % cores, :, 0, :, HEADS * HEAD :] = by_dest[:, core]


def block_attention(all_queries, key_block, value_block, scalars, cache_len_dev, slice_len, blocks, cores):
    req_local = key_block.shape[0]
    span_len = all_queries.shape[0]
    query_width = all_queries.shape[1] // req_local
    key_rows = key_block.shape[1]
    kv_width = key_block.shape[2]
    chunk = span_len // blocks
    grid_spec = pltpu.PrefetchScalarGridSpec(
        num_scalar_prefetch=1,
        grid=(req_local,),
        in_specs=[
            pl.BlockSpec((span_len, query_width), lambda r, s: (0, r)),
            pl.BlockSpec((1, key_rows, kv_width), lambda r, s: (r, 0, 0)),
            pl.BlockSpec((1, key_rows, kv_width), lambda r, s: (r, 0, 0)),
        ],
        out_specs=pl.BlockSpec(
            (cores, blocks // cores, 1, chunk, query_width + 128), lambda r, s: (0, 0, r, 0, 0)
        ),
    )
    return pl.pallas_call(
        functools.partial(attention_kernel, cache_len_dev=cache_len_dev, slice_len=slice_len),
        grid_spec=grid_spec,
        out_shape=jax.ShapeDtypeStruct(
            (cores, blocks // cores, req_local, chunk, query_width + 128), jnp.bfloat16
        ),
    )(scalars, all_queries, key_block, value_block)


def combine_kernel(out_ref, result_ref):
    blocks, _, chunk, padded = out_ref.shape
    width = HEADS * HEAD
    stat_width = 2 * HEADS
    lane = lax.broadcasted_iota(jnp.int32, (chunk, 128), 1)

    def block_stats(block):
        return unpack_stats(out_ref[block, 0, :, width:].astype(jnp.float32))

    top = block_stats(0)
    for block in range(1, blocks):
        top = jnp.maximum(top, block_stats(block))
    top = jnp.where(lane < HEADS, top, 0.0)

    def step(block, carry):
        summed, total = carry
        row_stats = block_stats(block)
        factor = jnp.exp(jnp.where(lane < HEADS, row_stats, 0.0) - top)
        pieces = []
        new_total = []
        total = total + factor * pltpu.roll(row_stats, 128 - HEADS, 1)
        for head in range(HEADS):
            head_factor = jnp.broadcast_to(factor[:, head : head + 1], (chunk, HEAD))
            rows = out_ref[block, 0, :, head * HEAD : (head + 1) * HEAD].astype(jnp.float32)
            pieces.append(summed[head] + rows * head_factor)
        return (tuple(pieces), total)

    start = (
        tuple(jnp.zeros((chunk, HEAD), jnp.float32) for _ in range(HEADS)),
        jnp.zeros((chunk, 128), jnp.float32),
    )
    summed, total = lax.fori_loop(0, blocks, step, start, unroll=2)
    for head in range(HEADS):
        head_total = jnp.broadcast_to(total[:, head : head + 1], (chunk, HEAD))
        result_ref[0, :, head * HEAD : (head + 1) * HEAD] = (summed[head] / head_total).astype(
            result_ref.dtype
        )


def combine(got_out):
    blocks, req_local, chunk, padded = got_out.shape
    width = HEADS * HEAD
    return pl.pallas_call(
        combine_kernel,
        grid=(req_local,),
        in_specs=[pl.BlockSpec((blocks, 1, chunk, padded), lambda r: (0, r, 0, 0))],
        out_specs=pl.BlockSpec((1, chunk, width), lambda r: (r, 0, 0)),
        out_shape=jax.ShapeDtypeStruct((req_local, chunk, width), jnp.bfloat16),
    )(got_out)


def merge_kernel(keep_ref, received_ref, merged_ref):
    _, dests, _, chunk, padded = keep_ref.shape
    width = HEADS * HEAD
    lane = lax.broadcasted_iota(jnp.int32, (chunk, 128), 1)

    def step(dest, carry):
        first = unpack_stats(keep_ref[0, dest, 0, :, width:].astype(jnp.float32))
        second = unpack_stats(received_ref[dest, 0, :, width:].astype(jnp.float32))
        first_max = jnp.where(lane < HEADS, first, 0.0)
        second_max = jnp.where(lane < HEADS, second, 0.0)
        best = jnp.maximum(first_max, second_max)
        first_factor = jnp.exp(first_max - best)
        second_factor = jnp.exp(second_max - best)
        first_sums = pltpu.roll(first, 128 - HEADS, 1)
        second_sums = pltpu.roll(second, 128 - HEADS, 1)
        sums = first_factor * first_sums + second_factor * second_sums
        stats = jnp.where(lane < HEADS, best, jnp.where(lane < 2 * HEADS, pltpu.roll(sums, HEADS, 1), 0.0))
        for head in range(HEADS):
            columns = slice(head * HEAD, (head + 1) * HEAD)
            first_head = jnp.broadcast_to(first_factor[:, head : head + 1], (chunk, HEAD))
            second_head = jnp.broadcast_to(second_factor[:, head : head + 1], (chunk, HEAD))
            partial = (
                keep_ref[0, dest, 0, :, columns].astype(jnp.float32) * first_head
                + received_ref[dest, 0, :, columns].astype(jnp.float32) * second_head
            )
            merged_ref[dest, 0, :, columns] = partial.astype(merged_ref.dtype)
        merged_ref[dest, 0, :, width:] = pack_stats(stats, lane).astype(merged_ref.dtype)
        return carry

    lax.fori_loop(0, dests, step, 0, unroll=2)


def merge_pairs(out_all, received):
    sources, dests, req_local, chunk, padded = out_all.shape
    return pl.pallas_call(
        merge_kernel,
        grid=(req_local,),
        in_specs=[
            pl.BlockSpec((1, dests, 1, chunk, padded), lambda r: (0, 0, r, 0, 0)),
            pl.BlockSpec((dests, 1, chunk, padded), lambda r: (0, r, 0, 0)),
        ],
        out_specs=pl.BlockSpec((dests, 1, chunk, padded), lambda r: (0, r, 0, 0)),
        out_shape=jax.ShapeDtypeStruct((dests, req_local, chunk, padded), jnp.bfloat16),
    )(out_all, received)


def gather_by_exchange(rows, axis_name, count):
    tiles = jnp.broadcast_to(rows[None], (count,) + rows.shape)
    gathered = lax.all_to_all(tiles, axis_name, split_axis=0, concat_axis=0, tiled=True)
    return gathered.reshape(count * rows.shape[0], rows.shape[1])


def body(hidden_in, norm_gain, w_query, w_key, w_value, cache_keys, cache_values, cache_lengths):
    core_count = lax.axis_size("core")
    seq_count = lax.axis_size("sq") * core_count
    seq_seat = lax.axis_index("sq") * core_count + lax.axis_index("core")
    req_local, slice_len, model_width = hidden_in.shape
    cache_len_dev = cache_keys.shape[1]
    span_len = slice_len * seq_count
    inputs = hidden_in.astype(jnp.float32)
    normed = (
        inputs * lax.rsqrt(jnp.mean(inputs * inputs, axis=-1, keepdims=True) + EPSILON) * norm_gain
    ).astype(jnp.bfloat16)
    flat_rows = normed.reshape(req_local * slice_len, model_width)
    req_count = lax.axis_size("req")
    row_local = w_query.shape[0]
    query_cols = w_query.shape[1]
    key_cols = w_key.shape[1]
    joined = jnp.concatenate([w_query, w_key, w_value], axis=1)
    joined = gather_by_exchange(joined, "req", req_count)
    joined = lax.all_gather(joined, SEQ, axis=0, tiled=True)
    permuted_rows = (
        flat_rows.reshape(-1, req_count, seq_count, row_local)
        .transpose(0, 2, 1, 3)
        .reshape(-1, model_width)
    )
    projected = jnp.dot(permuted_rows, joined, preferred_element_type=jnp.float32)
    query_raw = projected[:, :query_cols]
    key_raw = projected[:, query_cols : query_cols + key_cols]
    value_raw = projected[:, query_cols + key_cols :]
    local_index = jnp.arange(slice_len, dtype=jnp.int32)
    positions = cache_lengths[:, None] + seq_seat * slice_len + local_index[None, :]
    cosine, sine_part = tables(positions, HEAD)
    queries = (
        rotate(query_raw.reshape(req_local, slice_len, HEADS, HEAD), cosine, sine_part)
        .reshape(req_local, slice_len, HEADS * HEAD)
        .astype(jnp.bfloat16)
    )
    new_keys = (
        rotate(key_raw.reshape(req_local, slice_len, KV_HEADS, HEAD), cosine, sine_part)
        .reshape(req_local, slice_len, KV_HEADS * HEAD)
        .astype(jnp.bfloat16)
    )
    new_values = value_raw.reshape(req_local, slice_len, KV_HEADS * HEAD).astype(jnp.bfloat16)
    token_major = queries.transpose(1, 0, 2).reshape(slice_len, req_local * HEADS * HEAD)
    all_queries = lax.all_gather(token_major, SEQ, axis=0, tiled=True)
    pad_rows = (-(cache_len_dev + slice_len)) % 128
    key_block = jnp.concatenate(
        [cache_keys, new_keys, jnp.zeros((req_local, pad_rows, KV_HEADS * HEAD), jnp.bfloat16)], axis=1
    )
    value_block = jnp.concatenate(
        [cache_values, new_values, jnp.zeros((req_local, pad_rows, KV_HEADS * HEAD), jnp.bfloat16)],
        axis=1,
    )
    scalars = jnp.concatenate([cache_lengths.astype(jnp.int32), seq_seat.astype(jnp.int32)[None]])
    out_all = block_attention(
        all_queries, key_block, value_block, scalars, cache_len_dev, slice_len, seq_count, core_count
    )
    swap = [(core, (core + 1) % core_count) for core in range(core_count)]
    received = lax.ppermute(out_all[1], "core", swap)
    merged = merge_pairs(out_all, received)
    got_out = lax.all_to_all(merged, "sq", split_axis=0, concat_axis=0, tiled=True)
    attended = combine(got_out)
    return (attended, new_keys, new_values)


def solution(mesh):
    core_count = 2
    req_count, seq_count = mesh.devices.shape
    split_mesh = Mesh(
        mesh.devices.reshape(req_count, seq_count // core_count, core_count), ("req", "sq", "core")
    )
    in_specs = (
        P("req", SEQ, None),
        P(),
        P(("req",) + SEQ, None),
        P(("req",) + SEQ, None),
        P(("req",) + SEQ, None),
        P("req", SEQ, None),
        P("req", SEQ, None),
        P("req"),
    )
    out_specs = (P("req", SEQ, None), P("req", SEQ, None), P("req", SEQ, None))
    return jax.shard_map(body, mesh=split_mesh, in_specs=in_specs, out_specs=out_specs, check_vma=False)
```
